32 devices in a mesh: group: 2 (over y), section: 4 (over x, core), shard: 4 (over z).
Axes of the slice: x: 2, y: 2, z: 4, core: 2. Of those that a mesh axis runs over, the one named last changes fastest.
Arguments:
- image_tokens: bfloat16 [4, 96, 8192], P('group', 'section', 'shard'), parts along dimension 0, may hold values from -6 to 6
- keyval_weight: bfloat16 [4, 8192, 1024], P('section', 'shard'), may hold values from -0.0625 to 0.0625
- query_gain: float32 [4, 4096], P('section'), may hold values from 0.5 to 5
- key_norm_gain: float32 [4, 512], P('section'), may hold values from 0.5 to 5
- gate_logit: float32 [4, 32], P('section'), may hold values from -1.5 to 1.5
- text_queries: bfloat16 [4, 256, 4096], P('group', 'shard'), parts along dimension 0, may hold values from -6 to 6
- text_document: int32 [4, 256], P('group', 'shard'), parts along dimension 0, may hold values from 0 to 7, never falling along the last dimension, each value on 1 to 128 neighbouring positions
- image_document: int32 [4, 96], P('group'), parts along dimension 0, may hold values from 0 to 7, never falling along the last dimension, each value on 1 to 48 neighbouring positions
- cotangent: bfloat16 [4, 4, 256, 4096], P('section', 'group', 'shard'), parts along dimension 1, may hold values from -6 to 6
Outputs:
- section_states: float32 [4, 4, 256, 4096], P('section', 'group', 'shard'), parts along dimension 1
- image_grad: float32 [4, 96, 8192], P('group', 'section', 'shard'), parts along dimension 0
The draws below stay inside these ranges and needn't reach their ends.
There are 2 independent parts, one for each index of `group`. The reference program is written for one: setup_inputs(seed, part) draws one part's arguments, and reference() takes and returns one part's arrays. A program takes and returns all parts, laid end to end along the dimension named above; an argument that names none is the same for every part. Nothing has to cross between parts.
Inputs may be any that keep to these rules, and one draw needn't show every extreme that they name: `text_document`: numbers never fall along a micro-batch's text tokens; every number from 0 to 7 appears in each micro-batch. `image_document`: numbers never fall along a micro-batch's image tokens; every number from 0 to 7 appears in each micro-batch.
All inputs are finite; a program needn't handle non-finite values.
Results may differ from the reference program's by a relative error of at most 0.034.
The reference program's roundings to bfloat16 on the way count: a program that leaves them out, or rounds other values in their place, can miss the bound.
Values may be sent and summed in bfloat16 or wider, within the bound.
No kernel may reach another device: no remote copies, remote signals or barrier semaphores. Data moves between devices by JAX's collectives and lax.ppermute only.
A program may use at most 128 MiB of HBM per device.

```python
import math
import jax
import jax.numpy as jnp
import numpy as np
from jax import lax

D = 8192
HEAD_SIZE = 128
QUERY_HEADS = 32
KEYVAL_HEADS = 4
MICRO_BATCHES = 2
NDOC = 8
CROSS_LAYERS = 4
QW = 4096
KEY_WIDTH = 512
TEXT_TOKENS = 256
IMAGE_TOKENS = 96


def gain_matrix(key, rows_count, head_count, width):
    second_key = jax.random.fold_in(key, 1)
    return jax.random.uniform(second_key, (rows_count, head_count * width), jnp.float32, 0.5, 1.5)


def draw_query_gain(key, part):
    return gain_matrix(jax.random.fold_in(key, 11), CROSS_LAYERS, QUERY_HEADS, HEAD_SIZE)


def draw_key_norm_gain(key, part):
    return gain_matrix(jax.random.fold_in(key, 23), CROSS_LAYERS, KEYVAL_HEADS, HEAD_SIZE)


def spiked(entries, key, source, target, shards_of, factor):
    owner, partner = [(jnp.arange(entries.shape[axis_at]) // (entries.shape[axis_at] // shards_of)).reshape([-1 if axis == axis_at else 1 for axis in range(entries.ndim)]) for axis_at in (source, target)]
    chosen = jax.random.permutation(key, shards_of)[partner]
    strong = (owner == chosen) | (owner == (partner + shards_of // 2) % shards_of)
    return jnp.where(strong, factor * entries, entries)


def level_of(key, dims, shards, least, top_value):
    factor_of = 1.0
    for dim, parts in shards:
        draws = jax.random.uniform(jax.random.fold_in(jax.random.fold_in(key, 6), dim), (parts,), jnp.float32, least / len(shards), top_value / len(shards))
        factor_of = factor_of * jnp.repeat(jnp.exp(draws), dims[dim] // parts).reshape((-1,) + (1,) * (len(dims) - 1 - dim))
    return factor_of


def profile(amount, total, most, skew):
    weights = [(1 << 20) // math.isqrt(grade ** skew) + 1 for grade in range(2, amount + 1)]
    rest, holding = total - most - (amount - 1), [1] * (amount - 1)
    while rest > 0:
        candidates = [i for i in range(amount - 1) if holding[i] < most]
        pool, remaining = sum([weights[i] for i in candidates]), rest
        for i in candidates:
            extra = min(most - holding[i], max(1, remaining * weights[i] // pool), rest)
            holding[i] = holding[i] + extra
            rest = rest - extra
    return np.array([most] + holding)


def ragged_sizes(rng, number_of, total, reach, skew):
    if number_of == 2:
        one = jax.random.randint(rng, (), max(1, total - reach), min(reach, total - 1) + 1)
        return jnp.stack([one, total - one])
    tallies = jnp.asarray(profile(number_of, total, reach, skew), jnp.int32)
    twos = (number_of - 1) // 2
    source_of, taker = tallies[1:1 + 2 * twos:2], tallies[2:2 + 2 * twos:2]
    slack = jnp.minimum(source_of - 1, reach - taker)
    passed = jax.random.randint(jax.random.fold_in(rng, 1), (twos,), 0, 1 << 20) % (slack + 1)
    tallies = tallies.at[1:1 + 2 * twos:2].set(source_of - passed).at[2:2 + 2 * twos:2].set(taker + passed)
    return tallies[jax.random.permutation(jax.random.fold_in(rng, 2), number_of)]


def bell_draw(key, dims, spread, most, cuts=(), kind=jnp.bfloat16):
    drawn = spread * jax.random.normal(key, dims, jnp.float32)
    if cuts:
        drawn = drawn * level_of(key, dims, cuts, -0.22, 0.18)
    return jnp.clip(drawn, -most, most).astype(kind)


def bell_draw_with(rng, shape, scale, limit, shards, heavy, dtype=jnp.bfloat16):
    array = scale * jax.random.normal(rng, shape, jnp.float32)
    if shards:
        array = array * level_of(rng, shape, shards, -0.22, 0.18)
    return jnp.clip(spiked(array, jax.random.fold_in(rng, 3), *heavy), -limit, limit).astype(dtype)


def setup_inputs(seed: int = 0, part: int = 0) -> dict:
    seeds = jax.random.split(jax.random.key(seed), 10)
    part_keys = jax.random.split(jax.random.fold_in(seeds[9], part), 10)
    image_tokens = bell_draw_with(part_keys[0], (MICRO_BATCHES, IMAGE_TOKENS, D), 1.0, 6.0, ((1, 4), (2, 4)), (2, 1, 4, 2.0))
    keyval_weight = bell_draw(seeds[1], (CROSS_LAYERS, D, 2 * KEY_WIDTH), D ** -0.5, 0.0625, ((0, 4), (1, 4)))
    query_gain = draw_query_gain(jax.random.fold_in(seeds[9], 71), part)
    key_norm_gain = draw_key_norm_gain(jax.random.fold_in(seeds[9], 71), part)
    gate_logit = jnp.clip(jax.random.uniform(seeds[4], (CROSS_LAYERS, QUERY_HEADS), jnp.float32, -1.5, 1.5) * level_of(seeds[4], (CROSS_LAYERS, QUERY_HEADS), ((0, 4),), -0.4, 0.0), -1.5, 1.5)
    text_queries = bell_draw(part_keys[5], (MICRO_BATCHES, TEXT_TOKENS, QW), 1.0, 6.0, ((1, 4),))
    text_document = jax.vmap(lambda own: jnp.searchsorted(jnp.cumsum(ragged_sizes(own, NDOC, TEXT_TOKENS, TEXT_TOKENS // 2, 0)), jnp.arange(TEXT_TOKENS), side="right"))(jax.random.split(part_keys[6], MICRO_BATCHES)).reshape((MICRO_BATCHES, TEXT_TOKENS)).astype(jnp.int32)
    image_document = jax.vmap(lambda own: jnp.searchsorted(jnp.cumsum(ragged_sizes(own, NDOC, IMAGE_TOKENS, IMAGE_TOKENS // 2, 0)), jnp.arange(IMAGE_TOKENS), side="right"))(jax.random.split(part_keys[7], MICRO_BATCHES)).reshape((MICRO_BATCHES, IMAGE_TOKENS)).astype(jnp.int32)
    cotangent = bell_draw(part_keys[8], (CROSS_LAYERS, MICRO_BATCHES, TEXT_TOKENS, QW), 1.0, 6.0, ((0, 4), (2, 4)))
    return dict(image_tokens=image_tokens, keyval_weight=keyval_weight, query_gain=query_gain, key_norm_gain=key_norm_gain, gate_logit=gate_logit, text_queries=text_queries, text_document=text_document, image_document=image_document, cotangent=cotangent)


epsilon = 1e-05

def head_normalize(input_rows, gain_row, head_count):
    shaped = input_rows.reshape(input_rows.shape[0], head_count, -1)
    factor = lax.rsqrt(lax.optimization_barrier(jnp.mean(shaped * shaped, axis=-1, keepdims=True)) + epsilon)
    return (shaped * factor * gain_row.reshape(1, head_count, -1)).reshape(input_rows.shape[0], -1)

def norm_gradient(input_rows, gain_row, incoming_gradient, head_count):
    shaped = input_rows.reshape(input_rows.shape[0], head_count, -1)
    scaled = incoming_gradient.reshape(input_rows.shape[0], head_count, -1) * gain_row.reshape(1, head_count, -1)
    factor = lax.rsqrt(lax.optimization_barrier(jnp.mean(shaped * shaped, axis=-1, keepdims=True)) + epsilon)
    inner_mean = lax.optimization_barrier(jnp.mean(shaped * scaled, axis=-1, keepdims=True))
    result = factor * scaled - shaped * factor * factor * factor * inner_mean
    return result.reshape(input_rows.shape[0], -1)

def reference(image_tokens, keyval_weight, query_gain, key_norm_gain, gate_logit, text_queries, text_document, image_document, cotangent):
    query_groups = QUERY_HEADS // KEYVAL_HEADS
    inverse_root = 1.0 / math.sqrt(HEAD_SIZE)
    flat_rows = image_tokens.reshape(MICRO_BATCHES * IMAGE_TOKENS, D)
    stream = text_queries.astype(jnp.float32)
    section_outputs = []
    image_grad = jnp.zeros((MICRO_BATCHES * IMAGE_TOKENS, D), jnp.float32)
    for layer_number in range(CROSS_LAYERS):
        unscaled_sum = jnp.dot(flat_rows, keyval_weight[layer_number], preferred_element_type=jnp.float32)
        key_matrix = head_normalize(unscaled_sum[:, :KEY_WIDTH], key_norm_gain[layer_number], KEYVAL_HEADS).astype(jnp.bfloat16).reshape(MICRO_BATCHES, IMAGE_TOKENS, KEYVAL_HEADS, HEAD_SIZE)
        value_matrix = unscaled_sum[:, KEY_WIDTH:].astype(jnp.bfloat16).reshape(MICRO_BATCHES, IMAGE_TOKENS, KEYVAL_HEADS, HEAD_SIZE)
        gate_factor = jnp.tanh(gate_logit[layer_number])
        next_states = []
        grad_parts = []
        for micro_batch_index in range(MICRO_BATCHES):
            current = stream[micro_batch_index]
            query_matrix = head_normalize(current.astype(jnp.float32), query_gain[layer_number], QUERY_HEADS).astype(jnp.bfloat16)
            query_single = query_matrix.astype(jnp.float32).reshape(TEXT_TOKENS, KEYVAL_HEADS, query_groups, HEAD_SIZE)
            key_float = key_matrix[micro_batch_index].astype(jnp.float32)
            value_float = value_matrix[micro_batch_index].astype(jnp.float32)
            scores = jnp.einsum('tkgd,ikd->kgti', query_single, key_float) * inverse_root
            same_document = text_document[micro_batch_index][:, None] == image_document[micro_batch_index][None, :]
            scores = jnp.where(same_document[None, None], scores, -jnp.inf)
            row_max = lax.optimization_barrier(jnp.max(scores, axis=-1, keepdims=True))
            powered = jnp.exp(scores - row_max)
            exact_probs = powered / lax.optimization_barrier(jnp.sum(powered, axis=-1, keepdims=True))
            probability = exact_probs.astype(jnp.bfloat16).astype(jnp.float32)
            attended = jnp.einsum('kgti,ikd->tkgd', probability, value_float)
            updated = current.astype(jnp.float32).reshape(TEXT_TOKENS, QUERY_HEADS, HEAD_SIZE) + gate_factor[None, :, None] * attended.reshape(TEXT_TOKENS, QUERY_HEADS, HEAD_SIZE)
            next_states.append(updated.reshape(TEXT_TOKENS, QW))
            incoming_gradient = cotangent[layer_number, micro_batch_index].astype(jnp.float32).reshape(TEXT_TOKENS, KEYVAL_HEADS, query_groups, HEAD_SIZE)
            value_grad = jnp.einsum('kgti,tkgd->ikd', probability, incoming_gradient)
            prob_grad = jnp.einsum('tkgd,ikd->kgti', incoming_gradient, value_float)
            score_grad = exact_probs * (prob_grad - lax.optimization_barrier(jnp.sum(exact_probs * prob_grad, axis=-1, keepdims=True)))
            score_grad = score_grad.astype(jnp.bfloat16).astype(jnp.float32)
            key_grad = jnp.einsum('kgti,tkgd->ikd', score_grad, query_single) * inverse_root
            grad_parts.append(jnp.concatenate([key_grad.reshape(IMAGE_TOKENS, KEY_WIDTH), value_grad.reshape(IMAGE_TOKENS, KEY_WIDTH)], axis=1))
        stream = jnp.stack(next_states)
        section_outputs.append(stream)
        gradient_total = jnp.concatenate(grad_parts, axis=0)
        key_portion = norm_gradient(unscaled_sum[:, :KEY_WIDTH], key_norm_gain[layer_number], gradient_total[:, :KEY_WIDTH], KEYVAL_HEADS)
        raw_grad = jnp.concatenate([key_portion, gradient_total[:, KEY_WIDTH:]], axis=1).astype(jnp.bfloat16)
        image_grad = image_grad + jnp.dot(raw_grad, keyval_weight[layer_number].T, preferred_element_type=jnp.float32)
    return (jnp.stack(section_outputs), image_grad.reshape(MICRO_BATCHES, IMAGE_TOKENS, D))
```

```python
import math

import jax
import jax.numpy as jnp
from jax import lax
from jax.sharding import PartitionSpec as P

epsilon = 1e-05


def head_normalize(input_rows, gain_row, head_count):
    shaped = input_rows.reshape(input_rows.shape[:-1] + (head_count, -1))
    factor = lax.rsqrt(jnp.mean(shaped * shaped, axis=-1, keepdims=True) + epsilon)
    gain = gain_row.reshape((1,) * (shaped.ndim - 2) + (head_count, -1))
    return (shaped * factor * gain).reshape(input_rows.shape)


def norm_gradient(input_rows, gain_row, incoming_gradient, head_count):
    shaped = input_rows.reshape(input_rows.shape[0], head_count, -1)
    scaled = incoming_gradient.reshape(input_rows.shape[0], head_count, -1) * gain_row.reshape(
        1, head_count, -1
    )
    factor = lax.rsqrt(jnp.mean(shaped * shaped, axis=-1, keepdims=True) + epsilon)
    inner_mean = jnp.mean(shaped * scaled, axis=-1, keepdims=True)
    result = factor * scaled - shaped * factor * factor * factor * inner_mean
    return result.reshape(input_rows.shape[0], -1)


def attend_scores(current, gain_row, key_block, same_document, head_count):
    micro, token_count = current.shape[0], current.shape[1]
    keyval_heads = key_block.shape[2]
    head_dim = key_block.shape[3]
    query_groups = head_count // keyval_heads
    query_matrix = head_normalize(current, gain_row, head_count).astype(jnp.bfloat16)
    query_matrix = query_matrix.reshape(micro, token_count, keyval_heads, query_groups, head_dim)
    scores = jnp.einsum(
        "mtkgd,mikd->mkgti", query_matrix, key_block, preferred_element_type=jnp.float32
    ) * (1.0 / math.sqrt(head_dim))
    scores = jnp.where(same_document[:, None, None], scores, -jnp.inf)
    row_max = jnp.max(scores, axis=-1, keepdims=True)
    powered = jnp.exp(scores - row_max)
    exact_probs = powered / jnp.sum(powered, axis=-1, keepdims=True)
    return (query_matrix, exact_probs)


def forward_layer(current, gain_row, gate_row, key_block, value_block, same_document, head_count):
    micro, token_count = current.shape[0], current.shape[1]
    head_dim = value_block.shape[3]
    query_matrix, exact_probs = attend_scores(
        current, gain_row, key_block, same_document, head_count
    )
    probability = exact_probs.astype(jnp.bfloat16)
    attended = jnp.einsum(
        "mkgti,mikd->mtkgd", probability, value_block, preferred_element_type=jnp.float32
    )
    updated = current.reshape(micro, token_count, head_count, head_dim)
    updated = updated + jnp.tanh(gate_row)[None, None, :, None] * attended.reshape(
        micro, token_count, head_count, head_dim
    )
    return updated.reshape(current.shape)


def backward_layer(current, gain_row, key_block, value_block, same_document, upstream, head_count):
    micro, token_count = current.shape[0], current.shape[1]
    image_count = key_block.shape[1]
    keyval_heads = key_block.shape[2]
    head_dim = key_block.shape[3]
    query_matrix, exact_probs = attend_scores(
        current, gain_row, key_block, same_document, head_count
    )
    probability = exact_probs.astype(jnp.bfloat16)
    incoming_gradient = upstream.reshape(
        micro, token_count, keyval_heads, head_count // keyval_heads, head_dim
    )
    value_grad = jnp.einsum(
        "mkgti,mtkgd->mikd", probability, incoming_gradient, preferred_element_type=jnp.float32
    )
    prob_grad = jnp.einsum(
        "mtkgd,mikd->mkgti", incoming_gradient, value_block, preferred_element_type=jnp.float32
    )
    score_grad = exact_probs * (
        prob_grad - jnp.sum(exact_probs * prob_grad, axis=-1, keepdims=True)
    )
    score_grad = score_grad.astype(jnp.bfloat16)
    key_grad = jnp.einsum(
        "mkgti,mtkgd->mikd", score_grad, query_matrix, preferred_element_type=jnp.float32
    ) * (1.0 / math.sqrt(head_dim))
    return jnp.concatenate(
        [
            key_grad.reshape(micro * image_count, -1),
            value_grad.reshape(micro * image_count, -1),
        ],
        axis=1,
    )


def per_device(
    image_tokens,
    keyval_weight,
    query_gain,
    key_norm_gain,
    gate_logit,
    text_queries,
    text_document,
    image_document,
    cotangent,
):
    section_count = lax.axis_size("section")
    section_index = lax.axis_index("section")
    micro_count = text_queries.shape[0]
    head_count = gate_logit.shape[1]
    key_width = key_norm_gain.shape[1]
    head_dim = query_gain.shape[1] // head_count
    keyval_heads = key_width // head_dim
    weights = keyval_weight[0]

    layer_params = lax.all_gather(
        jnp.concatenate([query_gain, gate_logit], axis=1), "section", axis=0, tiled=True
    )
    gains_all = layer_params[:, : query_gain.shape[1]]
    gates_all = layer_params[:, query_gain.shape[1] :]

    gathered = lax.all_gather(image_tokens, "section", axis=1, tiled=True)
    image_count = gathered.shape[1]
    total_rows = micro_count * image_count
    flat_rows = gathered.reshape(total_rows, gathered.shape[2])
    partial = jnp.dot(flat_rows, weights, preferred_element_type=jnp.float32)
    raw_rows = lax.psum_scatter(partial, "shard", scatter_dimension=0, tiled=True)
    key_rows = head_normalize(raw_rows[:, :key_width], key_norm_gain[0], keyval_heads)
    keyval_rows = jnp.concatenate(
        [key_rows.astype(jnp.bfloat16), raw_rows[:, key_width:].astype(jnp.bfloat16)], axis=1
    )
    keyval_all = lax.all_gather(keyval_rows, ("section", "shard"), axis=0, tiled=True)
    keyval_all = keyval_all.reshape(
        section_count, micro_count, image_count, 2, keyval_heads, head_dim
    )

    same_document = text_document[:, :, None] == image_document[:, None, :]
    stream = text_queries.astype(jnp.float32)
    streams = [stream]
    for layer in range(section_count):
        stream = forward_layer(
            stream,
            gains_all[layer],
            gates_all[layer],
            keyval_all[layer, :, :, 0],
            keyval_all[layer, :, :, 1],
            same_document,
            head_count,
        )
        streams.append(stream)
    entering = lax.select_n(section_index, *streams[:-1])
    leaving = lax.select_n(section_index, *streams[1:])

    own = lax.dynamic_index_in_dim(keyval_all, section_index, 0, keepdims=False)
    grad_local = backward_layer(
        entering,
        query_gain[0],
        own[:, :, 0],
        own[:, :, 1],
        same_document,
        cotangent[0],
        head_count,
    )
    grad_rows = lax.psum_scatter(
        grad_local.astype(jnp.bfloat16), "shard", scatter_dimension=0, tiled=True
    ).astype(jnp.float32)
    key_portion = norm_gradient(
        raw_rows[:, :key_width], key_norm_gain[0], grad_rows[:, :key_width], keyval_heads
    )
    raw_grad_rows = jnp.concatenate([key_portion, grad_rows[:, key_width:]], axis=1).astype(
        jnp.bfloat16
    )
    raw_grad = lax.all_gather(raw_grad_rows, "shard", axis=0, tiled=True)
    image_part = lax.dot_general(
        raw_grad, weights, (((1,), (1,)), ((), ())), preferred_element_type=jnp.float32
    )
    image_part = image_part.reshape(micro_count, image_count, weights.shape[0])
    image_grad = lax.psum_scatter(
        image_part.astype(jnp.bfloat16), "section", scatter_dimension=1, tiled=True
    ).astype(jnp.float32)
    return (leaving[None], image_grad)


def solution(mesh):
    placed = (
        P("group", "section", "shard"),
        P("section", "shard", None),
        P("section", None),
        P("section", None),
        P("section", None),
        P("group", "shard", None),
        P("group", "shard"),
        P("group", None),
        P("section", "group", "shard", None),
    )
    return jax.shard_map(
        per_device,
        mesh=mesh,
        in_specs=placed,
        out_specs=(P("section", "group", "shard", None), P("group", "section", "shard")),
        check_vma=False,
    )
```

```python
import functools
import math

import jax
import jax.numpy as jnp
from jax import lax
from jax.experimental import pallas as pl
from jax.experimental.pallas import tpu as pltpu
from jax.sharding import PartitionSpec as P

epsilon = 1e-05


def head_normalize(input_rows, gain_row, head_count):
    shaped = input_rows.reshape(input_rows.shape[:-1] + (head_count, -1))
    factor = lax.rsqrt(jnp.mean(shaped * shaped, axis=-1, keepdims=True) + epsilon)
    gain = gain_row.reshape((1,) * (shaped.ndim - 2) + (head_count, -1))
    return (shaped * factor * gain).reshape(input_rows.shape)


def norm_gradient(input_rows, gain_row, incoming_gradient, head_count):
    shaped = input_rows.reshape(input_rows.shape[0], head_count, -1)
    scaled = incoming_gradient.reshape(input_rows.shape[0], head_count, -1) * gain_row.reshape(
        1, head_count, -1
    )
    factor = lax.rsqrt(jnp.mean(shaped * shaped, axis=-1, keepdims=True) + epsilon)
    inner_mean = jnp.mean(shaped * scaled, axis=-1, keepdims=True)
    result = factor * scaled - shaped * factor * factor * factor * inner_mean
    return result.reshape(input_rows.shape[0], -1)


def attention_kernel(
    section_ref,
    gates_ref,
    queries_ref,
    keyval_ref,
    gains_ref,
    mask_ref,
    mask_t_ref,
    cot_ref,
    out_ref,
    grad_ref,
    *,
    head_count,
    keyval_heads,
):
    token_count, query_width = out_ref.shape
    head_dim = query_width // head_count
    key_width = keyval_heads * head_dim
    groups = head_count // keyval_heads
    scale = 1.0 / math.sqrt(head_dim)
    section = section_ref[0]
    out_ref[...] = queries_ref[...].astype(jnp.float32)

    def head_cols(h):
        return pl.ds(h * head_dim, head_dim)

    def queries_of(layer, k):
        parts = []
        for g in range(groups):
            h = k * groups + g
            x = out_ref[:, head_cols(h)]
            mean_square = jnp.sum(x * x, axis=-1, keepdims=True) * (1.0 / head_dim)
            gain = gains_ref[layer, :, head_cols(h)]
            parts.append((x * lax.rsqrt(mean_square + epsilon) * gain).astype(jnp.bfloat16))
        return jnp.concatenate(parts, axis=0)

    def forward(layer):
        same = mask_ref[...] > 0.5
        for k in range(keyval_heads):
            query = queries_of(layer, k)
            key = keyval_ref[layer, :, head_cols(k)]
            value = keyval_ref[layer, :, pl.ds(key_width + k * head_dim, head_dim)]
            scores = lax.dot_general(
                query, key, (((1,), (1,)), ((), ())), preferred_element_type=jnp.float32
            ) * scale
            scores = jnp.where(same, scores, -jnp.inf)
            powered = jnp.exp(scores - jnp.max(scores, axis=-1, keepdims=True))
            probs = powered / jnp.sum(powered, axis=-1, keepdims=True)
            attended = jnp.dot(
                probs.astype(jnp.bfloat16), value, preferred_element_type=jnp.float32
            )
            for g in range(groups):
                h = k * groups + g
                rows = attended[g * token_count : (g + 1) * token_count]
                out_ref[:, head_cols(h)] = out_ref[:, head_cols(h)] + gates_ref[layer, h] * rows

    def layer_step(layer, carry):
        forward(layer)
        return carry

    lax.fori_loop(0, section, layer_step, 0)

    same_t = mask_t_ref[...] > 0.5
    for k in range(keyval_heads):
        query = queries_of(section, k)
        key = keyval_ref[section, :, head_cols(k)]
        value = keyval_ref[section, :, pl.ds(key_width + k * head_dim, head_dim)]
        scores_t = lax.dot_general(
            key, query, (((1,), (1,)), ((), ())), preferred_element_type=jnp.float32
        ) * scale
        scores_t = jnp.where(same_t, scores_t, -jnp.inf)
        powered = jnp.exp(scores_t - jnp.max(scores_t, axis=0, keepdims=True))
        probs_t = powered / jnp.sum(powered, axis=0, keepdims=True)
        upstream = jnp.concatenate(
            [cot_ref[:, head_cols(k * groups + g)] for g in range(groups)], axis=0
        )
        value_grad = jnp.dot(
            probs_t.astype(jnp.bfloat16), upstream, preferred_element_type=jnp.float32
        )
        prob_grad_t = lax.dot_general(
            value, upstream, (((1,), (1,)), ((), ())), preferred_element_type=jnp.float32
        )
        inner = jnp.sum(probs_t * prob_grad_t, axis=0, keepdims=True)
        score_grad_t = (probs_t * (prob_grad_t - inner)).astype(jnp.bfloat16)
        key_grad = jnp.dot(score_grad_t, query, preferred_element_type=jnp.float32) * scale
        grad_ref[:, head_cols(k)] = key_grad
        grad_ref[:, pl.ds(key_width + k * head_dim, head_dim)] = value_grad

    forward(section)


def attention_layers(section_index, gates, queries, keyval_all, gains, same_document, upstream):
    layer_count, micro_count, image_count, pair_width = keyval_all.shape
    token_count, query_width = queries.shape[1], queries.shape[2]
    head_count = gates.shape[1]
    head_dim = query_width // head_count
    keyval_heads = pair_width // 2 // head_dim
    groups = head_count // keyval_heads
    mask = jnp.tile(same_document.astype(jnp.float32), (1, groups, 1))
    mask_t = jnp.swapaxes(mask, 1, 2)
    smem = pl.BlockSpec(memory_space=pltpu.SMEM)
    flops = 2 * micro_count * (layer_count + 3) * head_count * token_count * image_count * head_dim * 2
    return pl.pallas_call(
        functools.partial(attention_kernel, head_count=head_count, keyval_heads=keyval_heads),
        grid=(micro_count,),
        in_specs=[
            smem,
            smem,
            pl.BlockSpec((None, token_count, query_width), lambda m: (m, 0, 0)),
            pl.BlockSpec((layer_count, None, image_count, pair_width), lambda m: (0, m, 0, 0)),
            pl.BlockSpec((layer_count, 1, query_width), lambda m: (0, 0, 0)),
            pl.BlockSpec((None, groups * token_count, image_count), lambda m: (m, 0, 0)),
            pl.BlockSpec((None, image_count, groups * token_count), lambda m: (m, 0, 0)),
            pl.BlockSpec((None, token_count, query_width), lambda m: (m, 0, 0)),
        ],
        out_specs=[
            pl.BlockSpec((None, token_count, query_width), lambda m: (m, 0, 0)),
            pl.BlockSpec((None, image_count, pair_width), lambda m: (m, 0, 0)),
        ],
        out_shape=[
            jax.ShapeDtypeStruct((micro_count, token_count, query_width), jnp.float32),
            jax.ShapeDtypeStruct((micro_count, image_count, pair_width), jnp.float32),
        ],
        compiler_params=pltpu.CompilerParams(dimension_semantics=("arbitrary",)),
        cost_estimate=pl.CostEstimate(
            flops=flops,
            transcendentals=micro_count * (layer_count + 1) * head_count * token_count * image_count,
            bytes_accessed=keyval_all.size * 2 + queries.size * 8 + upstream.size * 2,
        ),
    )(
        jnp.reshape(section_index, (1,)).astype(jnp.int32),
        gates,
        queries,
        keyval_all,
        gains.reshape(layer_count, 1, query_width),
        mask,
        mask_t,
        upstream,
    )


def per_device(
    image_tokens,
    keyval_weight,
    query_gain,
    key_norm_gain,
    gate_logit,
    text_queries,
    text_document,
    image_document,
    cotangent,
):
    section_count = lax.axis_size("section")
    section_index = lax.axis_index("section")
    micro_count = text_queries.shape[0]
    head_count = gate_logit.shape[1]
    key_width = key_norm_gain.shape[1]
    head_dim = query_gain.shape[1] // head_count
    keyval_heads = key_width // head_dim
    weights = keyval_weight[0]

    layer_params = lax.all_gather(
        jnp.concatenate([query_gain, gate_logit], axis=1), "section", axis=0, tiled=True
    )
    gains_all = layer_params[:, : query_gain.shape[1]]
    gates_all = layer_params[:, query_gain.shape[1] :]

    gathered = lax.all_gather(image_tokens, "section", axis=1, tiled=True)
    image_count = gathered.shape[1]
    total_rows = micro_count * image_count
    flat_rows = gathered.reshape(total_rows, gathered.shape[2])
    partial = jnp.dot(flat_rows, weights, preferred_element_type=jnp.float32)
    raw_rows = lax.psum_scatter(partial, "shard", scatter_dimension=0, tiled=True)
    key_rows = head_normalize(raw_rows[:, :key_width], key_norm_gain[0], keyval_heads)
    keyval_rows = jnp.concatenate(
        [key_rows.astype(jnp.bfloat16), raw_rows[:, key_width:].astype(jnp.bfloat16)], axis=1
    )
    keyval_all = lax.all_gather(keyval_rows, ("section", "shard"), axis=0, tiled=True)

    same_document = text_document[:, :, None] == image_document[:, None, :]
    leaving, grad_local = attention_layers(
        section_index,
        jnp.tanh(gates_all),
        text_queries,
        keyval_all.reshape(section_count, micro_count, image_count, 2 * key_width),
        gains_all,
        same_document,
        cotangent[0],
    )
    grad_local = grad_local.reshape(total_rows, 2 * key_width)
    grad_rows = lax.psum_scatter(
        grad_local.astype(jnp.bfloat16), "shard", scatter_dimension=0, tiled=True
    ).astype(jnp.float32)
    key_portion = norm_gradient(
        raw_rows[:, :key_width], key_norm_gain[0], grad_rows[:, :key_width], keyval_heads
    )
    raw_grad_rows = jnp.concatenate([key_portion, grad_rows[:, key_width:]], axis=1).astype(
        jnp.bfloat16
    )
    raw_grad = lax.all_gather(raw_grad_rows, "shard", axis=0, tiled=True)
    image_part = lax.dot_general(
        raw_grad, weights, (((1,), (1,)), ((), ())), preferred_element_type=jnp.float32
    )
    image_part = image_part.reshape(micro_count, image_count, weights.shape[0])
    image_grad = lax.psum_scatter(
        image_part.astype(jnp.bfloat16), "section", scatter_dimension=1, tiled=True
    ).astype(jnp.float32)
    return (leaving[None], image_grad)


def solution(mesh):
    placed = (
        P("group", "section", "shard"),
        P("section", "shard", None),
        P("section", None),
        P("section", None),
        P("section", None),
        P("group", "shard", None),
        P("group", "shard"),
        P("group", None),
        P("section", "group", "shard", None),
    )
    return jax.shard_map(
        per_device,
        mesh=mesh,
        in_specs=placed,
        out_specs=(P("section", "group", "shard", None), P("group", "section", "shard")),
        check_vma=False,
    )
```

```python
import functools
import math

import jax
import jax.numpy as jnp
from jax import lax
from jax.experimental import pallas as pl
from jax.experimental.pallas import tpu as pltpu
from jax.sharding import PartitionSpec as P

epsilon = 1e-05


def head_normalize(input_rows, gain_row, head_count):
    shaped = input_rows.reshape(input_rows.shape[:-1] + (head_count, -1))
    factor = lax.rsqrt(jnp.mean(shaped * shaped, axis=-1, keepdims=True) + epsilon)
    gain = gain_row.reshape((1,) * (shaped.ndim - 2) + (head_count, -1))
    return (shaped * factor * gain).reshape(input_rows.shape)


def norm_gradient(input_rows, gain_row, incoming_gradient, head_count):
    shaped = input_rows.reshape(input_rows.shape[0], head_count, -1)
    scaled = incoming_gradient.reshape(input_rows.shape[0], head_count, -1) * gain_row.reshape(
        1, head_count, -1
    )
    factor = lax.rsqrt(jnp.mean(shaped * shaped, axis=-1, keepdims=True) + epsilon)
    inner_mean = jnp.mean(shaped * scaled, axis=-1, keepdims=True)
    result = factor * scaled - shaped * factor * factor * factor * inner_mean
    return result.reshape(input_rows.shape[0], -1)


def attention_kernel(
    section_ref,
    gates_ref,
    queries_ref,
    keyval_ref,
    gains_ref,
    mask_ref,
    mask_t_ref,
    cot_ref,
    out_ref,
    grad_ref,
    *,
    head_count,
    keyval_heads,
):
    token_count, query_width = out_ref.shape
    head_dim = query_width // head_count
    key_width = keyval_heads * head_dim
    groups = head_count // keyval_heads
    scale = 1.0 / math.sqrt(head_dim)
    section = section_ref[0]
    out_ref[...] = queries_ref[...].astype(jnp.float32)

    def head_cols(h):
        return pl.ds(h * head_dim, head_dim)

    def queries_of(layer, k):
        parts = []
        for g in range(groups):
            h = k * groups + g
            x = out_ref[:, head_cols(h)]
            mean_square = jnp.sum(x * x, axis=-1, keepdims=True) * (1.0 / head_dim)
            gain = gains_ref[layer, :, head_cols(h)]
            parts.append((x * lax.rsqrt(mean_square + epsilon) * gain).astype(jnp.bfloat16))
        return jnp.concatenate(parts, axis=0)

    def forward(layer):
        same = mask_ref[...] > 0.5
        for k in range(keyval_heads):
            query = queries_of(layer, k)
            key = keyval_ref[layer, :, head_cols(k)]
            value = keyval_ref[layer, :, pl.ds(key_width + k * head_dim, head_dim)]
            scores = lax.dot_general(
                query, key, (((1,), (1,)), ((), ())), preferred_element_type=jnp.float32
            ) * scale
            scores = jnp.where(same, scores, -jnp.inf)
            powered = jnp.exp(scores - jnp.max(scores, axis=-1, keepdims=True))
            probs = powered / jnp.sum(powered, axis=-1, keepdims=True)
            attended = jnp.dot(
                probs.astype(jnp.bfloat16), value, preferred_element_type=jnp.float32
            )
            for g in range(groups):
                h = k * groups + g
                rows = attended[g * token_count : (g + 1) * token_count]
                out_ref[:, head_cols(h)] = out_ref[:, head_cols(h)] + gates_ref[layer, h] * rows

    def layer_step(layer, carry):
        forward(layer)
        return carry

    lax.fori_loop(0, section, layer_step, 0)

    same_t = mask_t_ref[...] > 0.5
    for k in range(keyval_heads):
        query = queries_of(section, k)
        key = keyval_ref[section, :, head_cols(k)]
        value = keyval_ref[section, :, pl.ds(key_width + k * head_dim, head_dim)]
        scores_t = lax.dot_general(
            key, query, (((1,), (1,)), ((), ())), preferred_element_type=jnp.float32
        ) * scale
        scores_t = jnp.where(same_t, scores_t, -jnp.inf)
        powered = jnp.exp(scores_t - jnp.max(scores_t, axis=0, keepdims=True))
        probs_t = powered / jnp.sum(powered, axis=0, keepdims=True)
        upstream = jnp.concatenate(
            [cot_ref[:, head_cols(k * groups + g)] for g in range(groups)], axis=0
        )
        value_grad = jnp.dot(
            probs_t.astype(jnp.bfloat16), upstream, preferred_element_type=jnp.float32
        )
        prob_grad_t = lax.dot_general(
            value, upstream, (((1,), (1,)), ((), ())), preferred_element_type=jnp.float32
        )
        inner = jnp.sum(probs_t * prob_grad_t, axis=0, keepdims=True)
        score_grad_t = (probs_t * (prob_grad_t - inner)).astype(jnp.bfloat16)
        key_grad = jnp.dot(score_grad_t, query, preferred_element_type=jnp.float32) * scale
        grad_ref[:, head_cols(k)] = key_grad
        grad_ref[:, pl.ds(key_width + k * head_dim, head_dim)] = value_grad

    forward(section)


def attention_layers(section_index, gates, queries, keyval_all, gains, same_document, upstream):
    layer_count, micro_count, image_count, pair_width = keyval_all.shape
    token_count, query_width = queries.shape[1], queries.shape[2]
    head_count = gates.shape[1]
    head_dim = query_width // head_count
    keyval_heads = pair_width // 2 // head_dim
    groups = head_count // keyval_heads
    mask = jnp.tile(same_document.astype(jnp.float32), (1, groups, 1))
    mask_t = jnp.swapaxes(mask, 1, 2)
    smem = pl.BlockSpec(memory_space=pltpu.SMEM)
    flops = 2 * micro_count * (layer_count + 3) * head_count * token_count * image_count * head_dim * 2
    return pl.pallas_call(
        functools.partial(attention_kernel, head_count=head_count, keyval_heads=keyval_heads),
        grid=(micro_count,),
        in_specs=[
            smem,
            smem,
            pl.BlockSpec((None, token_count, query_width), lambda m: (m, 0, 0)),
            pl.BlockSpec((layer_count, None, image_count, pair_width), lambda m: (0, m, 0, 0)),
            pl.BlockSpec((layer_count, 1, query_width), lambda m: (0, 0, 0)),
            pl.BlockSpec((None, groups * token_count, image_count), lambda m: (m, 0, 0)),
            pl.BlockSpec((None, image_count, groups * token_count), lambda m: (m, 0, 0)),
            pl.BlockSpec((None, token_count, query_width), lambda m: (m, 0, 0)),
        ],
        out_specs=[
            pl.BlockSpec((None, token_count, query_width), lambda m: (m, 0, 0)),
            pl.BlockSpec((None, image_count, pair_width), lambda m: (m, 0, 0)),
        ],
        out_shape=[
            jax.ShapeDtypeStruct((micro_count, token_count, query_width), jnp.float32),
            jax.ShapeDtypeStruct((micro_count, image_count, pair_width), jnp.float32),
        ],
        compiler_params=pltpu.CompilerParams(dimension_semantics=("arbitrary",)),
        cost_estimate=pl.CostEstimate(
            flops=flops,
            transcendentals=micro_count * (layer_count + 1) * head_count * token_count * image_count,
            bytes_accessed=keyval_all.size * 2 + queries.size * 8 + upstream.size * 2,
        ),
    )(
        jnp.reshape(section_index, (1,)).astype(jnp.int32),
        gates,
        queries,
        keyval_all,
        gains.reshape(layer_count, 1, query_width),
        mask,
        mask_t,
        upstream,
    )


def gather_blocks(block, axis):
    count = lax.axis_size(axis)
    if count > 8:
        return lax.all_gather(block, axis, axis=0, tiled=False)
    index = lax.axis_index(axis)
    received = [block] + [
        lax.ppermute(block, axis, [(i, (i + d) % count) for i in range(count)])
        for d in range(1, count)
    ]
    stacked = jnp.stack(received)
    return jnp.take(stacked, (index - jnp.arange(count)) % count, axis=0)


def scatter_blocks(blocks, axis):
    count = lax.axis_size(axis)
    if count > 8:
        return lax.psum_scatter(blocks, axis, scatter_dimension=0, tiled=True)[0].astype(
            jnp.float32
        )
    index = lax.axis_index(axis)
    total = lax.dynamic_index_in_dim(blocks, index, 0, keepdims=False).astype(jnp.float32)
    for d in range(1, count):
        part = lax.dynamic_index_in_dim(blocks, (index + d) % count, 0, keepdims=False)
        total = total + lax.ppermute(
            part, axis, [(i, (i + d) % count) for i in range(count)]
        ).astype(jnp.float32)
    return total


def per_device(
    image_tokens,
    keyval_weight,
    query_gain,
    key_norm_gain,
    gate_logit,
    text_queries,
    text_document,
    image_document,
    cotangent,
):
    section_count = lax.axis_size("section")
    section_index = lax.axis_index("section")
    micro_count = text_queries.shape[0]
    head_count = gate_logit.shape[1]
    key_width = key_norm_gain.shape[1]
    head_dim = query_gain.shape[1] // head_count
    keyval_heads = key_width // head_dim
    weights = keyval_weight[0]

    layer_params = lax.all_gather(
        jnp.concatenate([query_gain, gate_logit], axis=1), "section", axis=0, tiled=True
    )
    gains_all = layer_params[:, : query_gain.shape[1]]
    gates_all = layer_params[:, query_gain.shape[1] :]

    gathered = lax.all_gather(image_tokens, "section", axis=1, tiled=True)
    shard_count = lax.axis_size("shard")
    image_count = gathered.shape[1]
    total_rows = micro_count * image_count
    flat_rows = gathered.reshape(total_rows, gathered.shape[2])
    partial = jnp.dot(flat_rows, weights, preferred_element_type=jnp.float32)
    raw_rows = scatter_blocks(
        partial.reshape(shard_count, total_rows // shard_count, 2 * key_width), "shard"
    )
    key_rows = head_normalize(raw_rows[:, :key_width], key_norm_gain[0], keyval_heads)
    keyval_rows = jnp.concatenate(
        [key_rows.astype(jnp.bfloat16), raw_rows[:, key_width:].astype(jnp.bfloat16)], axis=1
    )
    keyval_own = gather_blocks(keyval_rows, "shard").reshape(total_rows, 2 * key_width)
    keyval_all = gather_blocks(keyval_own, "section")

    same_document = text_document[:, :, None] == image_document[:, None, :]
    leaving, grad_local = attention_layers(
        section_index,
        jnp.tanh(gates_all),
        text_queries,
        keyval_all.reshape(section_count, micro_count, image_count, 2 * key_width),
        gains_all,
        same_document,
        cotangent[0],
    )
    grad_rows = scatter_blocks(
        grad_local.astype(jnp.bfloat16).reshape(
            shard_count, total_rows // shard_count, 2 * key_width
        ),
        "shard",
    )
    key_portion = norm_gradient(
        raw_rows[:, :key_width], key_norm_gain[0], grad_rows[:, :key_width], keyval_heads
    )
    raw_grad_rows = jnp.concatenate([key_portion, grad_rows[:, key_width:]], axis=1).astype(
        jnp.bfloat16
    )
    raw_grad = gather_blocks(raw_grad_rows, "shard").reshape(total_rows, 2 * key_width)
    owned = image_count // section_count
    raw_grad = (
        raw_grad.reshape(micro_count, section_count, owned, 2 * key_width)
        .transpose(1, 0, 2, 3)
        .reshape(total_rows, 2 * key_width)
    )
    image_part = lax.dot_general(
        raw_grad, weights, (((1,), (1,)), ((), ())), preferred_element_type=jnp.float32
    )
    image_part = image_part.astype(jnp.bfloat16).reshape(
        section_count, micro_count, owned, weights.shape[0]
    )
    image_grad = scatter_blocks(image_part, "section")
    return (leaving[None], image_grad)


def solution(mesh):
    placed = (
        P("group", "section", "shard"),
        P("section", "shard", None),
        P("section", None),
        P("section", None),
        P("section", None),
        P("group", "shard", None),
        P("group", "shard"),
        P("group", None),
        P("section", "group", "shard", None),
    )
    return jax.shard_map(
        per_device,
        mesh=mesh,
        in_specs=placed,
        out_specs=(P("section", "group", "shard", None), P("group", "section", "shard")),
        check_vma=False,
    )
```

```python
import functools
import math

import jax
import jax.numpy as jnp
from jax import lax
from jax.experimental import pallas as pl
from jax.experimental.pallas import tpu as pltpu
from jax.sharding import PartitionSpec as P

epsilon = 1e-05


def head_normalize(input_rows, gain_row, head_count):
    shaped = input_rows.reshape(input_rows.shape[:-1] + (head_count, -1))
    factor = lax.rsqrt(jnp.mean(shaped * shaped, axis=-1, keepdims=True) + epsilon)
    gain = gain_row.reshape((1,) * (shaped.ndim - 2) + (head_count, -1))
    return (shaped * factor * gain).reshape(input_rows.shape)


def norm_gradient(input_rows, gain_row, incoming_gradient, head_count):
    shaped = input_rows.reshape(input_rows.shape[0], head_count, -1)
    scaled = incoming_gradient.reshape(input_rows.shape[0], head_count, -1) * gain_row.reshape(
        1, head_count, -1
    )
    factor = lax.rsqrt(jnp.mean(shaped * shaped, axis=-1, keepdims=True) + epsilon)
    inner_mean = jnp.mean(shaped * scaled, axis=-1, keepdims=True)
    result = factor * scaled - shaped * factor * factor * factor * inner_mean
    return result.reshape(input_rows.shape[0], -1)


def attention_kernel(
    section_ref,
    slots_ref,
    gates_ref,
    queries_ref,
    keyval_ref,
    gains_ref,
    mask_ref,
    mask_t_ref,
    cot_ref,
    out_ref,
    grad_ref,
    *,
    head_count,
    keyval_heads,
):
    token_count, query_width = out_ref.shape
    head_dim = query_width // head_count
    key_width = keyval_heads * head_dim
    groups = head_count // keyval_heads
    scale = 1.0 / math.sqrt(head_dim)
    section = section_ref[0]
    out_ref[...] = queries_ref[...].astype(jnp.float32)

    def head_cols(h):
        return pl.ds(h * head_dim, head_dim)

    def queries_of(slot, k):
        parts = []
        for g in range(groups):
            h = k * groups + g
            x = out_ref[:, head_cols(h)]
            mean_square = jnp.sum(x * x, axis=-1, keepdims=True) * (1.0 / head_dim)
            gain = gains_ref[slot, :, head_cols(h)]
            parts.append((x * lax.rsqrt(mean_square + epsilon) * gain).astype(jnp.bfloat16))
        return jnp.concatenate(parts, axis=0)

    def forward(layer):
        slot = slots_ref[layer]
        same = mask_ref[...] > 0.5
        for k in range(keyval_heads):
            query = queries_of(slot, k)
            key = keyval_ref[slot, :, head_cols(k)]
            value = keyval_ref[slot, :, pl.ds(key_width + k * head_dim, head_dim)]
            scores = lax.dot_general(
                query, key, (((1,), (1,)), ((), ())), preferred_element_type=jnp.float32
            ) * scale
            scores = jnp.where(same, scores, -jnp.inf)
            powered = jnp.exp(scores - jnp.max(scores, axis=-1, keepdims=True))
            probs = powered / jnp.sum(powered, axis=-1, keepdims=True)
            attended = jnp.dot(
                probs.astype(jnp.bfloat16), value, preferred_element_type=jnp.float32
            )
            for g in range(groups):
                h = k * groups + g
                rows = attended[g * token_count : (g + 1) * token_count]
                out_ref[:, head_cols(h)] = out_ref[:, head_cols(h)] + gates_ref[slot, h] * rows

    def layer_step(layer, carry):
        forward(layer)
        return carry

    lax.fori_loop(0, section, layer_step, 0)

    same_t = mask_t_ref[...] > 0.5
    own = slots_ref[section]
    for k in range(keyval_heads):
        query = queries_of(own, k)
        key = keyval_ref[own, :, head_cols(k)]
        value = keyval_ref[own, :, pl.ds(key_width + k * head_dim, head_dim)]
        scores_t = lax.dot_general(
            key, query, (((1,), (1,)), ((), ())), preferred_element_type=jnp.float32
        ) * scale
        scores_t = jnp.where(same_t, scores_t, -jnp.inf)
        powered = jnp.exp(scores_t - jnp.max(scores_t, axis=0, keepdims=True))
        probs_t = powered / jnp.sum(powered, axis=0, keepdims=True)
        upstream = jnp.concatenate(
            [cot_ref[:, head_cols(k * groups + g)] for g in range(groups)], axis=0
        )
        value_grad = jnp.dot(
            probs_t.astype(jnp.bfloat16), upstream, preferred_element_type=jnp.float32
        )
        prob_grad_t = lax.dot_general(
            value, upstream, (((1,), (1,)), ((), ())), preferred_element_type=jnp.float32
        )
        inner = jnp.sum(probs_t * prob_grad_t, axis=0, keepdims=True)
        score_grad_t = (probs_t * (prob_grad_t - inner)).astype(jnp.bfloat16)
        key_grad = jnp.dot(score_grad_t, query, preferred_element_type=jnp.float32) * scale
        grad_ref[:, head_cols(k)] = key_grad
        grad_ref[:, pl.ds(key_width + k * head_dim, head_dim)] = value_grad

    forward(section)


def attention_layers(
    section_index, layer_slots, gates, queries, keyval_all, gains, same_document, upstream
):
    layer_count, micro_count, image_count, pair_width = keyval_all.shape
    token_count, query_width = queries.shape[1], queries.shape[2]
    head_count = gates.shape[1]
    head_dim = query_width // head_count
    keyval_heads = pair_width // 2 // head_dim
    groups = head_count // keyval_heads
    mask = jnp.tile(same_document.astype(jnp.float32), (1, groups, 1))
    mask_t = jnp.swapaxes(mask, 1, 2)
    smem = pl.BlockSpec(memory_space=pltpu.SMEM)
    flops = 2 * micro_count * (layer_count + 3) * head_count * token_count * image_count * head_dim * 2
    return pl.pallas_call(
        functools.partial(attention_kernel, head_count=head_count, keyval_heads=keyval_heads),
        grid=(micro_count,),
        in_specs=[
            smem,
            smem,
            smem,
            pl.BlockSpec((None, token_count, query_width), lambda m: (m, 0, 0)),
            pl.BlockSpec((layer_count, None, image_count, pair_width), lambda m: (0, m, 0, 0)),
            pl.BlockSpec((layer_count, 1, query_width), lambda m: (0, 0, 0)),
            pl.BlockSpec((None, groups * token_count, image_count), lambda m: (m, 0, 0)),
            pl.BlockSpec((None, image_count, groups * token_count), lambda m: (m, 0, 0)),
            pl.BlockSpec((None, token_count, query_width), lambda m: (m, 0, 0)),
        ],
        out_specs=[
            pl.BlockSpec((None, token_count, query_width), lambda m: (m, 0, 0)),
            pl.BlockSpec((None, image_count, pair_width), lambda m: (m, 0, 0)),
        ],
        out_shape=[
            jax.ShapeDtypeStruct((micro_count, token_count, query_width), jnp.float32),
            jax.ShapeDtypeStruct((micro_count, image_count, pair_width), jnp.float32),
        ],
        compiler_params=pltpu.CompilerParams(dimension_semantics=("arbitrary",)),
        cost_estimate=pl.CostEstimate(
            flops=flops,
            transcendentals=micro_count * (layer_count + 1) * head_count * token_count * image_count,
            bytes_accessed=keyval_all.size * 2 + queries.size * 8 + upstream.size * 2,
        ),
    )(
        jnp.reshape(section_index, (1,)).astype(jnp.int32),
        layer_slots.astype(jnp.int32),
        gates,
        queries,
        keyval_all,
        gains.reshape(layer_count, 1, query_width),
        mask,
        mask_t,
        upstream,
    )


def gather_blocks(block, axis):
    count = lax.axis_size(axis)
    index = lax.axis_index(axis)
    positions = jnp.arange(count, dtype=jnp.int32)
    if count > 8:
        return lax.all_gather(block, axis, axis=0, tiled=False), positions
    if count == 4:
        partner = [(i, i ^ 1) for i in range(count)]
        across = lax.ppermute(block, axis, [(i, i ^ 2) for i in range(count)])
        received = [block, lax.ppermute(block, axis, partner), across, lax.ppermute(across, axis, partner)]
        return jnp.stack(received), lax.bitwise_xor(index, positions)
    received = [block] + [
        lax.ppermute(block, axis, [(i, (i + d) % count) for i in range(count)])
        for d in range(1, count)
    ]
    return jnp.stack(received), (index - positions) % count


def in_order(block, axis):
    stacked, slots = gather_blocks(block, axis)
    return jnp.take(stacked, slots, axis=0)


def scatter_blocks(blocks, axis):
    count = lax.axis_size(axis)
    if count > 8:
        return lax.psum_scatter(blocks, axis, scatter_dimension=0, tiled=True)[0].astype(
            jnp.float32
        )
    index = lax.axis_index(axis)

    def pick(i):
        return lax.dynamic_index_in_dim(blocks, i, 0, keepdims=False)

    if count == 4:
        partner = [(i, i ^ 1) for i in range(count)]
        got = lax.ppermute(jnp.stack([pick(index ^ 1), pick(index ^ 3)]), axis, partner)
        theirs = (pick(index ^ 2).astype(jnp.float32) + got[1].astype(jnp.float32)).astype(
            blocks.dtype
        )
        back = lax.ppermute(theirs, axis, [(i, i ^ 2) for i in range(count)])
        return (
            pick(index).astype(jnp.float32)
            + got[0].astype(jnp.float32)
            + back.astype(jnp.float32)
        )
    total = pick(index).astype(jnp.float32)
    for d in range(1, count):
        part = lax.dynamic_index_in_dim(blocks, (index + d) % count, 0, keepdims=False)
        total = total + lax.ppermute(
            part, axis, [(i, (i + d) % count) for i in range(count)]
        ).astype(jnp.float32)
    return total


def per_device(
    image_tokens,
    keyval_weight,
    query_gain,
    key_norm_gain,
    gate_logit,
    text_queries,
    text_document,
    image_document,
    cotangent,
):
    section_count = lax.axis_size("section")
    section_index = lax.axis_index("section")
    micro_count = text_queries.shape[0]
    head_count = gate_logit.shape[1]
    key_width = key_norm_gain.shape[1]
    head_dim = query_gain.shape[1] // head_count
    keyval_heads = key_width // head_dim
    weights = keyval_weight[0]

    layer_params, layer_slots = gather_blocks(
        jnp.concatenate([query_gain, gate_logit], axis=1)[0], "section"
    )
    gains_all = layer_params[:, : query_gain.shape[1]]
    gates_all = layer_params[:, query_gain.shape[1] :]

    gathered = lax.all_gather(image_tokens, "section", axis=1, tiled=True)
    shard_count = lax.axis_size("shard")
    image_count = gathered.shape[1]
    total_rows = micro_count * image_count
    flat_rows = gathered.reshape(total_rows, gathered.shape[2])
    partial = jnp.dot(flat_rows, weights, preferred_element_type=jnp.float32)
    raw_rows = scatter_blocks(
        partial.reshape(shard_count, total_rows // shard_count, 2 * key_width), "shard"
    )
    key_rows = head_normalize(raw_rows[:, :key_width], key_norm_gain[0], keyval_heads)
    keyval_rows = jnp.concatenate(
        [key_rows.astype(jnp.bfloat16), raw_rows[:, key_width:].astype(jnp.bfloat16)], axis=1
    )
    keyval_own = in_order(keyval_rows, "shard").reshape(total_rows, 2 * key_width)
    keyval_all, _ = gather_blocks(keyval_own, "section")

    same_document = text_document[:, :, None] == image_document[:, None, :]
    leaving, grad_local = attention_layers(
        section_index,
        layer_slots,
        jnp.tanh(gates_all),
        text_queries,
        keyval_all.reshape(section_count, micro_count, image_count, 2 * key_width),
        gains_all,
        same_document,
        cotangent[0],
    )
    grad_rows = scatter_blocks(
        grad_local.astype(jnp.bfloat16).reshape(
            shard_count, total_rows // shard_count, 2 * key_width
        ),
        "shard",
    )
    key_portion = norm_gradient(
        raw_rows[:, :key_width], key_norm_gain[0], grad_rows[:, :key_width], keyval_heads
    )
    raw_grad_rows = jnp.concatenate([key_portion, grad_rows[:, key_width:]], axis=1).astype(
        jnp.bfloat16
    )
    raw_grad = in_order(raw_grad_rows, "shard").reshape(total_rows, 2 * key_width)
    owned = image_count // section_count
    raw_grad = (
        raw_grad.reshape(micro_count, section_count, owned, 2 * key_width)
        .transpose(1, 0, 2, 3)
        .reshape(total_rows, 2 * key_width)
    )
    image_part = lax.dot_general(
        raw_grad, weights, (((1,), (1,)), ((), ())), preferred_element_type=jnp.float32
    )
    image_part = image_part.astype(jnp.bfloat16).reshape(
        section_count, micro_count, owned, weights.shape[0]
    )
    image_grad = scatter_blocks(image_part, "section")
    return (leaving[None], image_grad)


def solution(mesh):
    placed = (
        P("group", "section", "shard"),
        P("section", "shard", None),
        P("section", None),
        P("section", None),
        P("section", None),
        P("group", "shard", None),
        P("group", "shard"),
        P("group", None),
        P("section", "group", "shard", None),
    )
    return jax.shard_map(
        per_device,
        mesh=mesh,
        in_specs=placed,
        out_specs=(P("section", "group", "shard", None), P("group", "section", "shard")),
        check_vma=False,
    )
```

```python
import functools
import math

import jax
import jax.numpy as jnp
from jax import lax
from jax.experimental import pallas as pl
from jax.experimental.pallas import tpu as pltpu
from jax.sharding import PartitionSpec as P

epsilon = 1e-05


def head_normalize(input_rows, gain_row, head_count):
    shaped = input_rows.reshape(input_rows.shape[:-1] + (head_count, -1))
    factor = lax.rsqrt(jnp.mean(shaped * shaped, axis=-1, keepdims=True) + epsilon)
    gain = gain_row.reshape((1,) * (shaped.ndim - 2) + (head_count, -1))
    return (shaped * factor * gain).reshape(input_rows.shape)


def norm_gradient(input_rows, gain_row, incoming_gradient, head_count):
    shaped = input_rows.reshape(input_rows.shape[0], head_count, -1)
    scaled = incoming_gradient.reshape(input_rows.shape[0], head_count, -1) * gain_row.reshape(
        1, head_count, -1
    )
    factor = lax.rsqrt(jnp.mean(shaped * shaped, axis=-1, keepdims=True) + epsilon)
    inner_mean = jnp.mean(shaped * scaled, axis=-1, keepdims=True)
    result = factor * scaled - shaped * factor * factor * factor * inner_mean
    return result.reshape(input_rows.shape[0], -1)


def attention_kernel(
    section_ref,
    slots_ref,
    gates_ref,
    queries_ref,
    keyval_ref,
    gains_ref,
    mask_ref,
    mask_t_ref,
    cot_ref,
    out_ref,
    grad_ref,
    *,
    head_count,
    keyval_heads,
):
    token_count, query_width = out_ref.shape
    head_dim = query_width // head_count
    key_width = keyval_heads * head_dim
    groups = head_count // keyval_heads
    scale = 1.0 / math.sqrt(head_dim)
    section = section_ref[0]
    out_ref[...] = queries_ref[...].astype(jnp.float32)

    def head_cols(h):
        return pl.ds(h * head_dim, head_dim)

    def queries_of(slot, k):
        parts = []
        for g in range(groups):
            h = k * groups + g
            x = out_ref[:, head_cols(h)]
            mean_square = jnp.sum(x * x, axis=-1, keepdims=True) * (1.0 / head_dim)
            gain = gains_ref[slot, :, head_cols(h)]
            parts.append((x * lax.rsqrt(mean_square + epsilon) * gain).astype(jnp.bfloat16))
        return jnp.concatenate(parts, axis=0)

    def forward(layer):
        slot = slots_ref[layer]
        same = mask_ref[...] > 0.5
        for k in range(keyval_heads):
            query = queries_of(slot, k)
            key = keyval_ref[slot, :, head_cols(k)]
            value = keyval_ref[slot, :, pl.ds(key_width + k * head_dim, head_dim)]
            scores = lax.dot_general(
                query, key, (((1,), (1,)), ((), ())), preferred_element_type=jnp.float32
            ) * scale
            scores = jnp.where(same, scores, -jnp.inf)
            powered = jnp.exp(scores - jnp.max(scores, axis=-1, keepdims=True))
            probs = powered / jnp.sum(powered, axis=-1, keepdims=True)
            attended = jnp.dot(
                probs.astype(jnp.bfloat16), value, preferred_element_type=jnp.float32
            )
            for g in range(groups):
                h = k * groups + g
                rows = attended[g * token_count : (g + 1) * token_count]
                out_ref[:, head_cols(h)] = out_ref[:, head_cols(h)] + gates_ref[slot, h] * rows

    def layer_step(layer, carry):
        forward(layer)
        return carry

    lax.fori_loop(0, section, layer_step, 0)

    same_t = mask_t_ref[...] > 0.5
    own = slots_ref[section]
    for k in range(keyval_heads):
        query = queries_of(own, k)
        key = keyval_ref[own, :, head_cols(k)]
        value = keyval_ref[own, :, pl.ds(key_width + k * head_dim, head_dim)]
        scores_t = lax.dot_general(
            key, query, (((1,), (1,)), ((), ())), preferred_element_type=jnp.float32
        ) * scale
        scores_t = jnp.where(same_t, scores_t, -jnp.inf)
        powered = jnp.exp(scores_t - jnp.max(scores_t, axis=0, keepdims=True))
        probs_t = powered / jnp.sum(powered, axis=0, keepdims=True)
        upstream = jnp.concatenate(
            [cot_ref[:, head_cols(k * groups + g)] for g in range(groups)], axis=0
        )
        value_grad = jnp.dot(
            probs_t.astype(jnp.bfloat16), upstream, preferred_element_type=jnp.float32
        )
        prob_grad_t = lax.dot_general(
            value, upstream, (((1,), (1,)), ((), ())), preferred_element_type=jnp.float32
        )
        inner = jnp.sum(probs_t * prob_grad_t, axis=0, keepdims=True)
        score_grad_t = (probs_t * (prob_grad_t - inner)).astype(jnp.bfloat16)
        key_grad = jnp.dot(score_grad_t, query, preferred_element_type=jnp.float32) * scale
        grad_ref[:, head_cols(k)] = key_grad.astype(grad_ref.dtype)
        grad_ref[:, pl.ds(key_width + k * head_dim, head_dim)] = value_grad.astype(grad_ref.dtype)

    forward(section)


def attention_layers(
    section_index, layer_slots, gates, queries, keyval_all, gains, same_document, upstream
):
    layer_count, micro_count, image_count, pair_width = keyval_all.shape
    token_count, query_width = queries.shape[1], queries.shape[2]
    head_count = gates.shape[1]
    head_dim = query_width // head_count
    keyval_heads = pair_width // 2 // head_dim
    groups = head_count // keyval_heads
    mask = jnp.tile(same_document.astype(jnp.float32), (1, groups, 1))
    mask_t = jnp.swapaxes(mask, 1, 2)
    smem = pl.BlockSpec(memory_space=pltpu.SMEM)
    flops = 2 * micro_count * (layer_count + 3) * head_count * token_count * image_count * head_dim * 2
    return pl.pallas_call(
        functools.partial(attention_kernel, head_count=head_count, keyval_heads=keyval_heads),
        grid=(micro_count,),
        in_specs=[
            smem,
            smem,
            smem,
            pl.BlockSpec((None, token_count, query_width), lambda m: (m, 0, 0)),
            pl.BlockSpec((layer_count, None, image_count, pair_width), lambda m: (0, m, 0, 0)),
            pl.BlockSpec((layer_count, 1, query_width), lambda m: (0, 0, 0)),
            pl.BlockSpec((None, groups * token_count, image_count), lambda m: (m, 0, 0)),
            pl.BlockSpec((None, image_count, groups * token_count), lambda m: (m, 0, 0)),
            pl.BlockSpec((None, token_count, query_width), lambda m: (m, 0, 0)),
        ],
        out_specs=[
            pl.BlockSpec((None, token_count, query_width), lambda m: (m, 0, 0)),
            pl.BlockSpec((None, image_count, pair_width), lambda m: (m, 0, 0)),
        ],
        out_shape=[
            jax.ShapeDtypeStruct((micro_count, token_count, query_width), jnp.float32),
            jax.ShapeDtypeStruct((micro_count, image_count, pair_width), jnp.bfloat16),
        ],
        compiler_params=pltpu.CompilerParams(dimension_semantics=("arbitrary",)),
        cost_estimate=pl.CostEstimate(
            flops=flops,
            transcendentals=micro_count * (layer_count + 1) * head_count * token_count * image_count,
            bytes_accessed=keyval_all.size * 2 + queries.size * 8 + upstream.size * 2,
        ),
    )(
        jnp.reshape(section_index, (1,)).astype(jnp.int32),
        layer_slots.astype(jnp.int32),
        gates,
        queries,
        keyval_all,
        gains.reshape(layer_count, 1, query_width),
        mask,
        mask_t,
        upstream,
    )


def gather_blocks(block, axis):
    count = lax.axis_size(axis)
    index = lax.axis_index(axis)
    positions = jnp.arange(count, dtype=jnp.int32)
    if count > 8:
        return lax.all_gather(block, axis, axis=0, tiled=False), positions
    if count == 4:
        partner = [(i, i ^ 1) for i in range(count)]
        across = lax.ppermute(block, axis, [(i, i ^ 2) for i in range(count)])
        received = [block, lax.ppermute(block, axis, partner), across, lax.ppermute(across, axis, partner)]
        return jnp.stack(received), lax.bitwise_xor(index, positions)
    received = [block] + [
        lax.ppermute(block, axis, [(i, (i + d) % count) for i in range(count)])
        for d in range(1, count)
    ]
    return jnp.stack(received), (index - positions) % count


def in_order(block, axis):
    stacked, slots = gather_blocks(block, axis)
    return jnp.take(stacked, slots, axis=0)


def scatter_blocks(blocks, axis, pairs):
    count = lax.axis_size(axis)
    if count > 8:
        return lax.psum_scatter(blocks, axis, scatter_dimension=0, tiled=True)[0].astype(
            jnp.float32
        )
    index = lax.axis_index(axis)

    def pick(i):
        return lax.dynamic_index_in_dim(blocks, i, 0, keepdims=False)

    if pairs and count == 4:
        partner = [(i, i ^ 1) for i in range(count)]
        got = lax.ppermute(jnp.stack([pick(index ^ 1), pick(index ^ 3)]), axis, partner)
        theirs = (pick(index ^ 2).astype(jnp.float32) + got[1].astype(jnp.float32)).astype(
            blocks.dtype
        )
        back = lax.ppermute(theirs, axis, [(i, i ^ 2) for i in range(count)])
        return (
            pick(index).astype(jnp.float32)
            + got[0].astype(jnp.float32)
            + back.astype(jnp.float32)
        )
    total = pick(index).astype(jnp.float32)
    for d in range(1, count):
        part = lax.dynamic_index_in_dim(blocks, (index + d) % count, 0, keepdims=False)
        total = total + lax.ppermute(
            part, axis, [(i, (i + d) % count) for i in range(count)]
        ).astype(jnp.float32)
    return total


def per_device(
    image_tokens,
    keyval_weight,
    query_gain,
    key_norm_gain,
    gate_logit,
    text_queries,
    text_document,
    image_document,
    cotangent,
):
    section_count = lax.axis_size("section")
    section_index = lax.axis_index("section")
    micro_count = text_queries.shape[0]
    head_count = gate_logit.shape[1]
    key_width = key_norm_gain.shape[1]
    head_dim = query_gain.shape[1] // head_count
    keyval_heads = key_width // head_dim
    weights = keyval_weight[0]

    layer_params, layer_slots = gather_blocks(
        jnp.concatenate([query_gain, gate_logit], axis=1)[0], "section"
    )
    gains_all = layer_params[:, : query_gain.shape[1]]
    gates_all = layer_params[:, query_gain.shape[1] :]

    gathered = lax.all_gather(image_tokens, "section", axis=1, tiled=True)
    shard_count = lax.axis_size("shard")
    image_count = gathered.shape[1]
    total_rows = micro_count * image_count
    flat_rows = gathered.reshape(total_rows, gathered.shape[2])
    partial = jnp.dot(flat_rows, weights, preferred_element_type=jnp.float32)
    raw_rows = scatter_blocks(
        partial.reshape(shard_count, total_rows // shard_count, 2 * key_width), "shard", False
    )
    key_rows = head_normalize(raw_rows[:, :key_width], key_norm_gain[0], keyval_heads)
    keyval_rows = jnp.concatenate(
        [key_rows.astype(jnp.bfloat16), raw_rows[:, key_width:].astype(jnp.bfloat16)], axis=1
    )
    keyval_own = in_order(keyval_rows, "shard").reshape(total_rows, 2 * key_width)
    keyval_all, _ = gather_blocks(keyval_own, "section")

    same_document = text_document[:, :, None] == image_document[:, None, :]
    leaving, grad_local = attention_layers(
        section_index,
        layer_slots,
        jnp.tanh(gates_all),
        text_queries,
        keyval_all.reshape(section_count, micro_count, image_count, 2 * key_width),
        gains_all,
        same_document,
        cotangent[0],
    )
    grad_rows = scatter_blocks(
        grad_local.reshape(shard_count, total_rows // shard_count, 2 * key_width),
        "shard",
        False,
    )
    key_portion = norm_gradient(
        raw_rows[:, :key_width], key_norm_gain[0], grad_rows[:, :key_width], keyval_heads
    )
    raw_grad_rows = jnp.concatenate([key_portion, grad_rows[:, key_width:]], axis=1).astype(
        jnp.bfloat16
    )
    raw_grad = in_order(raw_grad_rows, "shard").reshape(total_rows, 2 * key_width)
    owned = image_count // section_count
    raw_grad = (
        raw_grad.reshape(micro_count, section_count, owned, 2 * key_width)
        .transpose(1, 0, 2, 3)
        .reshape(total_rows, 2 * key_width)
    )
    image_part = lax.dot_general(
        raw_grad, weights, (((1,), (1,)), ((), ())), preferred_element_type=jnp.float32
    )
    image_part = image_part.astype(jnp.bfloat16).reshape(
        section_count, micro_count, owned, weights.shape[0]
    )
    image_grad = scatter_blocks(image_part, "section", True)
    return (leaving[None], image_grad)


def solution(mesh):
    placed = (
        P("group", "section", "shard"),
        P("section", "shard", None),
        P("section", None),
        P("section", None),
        P("section", None),
        P("group", "shard", None),
        P("group", "shard"),
        P("group", None),
        P("section", "group", "shard", None),
    )
    return jax.shard_map(
        per_device,
        mesh=mesh,
        in_specs=placed,
        out_specs=(P("section", "group", "shard", None), P("group", "section", "shard")),
        check_vma=False,
    )
```

```python
import functools
import math

import jax
import jax.numpy as jnp
from jax import lax
from jax.experimental import pallas as pl
from jax.experimental.pallas import tpu as pltpu
from jax.sharding import PartitionSpec as P

epsilon = 1e-05


def head_normalize(input_rows, gain_row, head_count):
    shaped = input_rows.reshape(input_rows.shape[:-1] + (head_count, -1))
    factor = lax.rsqrt(jnp.mean(shaped * shaped, axis=-1, keepdims=True) + epsilon)
    gain = gain_row.reshape((1,) * (shaped.ndim - 2) + (head_count, -1))
    return (shaped * factor * gain).reshape(input_rows.shape)


def norm_gradient(input_rows, gain_row, incoming_gradient, head_count):
    shaped = input_rows.reshape(input_rows.shape[0], head_count, -1)
    scaled = incoming_gradient.reshape(input_rows.shape[0], head_count, -1) * gain_row.reshape(
        1, head_count, -1
    )
    factor = lax.rsqrt(jnp.mean(shaped * shaped, axis=-1, keepdims=True) + epsilon)
    inner_mean = jnp.mean(shaped * scaled, axis=-1, keepdims=True)
    result = factor * scaled - shaped * factor * factor * factor * inner_mean
    return result.reshape(input_rows.shape[0], -1)


def attention_kernel(
    section_ref,
    slots_ref,
    gates_ref,
    queries_ref,
    keyval_ref,
    gains_ref,
    mask_ref,
    mask_t_ref,
    cot_ref,
    out_ref,
    grad_ref,
    *,
    head_count,
    keyval_heads,
):
    token_count, query_width = out_ref.shape
    head_dim = query_width // head_count
    key_width = keyval_heads * head_dim
    groups = head_count // keyval_heads
    scale = 1.0 / math.sqrt(head_dim)
    section = section_ref[0]
    out_ref[...] = queries_ref[...].astype(jnp.float32)

    def head_cols(h):
        return pl.ds(h * head_dim, head_dim)

    def queries_of(slot, k):
        parts = []
        for g in range(groups):
            h = k * groups + g
            x = out_ref[:, head_cols(h)]
            mean_square = jnp.sum(x * x, axis=-1, keepdims=True) * (1.0 / head_dim)
            gain = gains_ref[slot, :, head_cols(h)]
            parts.append((x * lax.rsqrt(mean_square + epsilon) * gain).astype(jnp.bfloat16))
        return jnp.concatenate(parts, axis=0)

    def forward(layer):
        slot = slots_ref[layer]
        same = mask_ref[...] > 0.5
        for k in range(keyval_heads):
            query = queries_of(slot, k)
            key = keyval_ref[slot, :, head_cols(k)]
            value = keyval_ref[slot, :, pl.ds(key_width + k * head_dim, head_dim)]
            scores = lax.dot_general(
                query, key, (((1,), (1,)), ((), ())), preferred_element_type=jnp.float32
            ) * scale
            scores = jnp.where(same, scores, -jnp.inf)
            powered = jnp.exp(scores - jnp.max(scores, axis=-1, keepdims=True))
            probs = powered / jnp.sum(powered, axis=-1, keepdims=True)
            attended = jnp.dot(
                probs.astype(jnp.bfloat16), value, preferred_element_type=jnp.float32
            )
            for g in range(groups):
                h = k * groups + g
                rows = attended[g * token_count : (g + 1) * token_count]
                out_ref[:, head_cols(h)] = out_ref[:, head_cols(h)] + gates_ref[slot, h] * rows

    def layer_step(layer, carry):
        forward(layer)
        return carry

    lax.fori_loop(0, section, layer_step, 0)

    same_t = mask_t_ref[...] > 0.5
    own = slots_ref[section]
    for k in range(keyval_heads):
        query = queries_of(own, k)
        key = keyval_ref[own, :, head_cols(k)]
        value = keyval_ref[own, :, pl.ds(key_width + k * head_dim, head_dim)]
        scores_t = lax.dot_general(
            key, query, (((1,), (1,)), ((), ())), preferred_element_type=jnp.float32
        ) * scale
        scores_t = jnp.where(same_t, scores_t, -jnp.inf)
        powered = jnp.exp(scores_t - jnp.max(scores_t, axis=0, keepdims=True))
        probs_t = powered / jnp.sum(powered, axis=0, keepdims=True)
        upstream = jnp.concatenate(
            [cot_ref[:, head_cols(k * groups + g)] for g in range(groups)], axis=0
        )
        value_grad = jnp.dot(
            probs_t.astype(jnp.bfloat16), upstream, preferred_element_type=jnp.float32
        )
        prob_grad_t = lax.dot_general(
            value, upstream, (((1,), (1,)), ((), ())), preferred_element_type=jnp.float32
        )
        inner = jnp.sum(probs_t * prob_grad_t, axis=0, keepdims=True)
        score_grad_t = (probs_t * (prob_grad_t - inner)).astype(jnp.bfloat16)
        key_grad = jnp.dot(score_grad_t, query, preferred_element_type=jnp.float32) * scale
        grad_ref[:, head_cols(k)] = key_grad.astype(grad_ref.dtype)
        grad_ref[:, pl.ds(key_width + k * head_dim, head_dim)] = value_grad.astype(grad_ref.dtype)

    forward(section)


def attention_layers(
    section_index, layer_slots, gates, queries, keyval_all, gains, same_document, upstream
):
    layer_count, micro_count, image_count, pair_width = keyval_all.shape
    token_count, query_width = queries.shape[1], queries.shape[2]
    head_count = gates.shape[1]
    head_dim = query_width // head_count
    keyval_heads = pair_width // 2 // head_dim
    groups = head_count // keyval_heads
    mask = jnp.tile(same_document.astype(jnp.float32), (1, groups, 1))
    mask_t = jnp.swapaxes(mask, 1, 2)
    smem = pl.BlockSpec(memory_space=pltpu.SMEM)
    flops = 2 * micro_count * (layer_count + 3) * head_count * token_count * image_count * head_dim * 2
    return pl.pallas_call(
        functools.partial(attention_kernel, head_count=head_count, keyval_heads=keyval_heads),
        grid=(micro_count,),
        in_specs=[
            smem,
            smem,
            smem,
            pl.BlockSpec((None, token_count, query_width), lambda m: (m, 0, 0)),
            pl.BlockSpec((layer_count, None, image_count, pair_width), lambda m: (0, m, 0, 0)),
            pl.BlockSpec((layer_count, 1, query_width), lambda m: (0, 0, 0)),
            pl.BlockSpec((None, groups * token_count, image_count), lambda m: (m, 0, 0)),
            pl.BlockSpec((None, image_count, groups * token_count), lambda m: (m, 0, 0)),
            pl.BlockSpec((None, token_count, query_width), lambda m: (m, 0, 0)),
        ],
        out_specs=[
            pl.BlockSpec((None, token_count, query_width), lambda m: (m, 0, 0)),
            pl.BlockSpec((None, image_count, pair_width), lambda m: (m, 0, 0)),
        ],
        out_shape=[
            jax.ShapeDtypeStruct((micro_count, token_count, query_width), jnp.float32),
            jax.ShapeDtypeStruct((micro_count, image_count, pair_width), jnp.bfloat16),
        ],
        compiler_params=pltpu.CompilerParams(dimension_semantics=("arbitrary",)),
        cost_estimate=pl.CostEstimate(
            flops=flops,
            transcendentals=micro_count * (layer_count + 1) * head_count * token_count * image_count,
            bytes_accessed=keyval_all.size * 2 + queries.size * 8 + upstream.size * 2,
        ),
    )(
        jnp.reshape(section_index, (1,)).astype(jnp.int32),
        layer_slots.astype(jnp.int32),
        gates,
        queries,
        keyval_all,
        gains.reshape(layer_count, 1, query_width),
        mask,
        mask_t,
        upstream,
    )


def gather_blocks(block, axis):
    count = lax.axis_size(axis)
    index = lax.axis_index(axis)
    positions = jnp.arange(count, dtype=jnp.int32)
    if count > 8:
        return lax.all_gather(block, axis, axis=0, tiled=False), positions
    if count == 4:
        partner = [(i, i ^ 1) for i in range(count)]
        across = lax.ppermute(block, axis, [(i, i ^ 2) for i in range(count)])
        received = [block, lax.ppermute(block, axis, partner), across, lax.ppermute(across, axis, partner)]
        return jnp.stack(received), lax.bitwise_xor(index, positions)
    received = [block] + [
        lax.ppermute(block, axis, [(i, (i + d) % count) for i in range(count)])
        for d in range(1, count)
    ]
    return jnp.stack(received), (index - positions) % count


def in_order(block, axis):
    stacked, slots = gather_blocks(block, axis)
    return jnp.take(stacked, slots, axis=0)


def scatter_blocks(blocks, axis, pairs):
    count = lax.axis_size(axis)
    if count > 8:
        return lax.psum_scatter(blocks, axis, scatter_dimension=0, tiled=True)[0].astype(
            jnp.float32
        )
    index = lax.axis_index(axis)

    def pick(i):
        return lax.dynamic_index_in_dim(blocks, i, 0, keepdims=False)

    if pairs and count == 4:
        partner = [(i, i ^ 1) for i in range(count)]
        got = lax.ppermute(jnp.stack([pick(index ^ 1), pick(index ^ 3)]), axis, partner)
        theirs = (pick(index ^ 2).astype(jnp.float32) + got[1].astype(jnp.float32)).astype(
            blocks.dtype
        )
        back = lax.ppermute(theirs, axis, [(i, i ^ 2) for i in range(count)])
        return (
            pick(index).astype(jnp.float32)
            + got[0].astype(jnp.float32)
            + back.astype(jnp.float32)
        )
    total = pick(index).astype(jnp.float32)
    for d in range(1, count):
        part = lax.dynamic_index_in_dim(blocks, (index + d) % count, 0, keepdims=False)
        total = total + lax.ppermute(
            part, axis, [(i, (i + d) % count) for i in range(count)]
        ).astype(jnp.float32)
    return total


def per_device(
    image_tokens,
    keyval_weight,
    query_gain,
    key_norm_gain,
    gate_logit,
    text_queries,
    text_document,
    image_document,
    cotangent,
):
    section_count = lax.axis_size("section")
    section_index = lax.axis_index("section")
    micro_count = text_queries.shape[0]
    head_count = gate_logit.shape[1]
    key_width = key_norm_gain.shape[1]
    head_dim = query_gain.shape[1] // head_count
    keyval_heads = key_width // head_dim
    weights = keyval_weight[0]

    layer_params, layer_slots = gather_blocks(
        jnp.concatenate([query_gain, gate_logit], axis=1)[0], "section"
    )
    gains_all = layer_params[:, : query_gain.shape[1]]
    gates_all = layer_params[:, query_gain.shape[1] :]

    gathered = in_order(image_tokens, "section")
    gathered = gathered.transpose(1, 0, 2, 3).reshape(
        micro_count, -1, image_tokens.shape[2]
    )
    shard_count = lax.axis_size("shard")
    image_count = gathered.shape[1]
    total_rows = micro_count * image_count
    flat_rows = gathered.reshape(total_rows, gathered.shape[2])
    partial = jnp.dot(flat_rows, weights, preferred_element_type=jnp.float32)
    raw_rows = scatter_blocks(
        partial.astype(jnp.bfloat16).reshape(shard_count, total_rows // shard_count, 2 * key_width),
        "shard",
        False,
    )
    key_rows = head_normalize(raw_rows[:, :key_width], key_norm_gain[0], keyval_heads)
    keyval_rows = jnp.concatenate(
        [key_rows.astype(jnp.bfloat16), raw_rows[:, key_width:].astype(jnp.bfloat16)], axis=1
    )
    keyval_own = in_order(keyval_rows, "shard").reshape(total_rows, 2 * key_width)
    keyval_all, _ = gather_blocks(keyval_own, "section")

    same_document = text_document[:, :, None] == image_document[:, None, :]
    leaving, grad_local = attention_layers(
        section_index,
        layer_slots,
        jnp.tanh(gates_all),
        text_queries,
        keyval_all.reshape(section_count, micro_count, image_count, 2 * key_width),
        gains_all,
        same_document,
        cotangent[0],
    )
    grad_rows = scatter_blocks(
        grad_local.reshape(shard_count, total_rows // shard_count, 2 * key_width),
        "shard",
        False,
    )
    key_portion = norm_gradient(
        raw_rows[:, :key_width], key_norm_gain[0], grad_rows[:, :key_width], keyval_heads
    )
    raw_grad_rows = jnp.concatenate([key_portion, grad_rows[:, key_width:]], axis=1).astype(
        jnp.bfloat16
    )
    raw_grad = in_order(raw_grad_rows, "shard").reshape(total_rows, 2 * key_width)
    owned = image_count // section_count
    raw_grad = (
        raw_grad.reshape(micro_count, section_count, owned, 2 * key_width)
        .transpose(1, 0, 2, 3)
        .reshape(total_rows, 2 * key_width)
    )
    image_part = lax.dot_general(
        raw_grad, weights, (((1,), (1,)), ((), ())), preferred_element_type=jnp.float32
    )
    image_part = image_part.astype(jnp.bfloat16).reshape(
        section_count, micro_count, owned, weights.shape[0]
    )
    image_grad = scatter_blocks(image_part, "section", True)
    return (leaving[None], image_grad)


def solution(mesh):
    placed = (
        P("group", "section", "shard"),
        P("section", "shard", None),
        P("section", None),
        P("section", None),
        P("section", None),
        P("group", "shard", None),
        P("group", "shard"),
        P("group", None),
        P("section", "group", "shard", None),
    )
    return jax.shard_map(
        per_device,
        mesh=mesh,
        in_specs=placed,
        out_specs=(P("section", "group", "shard", None), P("group", "section", "shard")),
        check_vma=False,
    )
```

```python
import functools
import math

import jax
import jax.numpy as jnp
from jax import lax
from jax.experimental import pallas as pl
from jax.experimental.pallas import tpu as pltpu
from jax.sharding import PartitionSpec as P

epsilon = 1e-05


def head_normalize(input_rows, gain_row, head_count):
    shaped = input_rows.reshape(input_rows.shape[:-1] + (head_count, -1))
    factor = lax.rsqrt(jnp.mean(shaped * shaped, axis=-1, keepdims=True) + epsilon)
    gain = gain_row.reshape((1,) * (shaped.ndim - 2) + (head_count, -1))
    return (shaped * factor * gain).reshape(input_rows.shape)


def norm_gradient(input_rows, gain_row, incoming_gradient, head_count):
    shaped = input_rows.reshape(input_rows.shape[0], head_count, -1)
    scaled = incoming_gradient.reshape(input_rows.shape[0], head_count, -1) * gain_row.reshape(
        1, head_count, -1
    )
    factor = lax.rsqrt(jnp.mean(shaped * shaped, axis=-1, keepdims=True) + epsilon)
    inner_mean = jnp.mean(shaped * scaled, axis=-1, keepdims=True)
    result = factor * scaled - shaped * factor * factor * factor * inner_mean
    return result.reshape(input_rows.shape[0], -1)


def attention_kernel(
    section_ref,
    slots_ref,
    gates_ref,
    queries_ref,
    keyval_ref,
    gains_ref,
    mask_ref,
    mask_t_ref,
    cot_ref,
    out_ref,
    grad_ref,
    *,
    head_count,
    keyval_heads,
):
    token_count, query_width = out_ref.shape
    head_dim = query_width // head_count
    key_width = keyval_heads * head_dim
    groups = head_count // keyval_heads
    scale = 1.0 / math.sqrt(head_dim)
    section = section_ref[0]
    out_ref[...] = queries_ref[...].astype(jnp.float32)

    def head_cols(h):
        return pl.ds(h * head_dim, head_dim)

    def queries_of(slot, k):
        parts = []
        for g in range(groups):
            h = k * groups + g
            x = out_ref[:, head_cols(h)]
            mean_square = jnp.sum(x * x, axis=-1, keepdims=True) * (1.0 / head_dim)
            gain = gains_ref[slot, :, head_cols(h)]
            parts.append((x * lax.rsqrt(mean_square + epsilon) * gain).astype(jnp.bfloat16))
        return jnp.concatenate(parts, axis=0)

    def forward(layer):
        slot = slots_ref[layer]
        same = mask_ref[...] > 0.5
        for k in range(keyval_heads):
            query = queries_of(slot, k)
            key = keyval_ref[slot, :, head_cols(k)]
            value = keyval_ref[slot, :, pl.ds(key_width + k * head_dim, head_dim)]
            scores = lax.dot_general(
                query, key, (((1,), (1,)), ((), ())), preferred_element_type=jnp.float32
            ) * scale
            scores = jnp.where(same, scores, -jnp.inf)
            powered = jnp.exp(scores - jnp.max(scores, axis=-1, keepdims=True))
            probs = powered * (1.0 / jnp.sum(powered, axis=-1, keepdims=True))
            attended = jnp.dot(
                probs.astype(jnp.bfloat16), value, preferred_element_type=jnp.float32
            )
            for g in range(groups):
                h = k * groups + g
                rows = attended[g * token_count : (g + 1) * token_count]
                out_ref[:, head_cols(h)] = out_ref[:, head_cols(h)] + gates_ref[slot, h] * rows

    def layer_step(layer, carry):
        forward(layer)
        return carry

    lax.fori_loop(0, section, layer_step, 0)

    same_t = mask_t_ref[...] > 0.5
    own = slots_ref[section]
    for k in range(keyval_heads):
        query = queries_of(own, k)
        key = keyval_ref[own, :, head_cols(k)]
        value = keyval_ref[own, :, pl.ds(key_width + k * head_dim, head_dim)]
        scores_t = lax.dot_general(
            key, query, (((1,), (1,)), ((), ())), preferred_element_type=jnp.float32
        ) * scale
        scores_t = jnp.where(same_t, scores_t, -jnp.inf)
        powered = jnp.exp(scores_t - jnp.max(scores_t, axis=0, keepdims=True))
        probs_t = powered * (1.0 / jnp.sum(powered, axis=0, keepdims=True))
        upstream = jnp.concatenate(
            [cot_ref[:, head_cols(k * groups + g)] for g in range(groups)], axis=0
        )
        value_grad = jnp.dot(
            probs_t.astype(jnp.bfloat16), upstream, preferred_element_type=jnp.float32
        )
        prob_grad_t = lax.dot_general(
            value, upstream, (((1,), (1,)), ((), ())), preferred_element_type=jnp.float32
        )
        inner = jnp.sum(probs_t * prob_grad_t, axis=0, keepdims=True)
        score_grad_t = (probs_t * (prob_grad_t - inner)).astype(jnp.bfloat16)
        key_grad = jnp.dot(score_grad_t, query, preferred_element_type=jnp.float32) * scale
        grad_ref[:, head_cols(k)] = key_grad.astype(grad_ref.dtype)
        grad_ref[:, pl.ds(key_width + k * head_dim, head_dim)] = value_grad.astype(grad_ref.dtype)

    forward(section)


def attention_layers(
    section_index, layer_slots, gates, queries, keyval_all, gains, same_document, upstream
):
    layer_count, micro_count, image_count, pair_width = keyval_all.shape
    token_count, query_width = queries.shape[1], queries.shape[2]
    head_count = gates.shape[1]
    head_dim = query_width // head_count
    keyval_heads = pair_width // 2 // head_dim
    groups = head_count // keyval_heads
    mask = jnp.tile(same_document.astype(jnp.float32), (1, groups, 1))
    mask_t = jnp.swapaxes(mask, 1, 2)
    smem = pl.BlockSpec(memory_space=pltpu.SMEM)
    flops = 2 * micro_count * (layer_count + 3) * head_count * token_count * image_count * head_dim * 2
    return pl.pallas_call(
        functools.partial(attention_kernel, head_count=head_count, keyval_heads=keyval_heads),
        grid=(micro_count,),
        in_specs=[
            smem,
            smem,
            smem,
            pl.BlockSpec((None, token_count, query_width), lambda m: (m, 0, 0)),
            pl.BlockSpec((layer_count, None, image_count, pair_width), lambda m: (0, m, 0, 0)),
            pl.BlockSpec((layer_count, 1, query_width), lambda m: (0, 0, 0)),
            pl.BlockSpec((None, groups * token_count, image_count), lambda m: (m, 0, 0)),
            pl.BlockSpec((None, image_count, groups * token_count), lambda m: (m, 0, 0)),
            pl.BlockSpec((None, token_count, query_width), lambda m: (m, 0, 0)),
        ],
        out_specs=[
            pl.BlockSpec((None, token_count, query_width), lambda m: (m, 0, 0)),
            pl.BlockSpec((None, image_count, pair_width), lambda m: (m, 0, 0)),
        ],
        out_shape=[
            jax.ShapeDtypeStruct((micro_count, token_count, query_width), jnp.float32),
            jax.ShapeDtypeStruct((micro_count, image_count, pair_width), jnp.bfloat16),
        ],
        compiler_params=pltpu.CompilerParams(dimension_semantics=("arbitrary",)),
        cost_estimate=pl.CostEstimate(
            flops=flops,
            transcendentals=micro_count * (layer_count + 1) * head_count * token_count * image_count,
            bytes_accessed=keyval_all.size * 2 + queries.size * 8 + upstream.size * 2,
        ),
    )(
        jnp.reshape(section_index, (1,)).astype(jnp.int32),
        layer_slots.astype(jnp.int32),
        gates,
        queries,
        keyval_all,
        gains.reshape(layer_count, 1, query_width),
        mask,
        mask_t,
        upstream,
    )


def gather_blocks(block, axis):
    count = lax.axis_size(axis)
    index = lax.axis_index(axis)
    positions = jnp.arange(count, dtype=jnp.int32)
    if count > 8:
        return lax.all_gather(block, axis, axis=0, tiled=False), positions
    if count == 4:
        partner = [(i, i ^ 1) for i in range(count)]
        across = lax.ppermute(block, axis, [(i, i ^ 2) for i in range(count)])
        received = [block, lax.ppermute(block, axis, partner), across, lax.ppermute(across, axis, partner)]
        return jnp.stack(received), lax.bitwise_xor(index, positions)
    received = [block] + [
        lax.ppermute(block, axis, [(i, (i + d) % count) for i in range(count)])
        for d in range(1, count)
    ]
    return jnp.stack(received), (index - positions) % count


def in_order(block, axis):
    stacked, slots = gather_blocks(block, axis)
    return jnp.take(stacked, slots, axis=0)


def scatter_blocks(blocks, axis, pairs):
    count = lax.axis_size(axis)
    if count > 8:
        return lax.psum_scatter(blocks, axis, scatter_dimension=0, tiled=True)[0].astype(
            jnp.float32
        )
    index = lax.axis_index(axis)

    def pick(i):
        return lax.dynamic_index_in_dim(blocks, i, 0, keepdims=False)

    if pairs and count == 4:
        partner = [(i, i ^ 1) for i in range(count)]
        got = lax.ppermute(jnp.stack([pick(index ^ 1), pick(index ^ 3)]), axis, partner)
        theirs = (pick(index ^ 2).astype(jnp.float32) + got[1].astype(jnp.float32)).astype(
            blocks.dtype
        )
        back = lax.ppermute(theirs, axis, [(i, i ^ 2) for i in range(count)])
        return (
            pick(index).astype(jnp.float32)
            + got[0].astype(jnp.float32)
            + back.astype(jnp.float32)
        )
    total = pick(index).astype(jnp.float32)
    for d in range(1, count):
        part = lax.dynamic_index_in_dim(blocks, (index + d) % count, 0, keepdims=False)
        total = total + lax.ppermute(
            part, axis, [(i, (i + d) % count) for i in range(count)]
        ).astype(jnp.float32)
    return total


def per_device(
    image_tokens,
    keyval_weight,
    query_gain,
    key_norm_gain,
    gate_logit,
    text_queries,
    text_document,
    image_document,
    cotangent,
):
    section_count = lax.axis_size("section")
    section_index = lax.axis_index("section")
    micro_count = text_queries.shape[0]
    head_count = gate_logit.shape[1]
    key_width = key_norm_gain.shape[1]
    head_dim = query_gain.shape[1] // head_count
    keyval_heads = key_width // head_dim
    weights = keyval_weight[0]

    layer_params, layer_slots = gather_blocks(
        jnp.concatenate([query_gain, gate_logit], axis=1)[0], "section"
    )
    gains_all = layer_params[:, : query_gain.shape[1]]
    gates_all = layer_params[:, query_gain.shape[1] :]

    gathered = in_order(image_tokens, "section")
    gathered = gathered.transpose(1, 0, 2, 3).reshape(
        micro_count, -1, image_tokens.shape[2]
    )
    shard_count = lax.axis_size("shard")
    image_count = gathered.shape[1]
    total_rows = micro_count * image_count
    flat_rows = gathered.reshape(total_rows, gathered.shape[2])
    partial = jnp.dot(flat_rows, weights, preferred_element_type=jnp.float32)
    raw_rows = scatter_blocks(
        partial.reshape(shard_count, total_rows // shard_count, 2 * key_width), "shard", False
    )
    key_rows = head_normalize(raw_rows[:, :key_width], key_norm_gain[0], keyval_heads)
    keyval_rows = jnp.concatenate(
        [key_rows.astype(jnp.bfloat16), raw_rows[:, key_width:].astype(jnp.bfloat16)], axis=1
    )
    keyval_own = in_order(keyval_rows, "shard").reshape(total_rows, 2 * key_width)
    keyval_all, _ = gather_blocks(keyval_own, "section")

    same_document = text_document[:, :, None] == image_document[:, None, :]
    leaving, grad_local = attention_layers(
        section_index,
        layer_slots,
        jnp.tanh(gates_all),
        text_queries,
        keyval_all.reshape(section_count, micro_count, image_count, 2 * key_width),
        gains_all,
        same_document,
        cotangent[0],
    )
    grad_rows = scatter_blocks(
        grad_local.reshape(shard_count, total_rows // shard_count, 2 * key_width),
        "shard",
        False,
    )
    key_portion = norm_gradient(
        raw_rows[:, :key_width], key_norm_gain[0], grad_rows[:, :key_width], keyval_heads
    )
    raw_grad_rows = jnp.concatenate([key_portion, grad_rows[:, key_width:]], axis=1).astype(
        jnp.bfloat16
    )
    raw_grad = in_order(raw_grad_rows, "shard").reshape(total_rows, 2 * key_width)
    owned = image_count // section_count
    raw_grad = (
        raw_grad.reshape(micro_count, section_count, owned, 2 * key_width)
        .transpose(1, 0, 2, 3)
        .reshape(total_rows, 2 * key_width)
    )
    image_part = lax.dot_general(
        raw_grad, weights, (((1,), (1,)), ((), ())), preferred_element_type=jnp.float32
    )
    image_part = image_part.astype(jnp.bfloat16).reshape(
        section_count, micro_count, owned, weights.shape[0]
    )
    image_grad = scatter_blocks(image_part, "section", True)
    return (leaving[None], image_grad)


def solution(mesh):
    placed = (
        P("group", "section", "shard"),
        P("section", "shard", None),
        P("section", None),
        P("section", None),
        P("section", None),
        P("group", "shard", None),
        P("group", "shard"),
        P("group", None),
        P("section", "group", "shard", None),
    )
    return jax.shard_map(
        per_device,
        mesh=mesh,
        in_specs=placed,
        out_specs=(P("section", "group", "shard", None), P("group", "section", "shard")),
        check_vma=False,
    )
```

```python
import functools
import math

import jax
import jax.numpy as jnp
from jax import lax
from jax.experimental import pallas as pl
from jax.experimental.pallas import tpu as pltpu
from jax.sharding import PartitionSpec as P

epsilon = 1e-05


def head_normalize(input_rows, gain_row, head_count):
    shaped = input_rows.reshape(input_rows.shape[:-1] + (head_count, -1))
    factor = lax.rsqrt(jnp.mean(shaped * shaped, axis=-1, keepdims=True) + epsilon)
    gain = gain_row.reshape((1,) * (shaped.ndim - 2) + (head_count, -1))
    return (shaped * factor * gain).reshape(input_rows.shape)


def norm_gradient(input_rows, gain_row, incoming_gradient, head_count):
    shaped = input_rows.reshape(input_rows.shape[0], head_count, -1)
    scaled = incoming_gradient.reshape(input_rows.shape[0], head_count, -1) * gain_row.reshape(
        1, head_count, -1
    )
    factor = lax.rsqrt(jnp.mean(shaped * shaped, axis=-1, keepdims=True) + epsilon)
    inner_mean = jnp.mean(shaped * scaled, axis=-1, keepdims=True)
    result = factor * scaled - shaped * factor * factor * factor * inner_mean
    return result.reshape(input_rows.shape[0], -1)


def attention_kernel(
    section_ref,
    slots_ref,
    gates_ref,
    queries_ref,
    keyval_ref,
    gains_ref,
    mask_ref,
    mask_t_ref,
    cot_ref,
    out_ref,
    grad_ref,
    *,
    head_count,
    keyval_heads,
):
    token_count, query_width = out_ref.shape
    head_dim = query_width // head_count
    key_width = keyval_heads * head_dim
    groups = head_count // keyval_heads
    scale = 1.0 / math.sqrt(head_dim)
    section = section_ref[0]
    out_ref[...] = queries_ref[...].astype(jnp.float32)

    def head_cols(h):
        return pl.ds(h * head_dim, head_dim)

    def queries_of(slot, k):
        parts = []
        for g in range(groups):
            h = k * groups + g
            x = out_ref[:, head_cols(h)]
            mean_square = jnp.sum(x * x, axis=-1, keepdims=True) * (1.0 / head_dim)
            gain = gains_ref[slot, :, head_cols(h)]
            parts.append((x * lax.rsqrt(mean_square + epsilon) * gain).astype(jnp.bfloat16))
        return jnp.concatenate(parts, axis=0)

    def forward(layer):
        slot = slots_ref[layer]
        same = mask_ref[...] > 0.5
        for k in range(keyval_heads):
            query = queries_of(slot, k)
            key = keyval_ref[slot, :, head_cols(k)]
            value = keyval_ref[slot, :, pl.ds(key_width + k * head_dim, head_dim)]
            scores = lax.dot_general(
                query, key, (((1,), (1,)), ((), ())), preferred_element_type=jnp.float32
            ) * scale
            scores = jnp.where(same, scores, -jnp.inf)
            powered = jnp.exp(scores - jnp.max(scores, axis=-1, keepdims=True))
            probs = powered * (1.0 / jnp.sum(powered, axis=-1, keepdims=True))
            attended = jnp.dot(
                probs.astype(jnp.bfloat16), value, preferred_element_type=jnp.float32
            )
            for g in range(groups):
                h = k * groups + g
                rows = attended[g * token_count : (g + 1) * token_count]
                out_ref[:, head_cols(h)] = out_ref[:, head_cols(h)] + gates_ref[slot, h] * rows

    def layer_step(layer, carry):
        forward(layer)
        return carry

    lax.fori_loop(0, section, layer_step, 0)

    same_t = mask_t_ref[...] > 0.5
    own = slots_ref[section]
    for k in range(keyval_heads):
        query = queries_of(own, k)
        key = keyval_ref[own, :, head_cols(k)]
        value = keyval_ref[own, :, pl.ds(key_width + k * head_dim, head_dim)]
        scores_t = lax.dot_general(
            key, query, (((1,), (1,)), ((), ())), preferred_element_type=jnp.float32
        ) * scale
        scores_t = jnp.where(same_t, scores_t, -jnp.inf)
        powered = jnp.exp(scores_t - jnp.max(scores_t, axis=0, keepdims=True))
        probs_t = powered * (1.0 / jnp.sum(powered, axis=0, keepdims=True))
        upstream = jnp.concatenate(
            [cot_ref[:, head_cols(k * groups + g)] for g in range(groups)], axis=0
        )
        value_grad = jnp.dot(
            probs_t.astype(jnp.bfloat16), upstream, preferred_element_type=jnp.float32
        )
        prob_grad_t = lax.dot_general(
            value, upstream, (((1,), (1,)), ((), ())), preferred_element_type=jnp.float32
        )
        inner = jnp.sum(probs_t * prob_grad_t, axis=0, keepdims=True)
        score_grad_t = (probs_t * (prob_grad_t - inner)).astype(jnp.bfloat16)
        key_grad = jnp.dot(score_grad_t, query, preferred_element_type=jnp.float32) * scale
        grad_ref[:, head_cols(k)] = key_grad.astype(grad_ref.dtype)
        grad_ref[:, pl.ds(key_width + k * head_dim, head_dim)] = value_grad.astype(grad_ref.dtype)

    forward(section)


def attention_layers(
    section_index, layer_slots, gates, queries, keyval_all, gains, same_document, upstream
):
    layer_count, micro_count, image_count, pair_width = keyval_all.shape
    token_count, query_width = queries.shape[1], queries.shape[2]
    head_count = gates.shape[1]
    head_dim = query_width // head_count
    keyval_heads = pair_width // 2 // head_dim
    groups = head_count // keyval_heads
    mask = jnp.tile(same_document.astype(jnp.float32), (1, groups, 1))
    mask_t = jnp.swapaxes(mask, 1, 2)
    smem = pl.BlockSpec(memory_space=pltpu.SMEM)
    flops = 2 * micro_count * (layer_count + 3) * head_count * token_count * image_count * head_dim * 2
    return pl.pallas_call(
        functools.partial(attention_kernel, head_count=head_count, keyval_heads=keyval_heads),
        grid=(micro_count,),
        in_specs=[
            smem,
            smem,
            smem,
            pl.BlockSpec((None, token_count, query_width), lambda m: (m, 0, 0)),
            pl.BlockSpec((layer_count, None, image_count, pair_width), lambda m: (0, m, 0, 0)),
            pl.BlockSpec((layer_count, 1, query_width), lambda m: (0, 0, 0)),
            pl.BlockSpec((None, groups * token_count, image_count), lambda m: (m, 0, 0)),
            pl.BlockSpec((None, image_count, groups * token_count), lambda m: (m, 0, 0)),
            pl.BlockSpec((None, token_count, query_width), lambda m: (m, 0, 0)),
        ],
        out_specs=[
            pl.BlockSpec((None, token_count, query_width), lambda m: (m, 0, 0)),
            pl.BlockSpec((None, image_count, pair_width), lambda m: (m, 0, 0)),
        ],
        out_shape=[
            jax.ShapeDtypeStruct((micro_count, token_count, query_width), jnp.float32),
            jax.ShapeDtypeStruct((micro_count, image_count, pair_width), jnp.bfloat16),
        ],
        compiler_params=pltpu.CompilerParams(dimension_semantics=("arbitrary",)),
        cost_estimate=pl.CostEstimate(
            flops=flops,
            transcendentals=micro_count * (layer_count + 1) * head_count * token_count * image_count,
            bytes_accessed=keyval_all.size * 2 + queries.size * 8 + upstream.size * 2,
        ),
    )(
        jnp.reshape(section_index, (1,)).astype(jnp.int32),
        layer_slots.astype(jnp.int32),
        gates,
        queries,
        keyval_all,
        gains.reshape(layer_count, 1, query_width),
        mask,
        mask_t,
        upstream,
    )


def gather_blocks(block, axis):
    count = lax.axis_size(axis)
    index = lax.axis_index(axis)
    positions = jnp.arange(count, dtype=jnp.int32)
    if count > 8:
        return lax.all_gather(block, axis, axis=0, tiled=False), positions
    if count == 4:
        partner = [(i, i ^ 1) for i in range(count)]
        across = lax.ppermute(block, axis, [(i, i ^ 2) for i in range(count)])
        received = [block, lax.ppermute(block, axis, partner), across, lax.ppermute(across, axis, partner)]
        return jnp.stack(received), lax.bitwise_xor(index, positions)
    received = [block] + [
        lax.ppermute(block, axis, [(i, (i + d) % count) for i in range(count)])
        for d in range(1, count)
    ]
    return jnp.stack(received), (index - positions) % count


def in_order(block, axis):
    stacked, slots = gather_blocks(block, axis)
    return jnp.take(stacked, slots, axis=0)


def scatter_blocks(blocks, axis, pairs):
    count = lax.axis_size(axis)
    if count > 8:
        return lax.psum_scatter(blocks, axis, scatter_dimension=0, tiled=True)[0].astype(
            jnp.float32
        )
    index = lax.axis_index(axis)

    def pick(i):
        return lax.dynamic_index_in_dim(blocks, i, 0, keepdims=False)

    if pairs and count == 4:
        partner = [(i, i ^ 1) for i in range(count)]
        got = lax.ppermute(jnp.stack([pick(index ^ 1), pick(index ^ 3)]), axis, partner)
        theirs = (pick(index ^ 2).astype(jnp.float32) + got[1].astype(jnp.float32)).astype(
            blocks.dtype
        )
        back = lax.ppermute(theirs, axis, [(i, i ^ 2) for i in range(count)])
        return (
            pick(index).astype(jnp.float32)
            + got[0].astype(jnp.float32)
            + back.astype(jnp.float32)
        )
    total = pick(index).astype(jnp.float32)
    for d in range(1, count):
        part = lax.dynamic_index_in_dim(blocks, (index + d) % count, 0, keepdims=False)
        total = total + lax.ppermute(
            part, axis, [(i, (i + d) % count) for i in range(count)]
        ).astype(jnp.float32)
    return total


def per_device(
    image_tokens,
    keyval_weight,
    query_gain,
    key_norm_gain,
    gate_logit,
    text_queries,
    text_document,
    image_document,
    cotangent,
):
    section_count = lax.axis_size("section")
    section_index = lax.axis_index("section")
    micro_count = text_queries.shape[0]
    head_count = gate_logit.shape[1]
    key_width = key_norm_gain.shape[1]
    head_dim = query_gain.shape[1] // head_count
    keyval_heads = key_width // head_dim
    weights = keyval_weight[0]

    layer_params, layer_slots = gather_blocks(
        jnp.concatenate([query_gain, gate_logit], axis=1)[0], "section"
    )
    gains_all = layer_params[:, : query_gain.shape[1]]
    gates_all = layer_params[:, query_gain.shape[1] :]

    shard_count = lax.axis_size("shard")
    same_document = text_document[:, :, None] == image_document[:, None, :]
    gate_factors = jnp.tanh(gates_all)

    def micro_chain(m):
        gathered = in_order(image_tokens[m], "section")
        image_count = gathered.shape[0] * gathered.shape[1]
        block_rows = image_count // shard_count
        flat_rows = gathered.reshape(image_count, gathered.shape[2])
        partial = jnp.dot(flat_rows, weights, preferred_element_type=jnp.float32)
        raw_rows = scatter_blocks(
            partial.reshape(shard_count, block_rows, 2 * key_width), "shard", False
        )
        key_rows = head_normalize(raw_rows[:, :key_width], key_norm_gain[0], keyval_heads)
        keyval_rows = jnp.concatenate(
            [key_rows.astype(jnp.bfloat16), raw_rows[:, key_width:].astype(jnp.bfloat16)],
            axis=1,
        )
        keyval_own = in_order(keyval_rows, "shard").reshape(image_count, 2 * key_width)
        keyval_all, _ = gather_blocks(keyval_own, "section")
        leaving, grad_local = attention_layers(
            section_index,
            layer_slots,
            gate_factors,
            text_queries[m : m + 1],
            keyval_all[:, None],
            gains_all,
            same_document[m : m + 1],
            cotangent[0, m : m + 1],
        )
        grad_rows = scatter_blocks(
            grad_local.reshape(shard_count, block_rows, 2 * key_width), "shard", False
        )
        key_portion = norm_gradient(
            raw_rows[:, :key_width], key_norm_gain[0], grad_rows[:, :key_width], keyval_heads
        )
        raw_grad_rows = jnp.concatenate(
            [key_portion, grad_rows[:, key_width:]], axis=1
        ).astype(jnp.bfloat16)
        raw_grad = in_order(raw_grad_rows, "shard").reshape(image_count, 2 * key_width)
        image_part = lax.dot_general(
            raw_grad, weights, (((1,), (1,)), ((), ())), preferred_element_type=jnp.float32
        )
        image_part = image_part.astype(jnp.bfloat16).reshape(
            section_count, image_count // section_count, weights.shape[0]
        )
        return leaving[0], scatter_blocks(image_part, "section", True)

    chains = [micro_chain(m) for m in range(micro_count)]
    leaving = jnp.stack([c[0] for c in chains])
    image_grad = jnp.stack([c[1] for c in chains])
    return (leaving[None], image_grad)


def solution(mesh):
    placed = (
        P("group", "section", "shard"),
        P("section", "shard", None),
        P("section", None),
        P("section", None),
        P("section", None),
        P("group", "shard", None),
        P("group", "shard"),
        P("group", None),
        P("section", "group", "shard", None),
    )
    return jax.shard_map(
        per_device,
        mesh=mesh,
        in_specs=placed,
        out_specs=(P("section", "group", "shard", None), P("group", "section", "shard")),
        check_vma=False,
    )
```

```python
import functools
import math

import jax
import jax.numpy as jnp
from jax import lax
from jax.experimental import pallas as pl
from jax.experimental.pallas import tpu as pltpu
from jax.sharding import PartitionSpec as P

epsilon = 1e-05


def head_normalize(input_rows, gain_row, head_count):
    shaped = input_rows.reshape(input_rows.shape[:-1] + (head_count, -1))
    factor = lax.rsqrt(jnp.mean(shaped * shaped, axis=-1, keepdims=True) + epsilon)
    gain = gain_row.reshape((1,) * (shaped.ndim - 2) + (head_count, -1))
    return (shaped * factor * gain).reshape(input_rows.shape)


def norm_gradient(input_rows, gain_row, incoming_gradient, head_count):
    shaped = input_rows.reshape(input_rows.shape[0], head_count, -1)
    scaled = incoming_gradient.reshape(input_rows.shape[0], head_count, -1) * gain_row.reshape(
        1, head_count, -1
    )
    factor = lax.rsqrt(jnp.mean(shaped * shaped, axis=-1, keepdims=True) + epsilon)
    inner_mean = jnp.mean(shaped * scaled, axis=-1, keepdims=True)
    result = factor * scaled - shaped * factor * factor * factor * inner_mean
    return result.reshape(input_rows.shape[0], -1)


def attention_kernel(
    section_ref,
    slots_ref,
    gates_ref,
    queries_ref,
    keyval_ref,
    gains_ref,
    mask_ref,
    mask_t_ref,
    cot_ref,
    out_ref,
    grad_ref,
    *,
    head_count,
    keyval_heads,
):
    token_count, query_width = out_ref.shape
    head_dim = query_width // head_count
    key_width = keyval_heads * head_dim
    groups = head_count // keyval_heads
    scale = 1.0 / math.sqrt(head_dim)
    section = section_ref[0]
    out_ref[...] = queries_ref[...].astype(jnp.float32)

    def head_cols(h):
        return pl.ds(h * head_dim, head_dim)

    def queries_of(slot, k):
        parts = []
        for g in range(groups):
            h = k * groups + g
            x = out_ref[:, head_cols(h)]
            mean_square = jnp.sum(x * x, axis=-1, keepdims=True) * (1.0 / head_dim)
            gain = gains_ref[slot, :, head_cols(h)]
            parts.append((x * lax.rsqrt(mean_square + epsilon) * gain).astype(jnp.bfloat16))
        return jnp.concatenate(parts, axis=0)

    def forward(layer):
        slot = slots_ref[layer]
        same = mask_ref[...] > 0.5
        for k in range(keyval_heads):
            query = queries_of(slot, k)
            key = keyval_ref[slot, :, head_cols(k)]
            value = keyval_ref[slot, :, pl.ds(key_width + k * head_dim, head_dim)]
            scores = lax.dot_general(
                query, key, (((1,), (1,)), ((), ())), preferred_element_type=jnp.float32
            ) * scale
            scores = jnp.where(same, scores, -jnp.inf)
            powered = jnp.exp(scores - jnp.max(scores, axis=-1, keepdims=True))
            probs = powered * (1.0 / jnp.sum(powered, axis=-1, keepdims=True))
            attended = jnp.dot(
                probs.astype(jnp.bfloat16), value, preferred_element_type=jnp.float32
            )
            for g in range(groups):
                h = k * groups + g
                rows = attended[g * token_count : (g + 1) * token_count]
                out_ref[:, head_cols(h)] = out_ref[:, head_cols(h)] + gates_ref[slot, h] * rows

    def layer_step(layer, carry):
        forward(layer)
        return carry

    lax.fori_loop(0, section, layer_step, 0)

    same_t = mask_t_ref[...] > 0.5
    own = slots_ref[section]
    for k in range(keyval_heads):
        query = queries_of(own, k)
        key = keyval_ref[own, :, head_cols(k)]
        value = keyval_ref[own, :, pl.ds(key_width + k * head_dim, head_dim)]
        scores_t = lax.dot_general(
            key, query, (((1,), (1,)), ((), ())), preferred_element_type=jnp.float32
        ) * scale
        scores_t = jnp.where(same_t, scores_t, -jnp.inf)
        powered = jnp.exp(scores_t - jnp.max(scores_t, axis=0, keepdims=True))
        probs_t = powered * (1.0 / jnp.sum(powered, axis=0, keepdims=True))
        upstream = jnp.concatenate(
            [cot_ref[:, head_cols(k * groups + g)] for g in range(groups)], axis=0
        )
        value_grad = jnp.dot(
            probs_t.astype(jnp.bfloat16), upstream, preferred_element_type=jnp.float32
        )
        prob_grad_t = lax.dot_general(
            value, upstream, (((1,), (1,)), ((), ())), preferred_element_type=jnp.float32
        )
        inner = jnp.sum(probs_t * prob_grad_t, axis=0, keepdims=True)
        score_grad_t = (probs_t * (prob_grad_t - inner)).astype(jnp.bfloat16)
        key_grad = jnp.dot(score_grad_t, query, preferred_element_type=jnp.float32) * scale
        grad_ref[:, head_cols(k)] = key_grad.astype(grad_ref.dtype)
        grad_ref[:, pl.ds(key_width + k * head_dim, head_dim)] = value_grad.astype(grad_ref.dtype)

    forward(section)


def attention_layers(
    section_index, layer_slots, gates, queries, keyval_all, gains, same_document, upstream
):
    layer_count, micro_count, image_count, pair_width = keyval_all.shape
    token_count, query_width = queries.shape[1], queries.shape[2]
    head_count = gates.shape[1]
    head_dim = query_width // head_count
    keyval_heads = pair_width // 2 // head_dim
    groups = head_count // keyval_heads
    mask = jnp.tile(same_document.astype(jnp.float32), (1, groups, 1))
    mask_t = jnp.swapaxes(mask, 1, 2)
    smem = pl.BlockSpec(memory_space=pltpu.SMEM)
    flops = 2 * micro_count * (layer_count + 3) * head_count * token_count * image_count * head_dim * 2
    return pl.pallas_call(
        functools.partial(attention_kernel, head_count=head_count, keyval_heads=keyval_heads),
        grid=(micro_count,),
        in_specs=[
            smem,
            smem,
            smem,
            pl.BlockSpec((None, token_count, query_width), lambda m: (m, 0, 0)),
            pl.BlockSpec((layer_count, None, image_count, pair_width), lambda m: (0, m, 0, 0)),
            pl.BlockSpec((layer_count, 1, query_width), lambda m: (0, 0, 0)),
            pl.BlockSpec((None, groups * token_count, image_count), lambda m: (m, 0, 0)),
            pl.BlockSpec((None, image_count, groups * token_count), lambda m: (m, 0, 0)),
            pl.BlockSpec((None, token_count, query_width), lambda m: (m, 0, 0)),
        ],
        out_specs=[
            pl.BlockSpec((None, token_count, query_width), lambda m: (m, 0, 0)),
            pl.BlockSpec((None, image_count, pair_width), lambda m: (m, 0, 0)),
        ],
        out_shape=[
            jax.ShapeDtypeStruct((micro_count, token_count, query_width), jnp.float32),
            jax.ShapeDtypeStruct((micro_count, image_count, pair_width), jnp.bfloat16),
        ],
        compiler_params=pltpu.CompilerParams(dimension_semantics=("arbitrary",)),
        cost_estimate=pl.CostEstimate(
            flops=flops,
            transcendentals=micro_count * (layer_count + 1) * head_count * token_count * image_count,
            bytes_accessed=keyval_all.size * 2 + queries.size * 8 + upstream.size * 2,
        ),
    )(
        jnp.reshape(section_index, (1,)).astype(jnp.int32),
        layer_slots.astype(jnp.int32),
        gates,
        queries,
        keyval_all,
        gains.reshape(layer_count, 1, query_width),
        mask,
        mask_t,
        upstream,
    )


def gather_blocks(block, axis):
    count = lax.axis_size(axis)
    index = lax.axis_index(axis)
    positions = jnp.arange(count, dtype=jnp.int32)
    if count > 8:
        return lax.all_gather(block, axis, axis=0, tiled=False), positions
    if count == 4:
        partner = [(i, i ^ 1) for i in range(count)]
        across = lax.ppermute(block, axis, [(i, i ^ 2) for i in range(count)])
        received = [block, lax.ppermute(block, axis, partner), across, lax.ppermute(across, axis, partner)]
        return jnp.stack(received), lax.bitwise_xor(index, positions)
    received = [block] + [
        lax.ppermute(block, axis, [(i, (i + d) % count) for i in range(count)])
        for d in range(1, count)
    ]
    return jnp.stack(received), (index - positions) % count


def in_order(block, axis):
    stacked, slots = gather_blocks(block, axis)
    return jnp.take(stacked, slots, axis=0)


def scatter_blocks(blocks, axis, pairs):
    count = lax.axis_size(axis)
    if count > 8:
        return lax.psum_scatter(blocks, axis, scatter_dimension=0, tiled=True)[0].astype(
            jnp.float32
        )
    index = lax.axis_index(axis)

    def pick(i):
        return lax.dynamic_index_in_dim(blocks, i, 0, keepdims=False)

    if pairs and count == 4:
        partner = [(i, i ^ 1) for i in range(count)]
        got = lax.ppermute(jnp.stack([pick(index ^ 1), pick(index ^ 3)]), axis, partner)
        theirs = (pick(index ^ 2).astype(jnp.float32) + got[1].astype(jnp.float32)).astype(
            blocks.dtype
        )
        back = lax.ppermute(theirs, axis, [(i, i ^ 2) for i in range(count)])
        return (
            pick(index).astype(jnp.float32)
            + got[0].astype(jnp.float32)
            + back.astype(jnp.float32)
        )
    total = pick(index).astype(jnp.float32)
    for d in range(1, count):
        part = lax.dynamic_index_in_dim(blocks, (index + d) % count, 0, keepdims=False)
        total = total + lax.ppermute(
            part, axis, [(i, (i + d) % count) for i in range(count)]
        ).astype(jnp.float32)
    return total


def per_device(
    image_tokens,
    keyval_weight,
    query_gain,
    key_norm_gain,
    gate_logit,
    text_queries,
    text_document,
    image_document,
    cotangent,
):
    section_count = lax.axis_size("section")
    section_index = lax.axis_index("section")
    micro_count = text_queries.shape[0]
    head_count = gate_logit.shape[1]
    key_width = key_norm_gain.shape[1]
    head_dim = query_gain.shape[1] // head_count
    keyval_heads = key_width // head_dim
    weights = keyval_weight[0]

    gathered = in_order(image_tokens, "section")
    gathered = gathered.transpose(1, 0, 2, 3).reshape(
        micro_count, -1, image_tokens.shape[2]
    )
    shard_count = lax.axis_size("shard")
    image_count = gathered.shape[1]
    total_rows = micro_count * image_count
    flat_rows = gathered.reshape(total_rows, gathered.shape[2])
    partial = jnp.dot(flat_rows, weights, preferred_element_type=jnp.float32)
    raw_rows = scatter_blocks(
        partial.reshape(shard_count, total_rows // shard_count, 2 * key_width), "shard", False
    )
    key_rows = head_normalize(raw_rows[:, :key_width], key_norm_gain[0], keyval_heads)
    keyval_rows = jnp.concatenate(
        [key_rows.astype(jnp.bfloat16), raw_rows[:, key_width:].astype(jnp.bfloat16)], axis=1
    )
    keyval_own = in_order(keyval_rows, "shard").reshape(total_rows, 2 * key_width)
    params = jnp.concatenate([query_gain, gate_logit], axis=1)[0]
    high = params.astype(jnp.bfloat16)
    rest = params - high.astype(jnp.float32)
    middle = rest.astype(jnp.bfloat16)
    low = (rest - middle.astype(jnp.float32)).astype(jnp.bfloat16)
    coded = jnp.concatenate([high, middle, low])
    param_rows = -(-coded.shape[0] // (2 * key_width))
    coded = jnp.pad(coded, (0, param_rows * 2 * key_width - coded.shape[0]))
    payload = jnp.concatenate([keyval_own, coded.reshape(param_rows, 2 * key_width)], axis=0)
    payload_all, layer_slots = gather_blocks(payload, "section")
    keyval_all = payload_all[:, :total_rows]
    coded_all = payload_all[:, total_rows:].reshape(section_count, -1)[:, : 3 * params.shape[0]]
    coded_all = coded_all.astype(jnp.float32).reshape(section_count, 3, params.shape[0])
    layer_params = (coded_all[:, 0] + coded_all[:, 1]) + coded_all[:, 2]
    gains_all = layer_params[:, : query_gain.shape[1]]
    gates_all = layer_params[:, query_gain.shape[1] :]

    same_document = text_document[:, :, None] == image_document[:, None, :]
    leaving, grad_local = attention_layers(
        section_index,
        layer_slots,
        jnp.tanh(gates_all),
        text_queries,
        keyval_all.reshape(section_count, micro_count, image_count, 2 * key_width),
        gains_all,
        same_document,
        cotangent[0],
    )
    grad_rows = scatter_blocks(
        grad_local.reshape(shard_count, total_rows // shard_count, 2 * key_width),
        "shard",
        False,
    )
    key_portion = norm_gradient(
        raw_rows[:, :key_width], key_norm_gain[0], grad_rows[:, :key_width], keyval_heads
    )
    raw_grad_rows = jnp.concatenate([key_portion, grad_rows[:, key_width:]], axis=1).astype(
        jnp.bfloat16
    )
    raw_grad = in_order(raw_grad_rows, "shard").reshape(total_rows, 2 * key_width)
    owned = image_count // section_count
    raw_grad = (
        raw_grad.reshape(micro_count, section_count, owned, 2 * key_width)
        .transpose(1, 0, 2, 3)
        .reshape(total_rows, 2 * key_width)
    )
    image_part = lax.dot_general(
        raw_grad, weights, (((1,), (1,)), ((), ())), preferred_element_type=jnp.float32
    )
    image_part = image_part.astype(jnp.bfloat16).reshape(
        section_count, micro_count, owned, weights.shape[0]
    )
    image_grad = scatter_blocks(image_part, "section", True)
    return (leaving[None], image_grad)


def solution(mesh):
    placed = (
        P("group", "section", "shard"),
        P("section", "shard", None),
        P("section", None),
        P("section", None),
        P("section", None),
        P("group", "shard", None),
        P("group", "shard"),
        P("group", None),
        P("section", "group", "shard", None),
    )
    return jax.shard_map(
        per_device,
        mesh=mesh,
        in_specs=placed,
        out_specs=(P("section", "group", "shard", None), P("group", "section", "shard")),
        check_vma=False,
    )
```

```python
import functools
import math

import jax
import jax.numpy as jnp
from jax import lax
from jax.experimental import pallas as pl
from jax.experimental.pallas import tpu as pltpu
from jax.sharding import PartitionSpec as P

epsilon = 1e-05


def head_normalize(input_rows, gain_row, head_count):
    shaped = input_rows.reshape(input_rows.shape[:-1] + (head_count, -1))
    factor = lax.rsqrt(jnp.mean(shaped * shaped, axis=-1, keepdims=True) + epsilon)
    gain = gain_row.reshape((1,) * (shaped.ndim - 2) + (head_count, -1))
    return (shaped * factor * gain).reshape(input_rows.shape)


def norm_gradient(input_rows, gain_row, incoming_gradient, head_count):
    shaped = input_rows.reshape(input_rows.shape[0], head_count, -1)
    scaled = incoming_gradient.reshape(input_rows.shape[0], head_count, -1) * gain_row.reshape(
        1, head_count, -1
    )
    factor = lax.rsqrt(jnp.mean(shaped * shaped, axis=-1, keepdims=True) + epsilon)
    inner_mean = jnp.mean(shaped * scaled, axis=-1, keepdims=True)
    result = factor * scaled - shaped * factor * factor * factor * inner_mean
    return result.reshape(input_rows.shape[0], -1)


def attention_kernel(
    section_ref,
    slots_ref,
    gates_ref,
    queries_ref,
    keyval_ref,
    gains_ref,
    mask_ref,
    mask_t_ref,
    cot_ref,
    out_ref,
    grad_ref,
    *,
    head_count,
    keyval_heads,
):
    token_count, query_width = out_ref.shape
    head_dim = query_width // head_count
    key_width = keyval_heads * head_dim
    groups = head_count // keyval_heads
    scale = 1.0 / math.sqrt(head_dim)
    section = section_ref[0]
    out_ref[...] = queries_ref[...].astype(jnp.float32)

    def head_cols(h):
        return pl.ds(h * head_dim, head_dim)

    def queries_of(slot, k):
        parts = []
        for g in range(groups):
            h = k * groups + g
            x = out_ref[:, head_cols(h)]
            mean_square = jnp.sum(x * x, axis=-1, keepdims=True) * (1.0 / head_dim)
            gain = gains_ref[slot, :, head_cols(h)]
            parts.append((x * lax.rsqrt(mean_square + epsilon) * gain).astype(jnp.bfloat16))
        return jnp.concatenate(parts, axis=0)

    def forward(layer):
        slot = slots_ref[layer]
        same = mask_ref[...] > 0.5
        for k in range(keyval_heads):
            query = queries_of(slot, k)
            key = keyval_ref[slot, :, head_cols(k)]
            value = keyval_ref[slot, :, pl.ds(key_width + k * head_dim, head_dim)]
            scores = lax.dot_general(
                query, key, (((1,), (1,)), ((), ())), preferred_element_type=jnp.float32
            ) * scale
            scores = jnp.where(same, scores, -jnp.inf)
            powered = jnp.exp(scores - jnp.max(scores, axis=-1, keepdims=True))
            probs = powered * (1.0 / jnp.sum(powered, axis=-1, keepdims=True))
            attended = jnp.dot(
                probs.astype(jnp.bfloat16), value, preferred_element_type=jnp.float32
            )
            for g in range(groups):
                h = k * groups + g
                rows = attended[g * token_count : (g + 1) * token_count]
                out_ref[:, head_cols(h)] = out_ref[:, head_cols(h)] + gates_ref[slot, h] * rows

    def layer_step(layer, carry):
        forward(layer)
        return carry

    lax.fori_loop(0, section, layer_step, 0)

    same_t = mask_t_ref[...] > 0.5
    own = slots_ref[section]
    for k in range(keyval_heads):
        query = queries_of(own, k)
        key = keyval_ref[own, :, head_cols(k)]
        value = keyval_ref[own, :, pl.ds(key_width + k * head_dim, head_dim)]
        scores_t = lax.dot_general(
            key, query, (((1,), (1,)), ((), ())), preferred_element_type=jnp.float32
        ) * scale
        scores_t = jnp.where(same_t, scores_t, -jnp.inf)
        powered = jnp.exp(scores_t - jnp.max(scores_t, axis=0, keepdims=True))
        probs_t = powered * (1.0 / jnp.sum(powered, axis=0, keepdims=True))
        upstream = jnp.concatenate(
            [cot_ref[:, head_cols(k * groups + g)] for g in range(groups)], axis=0
        )
        value_grad = jnp.dot(
            probs_t.astype(jnp.bfloat16), upstream, preferred_element_type=jnp.float32
        )
        prob_grad_t = lax.dot_general(
            value, upstream, (((1,), (1,)), ((), ())), preferred_element_type=jnp.float32
        )
        inner = jnp.sum(probs_t * prob_grad_t, axis=0, keepdims=True)
        score_grad_t = (probs_t * (prob_grad_t - inner)).astype(jnp.bfloat16)
        key_grad = jnp.dot(score_grad_t, query, preferred_element_type=jnp.float32) * scale
        grad_ref[:, head_cols(k)] = key_grad.astype(grad_ref.dtype)
        grad_ref[:, pl.ds(key_width + k * head_dim, head_dim)] = value_grad.astype(grad_ref.dtype)

    forward(section)


def attention_layers(
    section_index, layer_slots, gates, queries, keyval_all, gains, same_document, upstream
):
    layer_count, micro_count, image_count, pair_width = keyval_all.shape
    token_count, query_width = queries.shape[1], queries.shape[2]
    head_count = gates.shape[1]
    head_dim = query_width // head_count
    keyval_heads = pair_width // 2 // head_dim
    groups = head_count // keyval_heads
    mask = jnp.tile(same_document.astype(jnp.float32), (1, groups, 1))
    mask_t = jnp.swapaxes(mask, 1, 2)
    smem = pl.BlockSpec(memory_space=pltpu.SMEM)
    flops = 2 * micro_count * (layer_count + 3) * head_count * token_count * image_count * head_dim * 2
    return pl.pallas_call(
        functools.partial(attention_kernel, head_count=head_count, keyval_heads=keyval_heads),
        grid=(micro_count,),
        in_specs=[
            smem,
            smem,
            smem,
            pl.BlockSpec((None, token_count, query_width), lambda m: (m, 0, 0)),
            pl.BlockSpec((layer_count, None, image_count, pair_width), lambda m: (0, m, 0, 0)),
            pl.BlockSpec((layer_count, 1, query_width), lambda m: (0, 0, 0)),
            pl.BlockSpec((None, groups * token_count, image_count), lambda m: (m, 0, 0)),
            pl.BlockSpec((None, image_count, groups * token_count), lambda m: (m, 0, 0)),
            pl.BlockSpec((None, token_count, query_width), lambda m: (m, 0, 0)),
        ],
        out_specs=[
            pl.BlockSpec((None, token_count, query_width), lambda m: (m, 0, 0)),
            pl.BlockSpec((None, image_count, pair_width), lambda m: (m, 0, 0)),
        ],
        out_shape=[
            jax.ShapeDtypeStruct((micro_count, token_count, query_width), jnp.float32),
            jax.ShapeDtypeStruct((micro_count, image_count, pair_width), jnp.bfloat16),
        ],
        compiler_params=pltpu.CompilerParams(dimension_semantics=("arbitrary",)),
        cost_estimate=pl.CostEstimate(
            flops=flops,
            transcendentals=micro_count * (layer_count + 1) * head_count * token_count * image_count,
            bytes_accessed=keyval_all.size * 2 + queries.size * 8 + upstream.size * 2,
        ),
    )(
        jnp.reshape(section_index, (1,)).astype(jnp.int32),
        layer_slots.astype(jnp.int32),
        gates,
        queries,
        keyval_all,
        gains.reshape(layer_count, 1, query_width),
        mask,
        mask_t,
        upstream,
    )


def gather_blocks(block, axis):
    count = lax.axis_size(axis)
    index = lax.axis_index(axis)
    positions = jnp.arange(count, dtype=jnp.int32)
    if count > 8:
        return lax.all_gather(block, axis, axis=0, tiled=False), positions
    if count == 4:
        partner = [(i, i ^ 1) for i in range(count)]
        across = lax.ppermute(block, axis, [(i, i ^ 2) for i in range(count)])
        received = [block, lax.ppermute(block, axis, partner), across, lax.ppermute(across, axis, partner)]
        return jnp.stack(received), lax.bitwise_xor(index, positions)
    received = [block] + [
        lax.ppermute(block, axis, [(i, (i + d) % count) for i in range(count)])
        for d in range(1, count)
    ]
    return jnp.stack(received), (index - positions) % count


def in_order(block, axis):
    stacked, slots = gather_blocks(block, axis)
    return jnp.take(stacked, slots, axis=0)


def scatter_blocks(blocks, axis, pairs):
    count = lax.axis_size(axis)
    if count > 8:
        return lax.psum_scatter(blocks, axis, scatter_dimension=0, tiled=True)[0].astype(
            jnp.float32
        )
    index = lax.axis_index(axis)

    def pick(i):
        return lax.dynamic_index_in_dim(blocks, i, 0, keepdims=False)

    if pairs and count == 4:
        partner = [(i, i ^ 1) for i in range(count)]
        got = lax.ppermute(jnp.stack([pick(index ^ 1), pick(index ^ 3)]), axis, partner)
        theirs = (pick(index ^ 2).astype(jnp.float32) + got[1].astype(jnp.float32)).astype(
            blocks.dtype
        )
        back = lax.ppermute(theirs, axis, [(i, i ^ 2) for i in range(count)])
        return (
            pick(index).astype(jnp.float32)
            + got[0].astype(jnp.float32)
            + back.astype(jnp.float32)
        )
    total = pick(index).astype(jnp.float32)
    for d in range(1, count):
        part = lax.dynamic_index_in_dim(blocks, (index + d) % count, 0, keepdims=False)
        total = total + lax.ppermute(
            part, axis, [(i, (i + d) % count) for i in range(count)]
        ).astype(jnp.float32)
    return total


def per_device(
    image_tokens,
    keyval_weight,
    query_gain,
    key_norm_gain,
    gate_logit,
    text_queries,
    text_document,
    image_document,
    cotangent,
):
    section_count = lax.axis_size("section")
    section_index = lax.axis_index("section")
    micro_count = text_queries.shape[0]
    head_count = gate_logit.shape[1]
    key_width = key_norm_gain.shape[1]
    head_dim = query_gain.shape[1] // head_count
    keyval_heads = key_width // head_dim
    weights = keyval_weight[0]

    layer_params, layer_slots = gather_blocks(
        jnp.concatenate([query_gain, gate_logit], axis=1)[0], "section"
    )
    gains_all = layer_params[:, : query_gain.shape[1]]
    gates_all = layer_params[:, query_gain.shape[1] :]

    shard_count = lax.axis_size("shard")
    owned = image_tokens.shape[1]
    image_count = owned * section_count
    total_rows = micro_count * image_count
    pair_width = 2 * key_width
    phased = section_count == 4 and shard_count == 2 * micro_count
    if phased:
        images, _ = gather_blocks(image_tokens, "section")
        raw_parts = []
        for phase in range(2):
            block = images[2 * phase : 2 * phase + 2].transpose(1, 0, 2, 3)
            block = block.reshape(-1, image_tokens.shape[2])
            partial = jnp.dot(block, weights, preferred_element_type=jnp.float32)
            raw_parts.append(
                scatter_blocks(partial.reshape(shard_count, owned, pair_width), "shard", False)
            )
        raw_rows = jnp.stack(raw_parts)
        sections = jnp.arange(section_count, dtype=jnp.int32)
        distance = lax.bitwise_xor(section_index, sections)
        micro_ids = jnp.arange(micro_count, dtype=jnp.int32)
        natural = (2 * micro_ids[:, None] + distance[None, :] % 2) * 2 + distance[None, :] // 2
        owners = jnp.arange(shard_count, dtype=jnp.int32)[:, None]
        phases = jnp.arange(2, dtype=jnp.int32)[None, :]
        held = (owners // 2) * section_count + lax.bitwise_xor(
            section_index, 2 * phases + owners % 2
        )

        def to_natural(rows):
            blocks = in_order(rows.reshape(2, owned, pair_width), "shard")
            return jnp.take(
                blocks.reshape(2 * shard_count, owned, pair_width), natural.reshape(-1), axis=0
            ).reshape(total_rows, pair_width)

        def to_owned(rows):
            return jnp.take(
                rows.reshape(micro_count * section_count, owned, pair_width),
                held.reshape(-1),
                axis=0,
            ).reshape(shard_count, 2 * owned, pair_width)

    else:
        gathered = in_order(image_tokens, "section")
        gathered = gathered.transpose(1, 0, 2, 3).reshape(total_rows, image_tokens.shape[2])
        partial = jnp.dot(gathered, weights, preferred_element_type=jnp.float32)
        raw_rows = scatter_blocks(
            partial.reshape(shard_count, total_rows // shard_count, pair_width), "shard", False
        )

        def to_natural(rows):
            return in_order(rows, "shard").reshape(total_rows, pair_width)

        def to_owned(rows):
            return rows.reshape(shard_count, total_rows // shard_count, pair_width)

    raw_rows = raw_rows.reshape(-1, pair_width)
    key_rows = head_normalize(raw_rows[:, :key_width], key_norm_gain[0], keyval_heads)
    keyval_rows = jnp.concatenate(
        [key_rows.astype(jnp.bfloat16), raw_rows[:, key_width:].astype(jnp.bfloat16)], axis=1
    )
    keyval_own = to_natural(keyval_rows)
    keyval_all, _ = gather_blocks(keyval_own, "section")

    same_document = text_document[:, :, None] == image_document[:, None, :]
    leaving, grad_local = attention_layers(
        section_index,
        layer_slots,
        jnp.tanh(gates_all),
        text_queries,
        keyval_all.reshape(section_count, micro_count, image_count, 2 * key_width),
        gains_all,
        same_document,
        cotangent[0],
    )
    grad_rows = scatter_blocks(to_owned(grad_local), "shard", False).reshape(-1, pair_width)
    key_portion = norm_gradient(
        raw_rows[:, :key_width], key_norm_gain[0], grad_rows[:, :key_width], keyval_heads
    )
    raw_grad_rows = jnp.concatenate([key_portion, grad_rows[:, key_width:]], axis=1).astype(
        jnp.bfloat16
    )
    raw_grad = to_natural(raw_grad_rows)
    owned = image_count // section_count
    raw_grad = (
        raw_grad.reshape(micro_count, section_count, owned, 2 * key_width)
        .transpose(1, 0, 2, 3)
        .reshape(total_rows, 2 * key_width)
    )
    image_part = lax.dot_general(
        raw_grad, weights, (((1,), (1,)), ((), ())), preferred_element_type=jnp.float32
    )
    image_part = image_part.astype(jnp.bfloat16).reshape(
        section_count, micro_count, owned, weights.shape[0]
    )
    image_grad = scatter_blocks(image_part, "section", True)
    return (leaving[None], image_grad)


def solution(mesh):
    placed = (
        P("group", "section", "shard"),
        P("section", "shard", None),
        P("section", None),
        P("section", None),
        P("section", None),
        P("group", "shard", None),
        P("group", "shard"),
        P("group", None),
        P("section", "group", "shard", None),
    )
    return jax.shard_map(
        per_device,
        mesh=mesh,
        in_specs=placed,
        out_specs=(P("section", "group", "shard", None), P("group", "section", "shard")),
        check_vma=False,
    )
```

```python
import functools
import math

import jax
import jax.numpy as jnp
from jax import lax
from jax.experimental import pallas as pl
from jax.experimental.pallas import tpu as pltpu
from jax.sharding import PartitionSpec as P

epsilon = 1e-05


def head_normalize(input_rows, gain_row, head_count):
    shaped = input_rows.reshape(input_rows.shape[:-1] + (head_count, -1))
    factor = lax.rsqrt(jnp.mean(shaped * shaped, axis=-1, keepdims=True) + epsilon)
    gain = gain_row.reshape((1,) * (shaped.ndim - 2) + (head_count, -1))
    return (shaped * factor * gain).reshape(input_rows.shape)


def norm_gradient(input_rows, gain_row, incoming_gradient, head_count):
    shaped = input_rows.reshape(input_rows.shape[0], head_count, -1)
    scaled = incoming_gradient.reshape(input_rows.shape[0], head_count, -1) * gain_row.reshape(
        1, head_count, -1
    )
    factor = lax.rsqrt(jnp.mean(shaped * shaped, axis=-1, keepdims=True) + epsilon)
    inner_mean = jnp.mean(shaped * scaled, axis=-1, keepdims=True)
    result = factor * scaled - shaped * factor * factor * factor * inner_mean
    return result.reshape(input_rows.shape[0], -1)


def attention_kernel(
    section_ref,
    slots_ref,
    gates_ref,
    queries_ref,
    keyval_ref,
    gains_ref,
    mask_ref,
    mask_t_ref,
    cot_ref,
    out_ref,
    grad_ref,
    *,
    head_count,
    keyval_heads,
):
    token_count, query_width = out_ref.shape
    head_dim = query_width // head_count
    key_width = keyval_heads * head_dim
    groups = head_count // keyval_heads
    scale = 1.0 / math.sqrt(head_dim)
    section = section_ref[0]
    out_ref[...] = queries_ref[...].astype(jnp.float32)

    def head_cols(h):
        return pl.ds(h * head_dim, head_dim)

    def queries_of(slot, k):
        parts = []
        for g in range(groups):
            h = k * groups + g
            x = out_ref[:, head_cols(h)]
            mean_square = jnp.sum(x * x, axis=-1, keepdims=True) * (1.0 / head_dim)
            gain = gains_ref[slot, :, head_cols(h)]
            parts.append((x * lax.rsqrt(mean_square + epsilon) * gain).astype(jnp.bfloat16))
        return jnp.concatenate(parts, axis=0)

    def forward(layer):
        slot = slots_ref[layer]
        same = mask_ref[...] > 0.5
        for k in range(keyval_heads):
            query = queries_of(slot, k)
            key = keyval_ref[slot, :, head_cols(k)]
            value = keyval_ref[slot, :, pl.ds(key_width + k * head_dim, head_dim)]
            scores = lax.dot_general(
                query, key, (((1,), (1,)), ((), ())), preferred_element_type=jnp.float32
            ) * scale
            scores = jnp.where(same, scores, -jnp.inf)
            powered = jnp.exp(scores - jnp.max(scores, axis=-1, keepdims=True))
            probs = powered * (1.0 / jnp.sum(powered, axis=-1, keepdims=True))
            attended = jnp.dot(
                probs.astype(jnp.bfloat16), value, preferred_element_type=jnp.float32
            )
            for g in range(groups):
                h = k * groups + g
                rows = attended[g * token_count : (g + 1) * token_count]
                out_ref[:, head_cols(h)] = out_ref[:, head_cols(h)] + gates_ref[slot, h] * rows

    def layer_step(layer, carry):
        forward(layer)
        return carry

    lax.fori_loop(0, section, layer_step, 0)

    same_t = mask_t_ref[...] > 0.5
    own = slots_ref[section]
    for k in range(keyval_heads):
        query = queries_of(own, k)
        key = keyval_ref[own, :, head_cols(k)]
        value = keyval_ref[own, :, pl.ds(key_width + k * head_dim, head_dim)]
        scores_t = lax.dot_general(
            key, query, (((1,), (1,)), ((), ())), preferred_element_type=jnp.float32
        ) * scale
        scores_t = jnp.where(same_t, scores_t, -jnp.inf)
        powered = jnp.exp(scores_t - jnp.max(scores_t, axis=0, keepdims=True))
        probs_t = powered * (1.0 / jnp.sum(powered, axis=0, keepdims=True))
        upstream = jnp.concatenate(
            [cot_ref[:, head_cols(k * groups + g)] for g in range(groups)], axis=0
        )
        value_grad = jnp.dot(
            probs_t.astype(jnp.bfloat16), upstream, preferred_element_type=jnp.float32
        )
        prob_grad_t = lax.dot_general(
            value, upstream, (((1,), (1,)), ((), ())), preferred_element_type=jnp.float32
        )
        inner = jnp.sum(probs_t * prob_grad_t, axis=0, keepdims=True)
        score_grad_t = (probs_t * (prob_grad_t - inner)).astype(jnp.bfloat16)
        key_grad = jnp.dot(score_grad_t, query, preferred_element_type=jnp.float32) * scale
        grad_ref[:, head_cols(k)] = key_grad.astype(grad_ref.dtype)
        grad_ref[:, pl.ds(key_width + k * head_dim, head_dim)] = value_grad.astype(grad_ref.dtype)

    forward(section)


def attention_layers(
    section_index, layer_slots, gates, queries, keyval_all, gains, same_document, upstream
):
    layer_count, micro_count, image_count, pair_width = keyval_all.shape
    token_count, query_width = queries.shape[1], queries.shape[2]
    head_count = gates.shape[1]
    head_dim = query_width // head_count
    keyval_heads = pair_width // 2 // head_dim
    groups = head_count // keyval_heads
    mask = jnp.tile(same_document.astype(jnp.float32), (1, groups, 1))
    mask_t = jnp.swapaxes(mask, 1, 2)
    smem = pl.BlockSpec(memory_space=pltpu.SMEM)
    flops = 2 * micro_count * (layer_count + 3) * head_count * token_count * image_count * head_dim * 2
    return pl.pallas_call(
        functools.partial(attention_kernel, head_count=head_count, keyval_heads=keyval_heads),
        grid=(micro_count,),
        in_specs=[
            smem,
            smem,
            smem,
            pl.BlockSpec((None, token_count, query_width), lambda m: (m, 0, 0)),
            pl.BlockSpec((layer_count, None, image_count, pair_width), lambda m: (0, m, 0, 0)),
            pl.BlockSpec((layer_count, 1, query_width), lambda m: (0, 0, 0)),
            pl.BlockSpec((None, groups * token_count, image_count), lambda m: (m, 0, 0)),
            pl.BlockSpec((None, image_count, groups * token_count), lambda m: (m, 0, 0)),
            pl.BlockSpec((None, token_count, query_width), lambda m: (m, 0, 0)),
        ],
        out_specs=[
            pl.BlockSpec((None, token_count, query_width), lambda m: (m, 0, 0)),
            pl.BlockSpec((None, image_count, pair_width), lambda m: (m, 0, 0)),
        ],
        out_shape=[
            jax.ShapeDtypeStruct((micro_count, token_count, query_width), jnp.float32),
            jax.ShapeDtypeStruct((micro_count, image_count, pair_width), jnp.bfloat16),
        ],
        compiler_params=pltpu.CompilerParams(dimension_semantics=("arbitrary",)),
        cost_estimate=pl.CostEstimate(
            flops=flops,
            transcendentals=micro_count * (layer_count + 1) * head_count * token_count * image_count,
            bytes_accessed=keyval_all.size * 2 + queries.size * 8 + upstream.size * 2,
        ),
    )(
        jnp.reshape(section_index, (1,)).astype(jnp.int32),
        layer_slots.astype(jnp.int32),
        gates,
        queries,
        keyval_all,
        gains.reshape(layer_count, 1, query_width),
        mask,
        mask_t,
        upstream,
    )


def gather_blocks(block, axis):
    count = lax.axis_size(axis)
    index = lax.axis_index(axis)
    positions = jnp.arange(count, dtype=jnp.int32)
    if count > 8:
        return lax.all_gather(block, axis, axis=0, tiled=False), positions
    if count == 4:
        partner = [(i, i ^ 1) for i in range(count)]
        across = lax.ppermute(block, axis, [(i, i ^ 2) for i in range(count)])
        received = [block, lax.ppermute(block, axis, partner), across, lax.ppermute(across, axis, partner)]
        return jnp.stack(received), lax.bitwise_xor(index, positions)
    received = [block] + [
        lax.ppermute(block, axis, [(i, (i + d) % count) for i in range(count)])
        for d in range(1, count)
    ]
    return jnp.stack(received), (index - positions) % count


def gather_parts(block, axis):
    count = lax.axis_size(axis)
    partner = [(i, i ^ 1) for i in range(count)]
    across = lax.ppermute(block, axis, [(i, i ^ 2) for i in range(count)])
    return [block, lax.ppermute(block, axis, partner), across, lax.ppermute(across, axis, partner)]


def in_order(block, axis):
    stacked, slots = gather_blocks(block, axis)
    return jnp.take(stacked, slots, axis=0)


def scatter_blocks(blocks, axis, pairs):
    count = lax.axis_size(axis)
    if count > 8:
        return lax.psum_scatter(blocks, axis, scatter_dimension=0, tiled=True)[0].astype(
            jnp.float32
        )
    index = lax.axis_index(axis)

    def pick(i):
        return lax.dynamic_index_in_dim(blocks, i, 0, keepdims=False)

    if pairs and count == 4:
        partner = [(i, i ^ 1) for i in range(count)]
        got = lax.ppermute(jnp.stack([pick(index ^ 1), pick(index ^ 3)]), axis, partner)
        theirs = (pick(index ^ 2).astype(jnp.float32) + got[1].astype(jnp.float32)).astype(
            blocks.dtype
        )
        back = lax.ppermute(theirs, axis, [(i, i ^ 2) for i in range(count)])
        return (
            pick(index).astype(jnp.float32)
            + got[0].astype(jnp.float32)
            + back.astype(jnp.float32)
        )
    total = pick(index).astype(jnp.float32)
    for d in range(1, count):
        part = lax.dynamic_index_in_dim(blocks, (index + d) % count, 0, keepdims=False)
        total = total + lax.ppermute(
            part, axis, [(i, (i + d) % count) for i in range(count)]
        ).astype(jnp.float32)
    return total


def per_device(
    image_tokens,
    keyval_weight,
    query_gain,
    key_norm_gain,
    gate_logit,
    text_queries,
    text_document,
    image_document,
    cotangent,
):
    section_count = lax.axis_size("section")
    section_index = lax.axis_index("section")
    micro_count = text_queries.shape[0]
    head_count = gate_logit.shape[1]
    key_width = key_norm_gain.shape[1]
    head_dim = query_gain.shape[1] // head_count
    keyval_heads = key_width // head_dim
    weights = keyval_weight[0]

    layer_params, layer_slots = gather_blocks(
        jnp.concatenate([query_gain, gate_logit], axis=1)[0], "section"
    )
    gains_all = layer_params[:, : query_gain.shape[1]]
    gates_all = layer_params[:, query_gain.shape[1] :]

    shard_count = lax.axis_size("shard")
    owned = image_tokens.shape[1]
    image_count = owned * section_count
    total_rows = micro_count * image_count
    pair_width = 2 * key_width
    phased = section_count == 4 and shard_count == 2 * micro_count
    if phased:
        images, _ = gather_blocks(image_tokens, "section")
        images, gains_all, gates_all, layer_slots = lax.optimization_barrier(
            (images, gains_all.reshape(section_count, 1, -1), jnp.tanh(gates_all), layer_slots)
        )
        gains_all = gains_all.reshape(section_count, -1)
        gate_factors = gates_all
        raw_parts = []
        for phase in range(2):
            block = images[2 * phase : 2 * phase + 2].transpose(1, 0, 2, 3)
            block = block.reshape(-1, image_tokens.shape[2])
            partial = jnp.dot(block, weights, preferred_element_type=jnp.float32)
            raw_parts.append(
                scatter_blocks(partial.reshape(shard_count, owned, pair_width), "shard", False)
            )
        raw_rows = jnp.stack(raw_parts)
        sections = jnp.arange(section_count, dtype=jnp.int32)
        distance = lax.bitwise_xor(section_index, sections)
        micro_ids = jnp.arange(micro_count, dtype=jnp.int32)
        natural = (2 * micro_ids[:, None] + distance[None, :] % 2) * 2 + distance[None, :] // 2
        owners = jnp.arange(shard_count, dtype=jnp.int32)[:, None]
        phases = jnp.arange(2, dtype=jnp.int32)[None, :]
        held = (owners // 2) * section_count + lax.bitwise_xor(
            section_index, 2 * phases + owners % 2
        )

        def to_natural(rows):
            blocks = in_order(rows.reshape(2, owned, pair_width), "shard")
            return jnp.take(
                blocks.reshape(2 * shard_count, owned, pair_width), natural.reshape(-1), axis=0
            ).reshape(total_rows, pair_width)

        def to_owned(rows):
            return jnp.take(
                rows.reshape(micro_count * section_count, owned, pair_width),
                held.reshape(-1),
                axis=0,
            ).reshape(shard_count, 2 * owned, pair_width)

    else:
        gate_factors = jnp.tanh(gates_all)
        gathered = in_order(image_tokens, "section")
        gathered = gathered.transpose(1, 0, 2, 3).reshape(total_rows, image_tokens.shape[2])
        partial = jnp.dot(gathered, weights, preferred_element_type=jnp.float32)
        raw_rows = scatter_blocks(
            partial.reshape(shard_count, total_rows // shard_count, pair_width), "shard", False
        )

        def to_natural(rows):
            return in_order(rows, "shard").reshape(total_rows, pair_width)

        def to_owned(rows):
            return rows.reshape(shard_count, total_rows // shard_count, pair_width)

    raw_rows = raw_rows.reshape(-1, pair_width)
    key_rows = head_normalize(raw_rows[:, :key_width], key_norm_gain[0], keyval_heads)
    keyval_rows = jnp.concatenate(
        [key_rows.astype(jnp.bfloat16), raw_rows[:, key_width:].astype(jnp.bfloat16)], axis=1
    )
    keyval_own = to_natural(keyval_rows)
    keyval_all, _ = gather_blocks(keyval_own, "section")

    same_document = text_document[:, :, None] == image_document[:, None, :]
    leaving, grad_local = attention_layers(
        section_index,
        layer_slots,
        gate_factors,
        text_queries,
        keyval_all.reshape(section_count, micro_count, image_count, 2 * key_width),
        gains_all,
        same_document,
        cotangent[0],
    )
    grad_rows = scatter_blocks(to_owned(grad_local), "shard", False).reshape(-1, pair_width)
    key_portion = norm_gradient(
        raw_rows[:, :key_width], key_norm_gain[0], grad_rows[:, :key_width], keyval_heads
    )
    raw_grad_rows = jnp.concatenate([key_portion, grad_rows[:, key_width:]], axis=1).astype(
        jnp.bfloat16
    )
    owned = image_count // section_count
    if phased:
        shard_index = lax.axis_index("shard")
        products = []
        for part in gather_parts(raw_grad_rows.reshape(2, owned, pair_width), "shard"):
            product = lax.dot_general(
                part.reshape(2 * owned, pair_width),
                weights,
                (((1,), (1,)), ((), ())),
                preferred_element_type=jnp.float32,
            )
            products.append(product.astype(jnp.bfloat16).reshape(2, owned, weights.shape[0]))
        step = lax.bitwise_xor(section_index, sections)[:, None]
        source = 2 * micro_ids[None, :] + step % 2
        where = lax.bitwise_xor(shard_index, source) * 2 + step // 2
        image_part = jnp.take(
            jnp.stack(products).reshape(-1, owned, weights.shape[0]), where.reshape(-1), axis=0
        ).reshape(section_count, micro_count, owned, weights.shape[0])
    else:
        raw_grad = to_natural(raw_grad_rows)
        raw_grad = (
            raw_grad.reshape(micro_count, section_count, owned, 2 * key_width)
            .transpose(1, 0, 2, 3)
            .reshape(total_rows, 2 * key_width)
        )
        image_part = lax.dot_general(
            raw_grad, weights, (((1,), (1,)), ((), ())), preferred_element_type=jnp.float32
        )
        image_part = image_part.astype(jnp.bfloat16).reshape(
            section_count, micro_count, owned, weights.shape[0]
        )
    image_grad = scatter_blocks(image_part, "section", True)
    return (leaving[None], image_grad)


def solution(mesh):
    placed = (
        P("group", "section", "shard"),
        P("section", "shard", None),
        P("section", None),
        P("section", None),
        P("section", None),
        P("group", "shard", None),
        P("group", "shard"),
        P("group", None),
        P("section", "group", "shard", None),
    )
    return jax.shard_map(
        per_device,
        mesh=mesh,
        in_specs=placed,
        out_specs=(P("section", "group", "shard", None), P("group", "section", "shard")),
        check_vma=False,
    )
```

```python
import functools
import math

import jax
import jax.numpy as jnp
from jax import lax
from jax.experimental import pallas as pl
from jax.experimental.pallas import tpu as pltpu
from jax.sharding import PartitionSpec as P

epsilon = 1e-05


def head_normalize(input_rows, gain_row, head_count):
    shaped = input_rows.reshape(input_rows.shape[:-1] + (head_count, -1))
    factor = lax.rsqrt(jnp.mean(shaped * shaped, axis=-1, keepdims=True) + epsilon)
    gain = gain_row.reshape((1,) * (shaped.ndim - 2) + (head_count, -1))
    return (shaped * factor * gain).reshape(input_rows.shape)


def norm_gradient(input_rows, gain_row, incoming_gradient, head_count):
    shaped = input_rows.reshape(input_rows.shape[0], head_count, -1)
    scaled = incoming_gradient.reshape(input_rows.shape[0], head_count, -1) * gain_row.reshape(
        1, head_count, -1
    )
    factor = lax.rsqrt(jnp.mean(shaped * shaped, axis=-1, keepdims=True) + epsilon)
    inner_mean = jnp.mean(shaped * scaled, axis=-1, keepdims=True)
    result = factor * scaled - shaped * factor * factor * factor * inner_mean
    return result.reshape(input_rows.shape[0], -1)


def attention_kernel(
    section_ref,
    slots_ref,
    gates_ref,
    queries_ref,
    keyval_ref,
    gains_ref,
    mask_ref,
    mask_t_ref,
    cot_ref,
    out_ref,
    grad_ref,
    *,
    head_count,
    keyval_heads,
):
    token_count, query_width = out_ref.shape
    head_dim = query_width // head_count
    key_width = keyval_heads * head_dim
    groups = head_count // keyval_heads
    scale = 1.0 / math.sqrt(head_dim)
    section = section_ref[0]
    out_ref[...] = queries_ref[...].astype(jnp.float32)

    def head_cols(h):
        return pl.ds(h * head_dim, head_dim)

    def queries_of(slot, k):
        parts = []
        for g in range(groups):
            h = k * groups + g
            x = out_ref[:, head_cols(h)]
            mean_square = jnp.sum(x * x, axis=-1, keepdims=True) * (1.0 / head_dim)
            gain = gains_ref[slot, :, head_cols(h)]
            parts.append((x * lax.rsqrt(mean_square + epsilon) * gain).astype(jnp.bfloat16))
        return jnp.concatenate(parts, axis=0)

    def forward(layer):
        slot = slots_ref[layer]
        same = mask_ref[...] > 0.5
        for k in range(keyval_heads):
            query = queries_of(slot, k)
            key = keyval_ref[slot, :, head_cols(k)]
            value = keyval_ref[slot, :, pl.ds(key_width + k * head_dim, head_dim)]
            scores = lax.dot_general(
                query, key, (((1,), (1,)), ((), ())), preferred_element_type=jnp.float32
            ) * scale
            scores = jnp.where(same, scores, -jnp.inf)
            powered = jnp.exp(scores - jnp.max(scores, axis=-1, keepdims=True))
            probs = powered * (1.0 / jnp.sum(powered, axis=-1, keepdims=True))
            attended = jnp.dot(
                probs.astype(jnp.bfloat16), value, preferred_element_type=jnp.float32
            )
            for g in range(groups):
                h = k * groups + g
                rows = attended[g * token_count : (g + 1) * token_count]
                out_ref[:, head_cols(h)] = out_ref[:, head_cols(h)] + gates_ref[slot, h] * rows

    def layer_step(layer, carry):
        forward(layer)
        return carry

    lax.fori_loop(0, section, layer_step, 0)

    same_t = mask_t_ref[...] > 0.5
    own = slots_ref[section]
    for k in range(keyval_heads):
        query = queries_of(own, k)
        key = keyval_ref[own, :, head_cols(k)]
        value = keyval_ref[own, :, pl.ds(key_width + k * head_dim, head_dim)]
        scores_t = lax.dot_general(
            key, query, (((1,), (1,)), ((), ())), preferred_element_type=jnp.float32
        ) * scale
        scores_t = jnp.where(same_t, scores_t, -jnp.inf)
        powered = jnp.exp(scores_t - jnp.max(scores_t, axis=0, keepdims=True))
        probs_t = powered * (1.0 / jnp.sum(powered, axis=0, keepdims=True))
        upstream = jnp.concatenate(
            [cot_ref[:, head_cols(k * groups + g)] for g in range(groups)], axis=0
        )
        value_grad = jnp.dot(
            probs_t.astype(jnp.bfloat16), upstream, preferred_element_type=jnp.float32
        )
        prob_grad_t = lax.dot_general(
            value, upstream, (((1,), (1,)), ((), ())), preferred_element_type=jnp.float32
        )
        inner = jnp.sum(probs_t * prob_grad_t, axis=0, keepdims=True)
        score_grad_t = (probs_t * (prob_grad_t - inner)).astype(jnp.bfloat16)
        key_grad = jnp.dot(score_grad_t, query, preferred_element_type=jnp.float32) * scale
        grad_ref[:, head_cols(k)] = key_grad.astype(grad_ref.dtype)
        grad_ref[:, pl.ds(key_width + k * head_dim, head_dim)] = value_grad.astype(grad_ref.dtype)

    forward(section)


def attention_layers(
    section_index, layer_slots, gates, queries, keyval_all, gains, same_document, upstream
):
    layer_count, micro_count, image_count, pair_width = keyval_all.shape
    token_count, query_width = queries.shape[1], queries.shape[2]
    head_count = gates.shape[1]
    head_dim = query_width // head_count
    keyval_heads = pair_width // 2 // head_dim
    groups = head_count // keyval_heads
    mask = jnp.tile(same_document.astype(jnp.float32), (1, groups, 1))
    mask_t = jnp.swapaxes(mask, 1, 2)
    smem = pl.BlockSpec(memory_space=pltpu.SMEM)
    flops = 2 * micro_count * (layer_count + 3) * head_count * token_count * image_count * head_dim * 2
    return pl.pallas_call(
        functools.partial(attention_kernel, head_count=head_count, keyval_heads=keyval_heads),
        grid=(micro_count,),
        in_specs=[
            smem,
            smem,
            smem,
            pl.BlockSpec((None, token_count, query_width), lambda m: (m, 0, 0)),
            pl.BlockSpec((layer_count, None, image_count, pair_width), lambda m: (0, m, 0, 0)),
            pl.BlockSpec((layer_count, 1, query_width), lambda m: (0, 0, 0)),
            pl.BlockSpec((None, groups * token_count, image_count), lambda m: (m, 0, 0)),
            pl.BlockSpec((None, image_count, groups * token_count), lambda m: (m, 0, 0)),
            pl.BlockSpec((None, token_count, query_width), lambda m: (m, 0, 0)),
        ],
        out_specs=[
            pl.BlockSpec((None, token_count, query_width), lambda m: (m, 0, 0)),
            pl.BlockSpec((None, image_count, pair_width), lambda m: (m, 0, 0)),
        ],
        out_shape=[
            jax.ShapeDtypeStruct((micro_count, token_count, query_width), jnp.float32),
            jax.ShapeDtypeStruct((micro_count, image_count, pair_width), jnp.bfloat16),
        ],
        compiler_params=pltpu.CompilerParams(dimension_semantics=("arbitrary",)),
        cost_estimate=pl.CostEstimate(
            flops=flops,
            transcendentals=micro_count * (layer_count + 1) * head_count * token_count * image_count,
            bytes_accessed=keyval_all.size * 2 + queries.size * 8 + upstream.size * 2,
        ),
    )(
        jnp.reshape(section_index, (1,)).astype(jnp.int32),
        layer_slots.astype(jnp.int32),
        gates,
        queries,
        keyval_all,
        gains.reshape(layer_count, 1, query_width),
        mask,
        mask_t,
        upstream,
    )


def gather_blocks(block, axis):
    count = lax.axis_size(axis)
    index = lax.axis_index(axis)
    positions = jnp.arange(count, dtype=jnp.int32)
    if count > 8:
        return lax.all_gather(block, axis, axis=0, tiled=False), positions
    if count == 4:
        partner = [(i, i ^ 1) for i in range(count)]
        across = lax.ppermute(block, axis, [(i, i ^ 2) for i in range(count)])
        received = [block, lax.ppermute(block, axis, partner), across, lax.ppermute(across, axis, partner)]
        return jnp.stack(received), lax.bitwise_xor(index, positions)
    received = [block] + [
        lax.ppermute(block, axis, [(i, (i + d) % count) for i in range(count)])
        for d in range(1, count)
    ]
    return jnp.stack(received), (index - positions) % count


def in_order(block, axis):
    stacked, slots = gather_blocks(block, axis)
    return jnp.take(stacked, slots, axis=0)


def scatter_blocks(blocks, axis, pairs):
    count = lax.axis_size(axis)
    if count > 8:
        return lax.psum_scatter(blocks, axis, scatter_dimension=0, tiled=True)[0].astype(
            jnp.float32
        )
    index = lax.axis_index(axis)

    def pick(i):
        return lax.dynamic_index_in_dim(blocks, i, 0, keepdims=False)

    if pairs and count == 4:
        partner = [(i, i ^ 1) for i in range(count)]
        got = lax.ppermute(jnp.stack([pick(index ^ 1), pick(index ^ 3)]), axis, partner)
        theirs = (pick(index ^ 2).astype(jnp.float32) + got[1].astype(jnp.float32)).astype(
            blocks.dtype
        )
        back = lax.ppermute(theirs, axis, [(i, i ^ 2) for i in range(count)])
        return (
            pick(index).astype(jnp.float32)
            + got[0].astype(jnp.float32)
            + back.astype(jnp.float32)
        )
    total = pick(index).astype(jnp.float32)
    for d in range(1, count):
        part = lax.dynamic_index_in_dim(blocks, (index + d) % count, 0, keepdims=False)
        total = total + lax.ppermute(
            part, axis, [(i, (i + d) % count) for i in range(count)]
        ).astype(jnp.float32)
    return total


def per_device(
    image_tokens,
    keyval_weight,
    query_gain,
    key_norm_gain,
    gate_logit,
    text_queries,
    text_document,
    image_document,
    cotangent,
):
    section_count = lax.axis_size("section")
    section_index = lax.axis_index("section")
    micro_count = text_queries.shape[0]
    head_count = gate_logit.shape[1]
    key_width = key_norm_gain.shape[1]
    head_dim = query_gain.shape[1] // head_count
    keyval_heads = key_width // head_dim
    weights = keyval_weight[0]

    layer_params, layer_slots = gather_blocks(
        jnp.concatenate([query_gain, gate_logit], axis=1)[0], "section"
    )
    gains_all = layer_params[:, : query_gain.shape[1]]
    gates_all = layer_params[:, query_gain.shape[1] :]

    shard_count = lax.axis_size("shard")
    owned = image_tokens.shape[1]
    image_count = owned * section_count
    total_rows = micro_count * image_count
    pair_width = 2 * key_width
    phased = section_count == 4 and shard_count == 2 * micro_count
    if phased:
        images, _ = gather_blocks(image_tokens, "section")
        raw_parts = []
        for phase in range(2):
            block = images[2 * phase : 2 * phase + 2].transpose(1, 0, 2, 3)
            block = block.reshape(-1, image_tokens.shape[2])
            partial = jnp.dot(block, weights, preferred_element_type=jnp.float32)
            raw_parts.append(
                scatter_blocks(partial.reshape(shard_count, owned, pair_width), "shard", False)
            )
        raw_rows = jnp.stack(raw_parts)
        sections = jnp.arange(section_count, dtype=jnp.int32)
        distance = lax.bitwise_xor(section_index, sections)
        micro_ids = jnp.arange(micro_count, dtype=jnp.int32)
        natural = (2 * micro_ids[:, None] + distance[None, :] % 2) * 2 + distance[None, :] // 2
        owners = jnp.arange(shard_count, dtype=jnp.int32)[:, None]
        phases = jnp.arange(2, dtype=jnp.int32)[None, :]
        held = (owners // 2) * section_count + lax.bitwise_xor(
            section_index, 2 * phases + owners % 2
        )

        def to_natural(rows):
            blocks = in_order(rows.reshape(2, owned, pair_width), "shard")
            return jnp.take(
                blocks.reshape(2 * shard_count, owned, pair_width), natural.reshape(-1), axis=0
            ).reshape(total_rows, pair_width)

        def to_owned(rows):
            return jnp.take(
                rows.reshape(micro_count * section_count, owned, pair_width),
                held.reshape(-1),
                axis=0,
            ).reshape(shard_count, 2 * owned, pair_width)

    else:
        gathered = in_order(image_tokens, "section")
        gathered = gathered.transpose(1, 0, 2, 3).reshape(total_rows, image_tokens.shape[2])
        partial = jnp.dot(gathered, weights, preferred_element_type=jnp.float32)
        raw_rows = scatter_blocks(
            partial.reshape(shard_count, total_rows // shard_count, pair_width), "shard", False
        )

        def to_natural(rows):
            return in_order(rows, "shard").reshape(total_rows, pair_width)

        def to_owned(rows):
            return rows.reshape(shard_count, total_rows // shard_count, pair_width)

    def keyval_of(raw):
        keys = head_normalize(raw[:, :key_width], key_norm_gain[0], keyval_heads)
        return jnp.concatenate(
            [keys.astype(jnp.bfloat16), raw[:, key_width:].astype(jnp.bfloat16)], axis=1
        )

    if phased:
        per_phase = []
        for phase in range(2):
            blocks = in_order(keyval_of(raw_parts[phase]), "shard")
            per_phase.append(gather_blocks(blocks, "section")[0])
        both = jnp.stack(per_phase, axis=1)
        slot_ids = sections[:, None, None]
        crossing = lax.bitwise_xor(
            lax.bitwise_xor(section_index, slot_ids), sections[None, None, :]
        )
        holder = 2 * micro_ids[None, :, None] + crossing % 2
        flat = (slot_ids * 2 + crossing // 2) * shard_count + holder
        keyval_all = jnp.take(
            both.reshape(-1, owned, pair_width), flat.reshape(-1), axis=0
        ).reshape(section_count, total_rows, pair_width)
    else:
        keyval_all, _ = gather_blocks(
            to_natural(keyval_of(raw_rows.reshape(-1, pair_width))), "section"
        )
    raw_rows = raw_rows.reshape(-1, pair_width)

    same_document = text_document[:, :, None] == image_document[:, None, :]
    leaving, grad_local = attention_layers(
        section_index,
        layer_slots,
        jnp.tanh(gates_all),
        text_queries,
        keyval_all.reshape(section_count, micro_count, image_count, 2 * key_width),
        gains_all,
        same_document,
        cotangent[0],
    )
    grad_rows = scatter_blocks(to_owned(grad_local), "shard", False).reshape(-1, pair_width)
    key_portion = norm_gradient(
        raw_rows[:, :key_width], key_norm_gain[0], grad_rows[:, :key_width], keyval_heads
    )
    raw_grad_rows = jnp.concatenate([key_portion, grad_rows[:, key_width:]], axis=1).astype(
        jnp.bfloat16
    )
    raw_grad = to_natural(raw_grad_rows)
    owned = image_count // section_count
    raw_grad = (
        raw_grad.reshape(micro_count, section_count, owned, 2 * key_width)
        .transpose(1, 0, 2, 3)
        .reshape(total_rows, 2 * key_width)
    )
    image_part = lax.dot_general(
        raw_grad, weights, (((1,), (1,)), ((), ())), preferred_element_type=jnp.float32
    )
    image_part = image_part.astype(jnp.bfloat16).reshape(
        section_count, micro_count, owned, weights.shape[0]
    )
    image_grad = scatter_blocks(image_part, "section", True)
    return (leaving[None], image_grad)


def solution(mesh):
    placed = (
        P("group", "section", "shard"),
        P("section", "shard", None),
        P("section", None),
        P("section", None),
        P("section", None),
        P("group", "shard", None),
        P("group", "shard"),
        P("group", None),
        P("section", "group", "shard", None),
    )
    return jax.shard_map(
        per_device,
        mesh=mesh,
        in_specs=placed,
        out_specs=(P("section", "group", "shard", None), P("group", "section", "shard")),
        check_vma=False,
    )
```

```python
import functools
import math

import jax
import jax.numpy as jnp
from jax import lax
from jax.experimental import pallas as pl
from jax.experimental.pallas import tpu as pltpu
from jax.sharding import PartitionSpec as P

epsilon = 1e-05


def head_normalize(input_rows, gain_row, head_count):
    shaped = input_rows.reshape(input_rows.shape[:-1] + (head_count, -1))
    factor = lax.rsqrt(jnp.mean(shaped * shaped, axis=-1, keepdims=True) + epsilon)
    gain = gain_row.reshape((1,) * (shaped.ndim - 2) + (head_count, -1))
    return (shaped * factor * gain).reshape(input_rows.shape)


def norm_gradient(input_rows, gain_row, incoming_gradient, head_count):
    shaped = input_rows.reshape(input_rows.shape[0], head_count, -1)
    scaled = incoming_gradient.reshape(input_rows.shape[0], head_count, -1) * gain_row.reshape(
        1, head_count, -1
    )
    factor = lax.rsqrt(jnp.mean(shaped * shaped, axis=-1, keepdims=True) + epsilon)
    inner_mean = jnp.mean(shaped * scaled, axis=-1, keepdims=True)
    result = factor * scaled - shaped * factor * factor * factor * inner_mean
    return result.reshape(input_rows.shape[0], -1)


def attention_kernel(
    section_ref,
    slots_ref,
    gates_ref,
    queries_ref,
    keyval_ref,
    gains_ref,
    mask_ref,
    mask_t_ref,
    cot_ref,
    out_ref,
    grad_ref,
    *,
    head_count,
    keyval_heads,
):
    token_count, query_width = out_ref.shape
    head_dim = query_width // head_count
    key_width = keyval_heads * head_dim
    groups = head_count // keyval_heads
    scale = 1.0 / math.sqrt(head_dim)
    section = section_ref[0]
    out_ref[...] = queries_ref[...].astype(jnp.float32)

    def head_cols(h):
        return pl.ds(h * head_dim, head_dim)

    def queries_of(slot, k):
        parts = []
        for g in range(groups):
            h = k * groups + g
            x = out_ref[:, head_cols(h)]
            mean_square = jnp.sum(x * x, axis=-1, keepdims=True) * (1.0 / head_dim)
            gain = gains_ref[slot, :, head_cols(h)]
            parts.append((x * lax.rsqrt(mean_square + epsilon) * gain).astype(jnp.bfloat16))
        return jnp.concatenate(parts, axis=0)

    def forward(layer):
        slot = slots_ref[layer]
        same = mask_ref[...] > 0.5
        for k in range(keyval_heads):
            query = queries_of(slot, k)
            key = keyval_ref[slot, :, head_cols(k)]
            value = keyval_ref[slot, :, pl.ds(key_width + k * head_dim, head_dim)]
            scores = lax.dot_general(
                query, key, (((1,), (1,)), ((), ())), preferred_element_type=jnp.float32
            ) * scale
            scores = jnp.where(same, scores, -jnp.inf)
            powered = jnp.exp(scores - jnp.max(scores, axis=-1, keepdims=True))
            probs = powered * (1.0 / jnp.sum(powered, axis=-1, keepdims=True))
            attended = jnp.dot(
                probs.astype(jnp.bfloat16), value, preferred_element_type=jnp.float32
            )
            for g in range(groups):
                h = k * groups + g
                rows = attended[g * token_count : (g + 1) * token_count]
                out_ref[:, head_cols(h)] = out_ref[:, head_cols(h)] + gates_ref[slot, h] * rows

    def layer_step(layer, carry):
        forward(layer)
        return carry

    lax.fori_loop(0, section, layer_step, 0)

    same_t = mask_t_ref[...] > 0.5
    own = slots_ref[section]
    for k in range(keyval_heads):
        query = queries_of(own, k)
        key = keyval_ref[own, :, head_cols(k)]
        value = keyval_ref[own, :, pl.ds(key_width + k * head_dim, head_dim)]
        scores_t = lax.dot_general(
            key, query, (((1,), (1,)), ((), ())), preferred_element_type=jnp.float32
        ) * scale
        scores_t = jnp.where(same_t, scores_t, -jnp.inf)
        powered = jnp.exp(scores_t - jnp.max(scores_t, axis=0, keepdims=True))
        probs_t = powered * (1.0 / jnp.sum(powered, axis=0, keepdims=True))
        upstream = jnp.concatenate(
            [cot_ref[:, head_cols(k * groups + g)] for g in range(groups)], axis=0
        )
        value_grad = jnp.dot(
            probs_t.astype(jnp.bfloat16), upstream, preferred_element_type=jnp.float32
        )
        prob_grad_t = lax.dot_general(
            value, upstream, (((1,), (1,)), ((), ())), preferred_element_type=jnp.float32
        )
        inner = jnp.sum(probs_t * prob_grad_t, axis=0, keepdims=True)
        score_grad_t = (probs_t * (prob_grad_t - inner)).astype(jnp.bfloat16)
        key_grad = jnp.dot(score_grad_t, query, preferred_element_type=jnp.float32) * scale
        grad_ref[:, head_cols(k)] = key_grad.astype(grad_ref.dtype)
        grad_ref[:, pl.ds(key_width + k * head_dim, head_dim)] = value_grad.astype(grad_ref.dtype)

    forward(section)


def attention_layers(
    section_index, layer_slots, gates, queries, keyval_all, gains, same_document, upstream
):
    layer_count, micro_count, image_count, pair_width = keyval_all.shape
    token_count, query_width = queries.shape[1], queries.shape[2]
    head_count = gates.shape[1]
    head_dim = query_width // head_count
    keyval_heads = pair_width // 2 // head_dim
    groups = head_count // keyval_heads
    mask = jnp.tile(same_document.astype(jnp.float32), (1, groups, 1))
    mask_t = jnp.swapaxes(mask, 1, 2)
    smem = pl.BlockSpec(memory_space=pltpu.SMEM)
    flops = 2 * micro_count * (layer_count + 3) * head_count * token_count * image_count * head_dim * 2
    return pl.pallas_call(
        functools.partial(attention_kernel, head_count=head_count, keyval_heads=keyval_heads),
        grid=(micro_count,),
        in_specs=[
            smem,
            smem,
            smem,
            pl.BlockSpec((None, token_count, query_width), lambda m: (m, 0, 0)),
            pl.BlockSpec((layer_count, None, image_count, pair_width), lambda m: (0, m, 0, 0)),
            pl.BlockSpec((layer_count, 1, query_width), lambda m: (0, 0, 0)),
            pl.BlockSpec((None, groups * token_count, image_count), lambda m: (m, 0, 0)),
            pl.BlockSpec((None, image_count, groups * token_count), lambda m: (m, 0, 0)),
            pl.BlockSpec((None, token_count, query_width), lambda m: (m, 0, 0)),
        ],
        out_specs=[
            pl.BlockSpec((None, token_count, query_width), lambda m: (m, 0, 0)),
            pl.BlockSpec((None, image_count, pair_width), lambda m: (m, 0, 0)),
        ],
        out_shape=[
            jax.ShapeDtypeStruct((micro_count, token_count, query_width), jnp.float32),
            jax.ShapeDtypeStruct((micro_count, image_count, pair_width), jnp.bfloat16),
        ],
        compiler_params=pltpu.CompilerParams(dimension_semantics=("arbitrary",)),
        cost_estimate=pl.CostEstimate(
            flops=flops,
            transcendentals=micro_count * (layer_count + 1) * head_count * token_count * image_count,
            bytes_accessed=keyval_all.size * 2 + queries.size * 8 + upstream.size * 2,
        ),
    )(
        jnp.reshape(section_index, (1,)).astype(jnp.int32),
        layer_slots.astype(jnp.int32),
        gates,
        queries,
        keyval_all,
        gains.reshape(layer_count, 1, query_width),
        mask,
        mask_t,
        upstream,
    )


def gather_blocks(block, axis):
    count = lax.axis_size(axis)
    index = lax.axis_index(axis)
    positions = jnp.arange(count, dtype=jnp.int32)
    if count > 8:
        return lax.all_gather(block, axis, axis=0, tiled=False), positions
    if count == 4:
        partner = [(i, i ^ 1) for i in range(count)]
        across = lax.ppermute(block, axis, [(i, i ^ 2) for i in range(count)])
        received = [block, lax.ppermute(block, axis, partner), across, lax.ppermute(across, axis, partner)]
        return jnp.stack(received), lax.bitwise_xor(index, positions)
    received = [block] + [
        lax.ppermute(block, axis, [(i, (i + d) % count) for i in range(count)])
        for d in range(1, count)
    ]
    return jnp.stack(received), (index - positions) % count


def in_order(block, axis):
    stacked, slots = gather_blocks(block, axis)
    return jnp.take(stacked, slots, axis=0)


def scatter_blocks(blocks, axis, pairs):
    count = lax.axis_size(axis)
    if count > 8:
        return lax.psum_scatter(blocks, axis, scatter_dimension=0, tiled=True)[0].astype(
            jnp.float32
        )
    index = lax.axis_index(axis)

    def pick(i):
        return lax.dynamic_index_in_dim(blocks, i, 0, keepdims=False)

    if pairs and count == 4:
        partner = [(i, i ^ 1) for i in range(count)]
        got = lax.ppermute(jnp.stack([pick(index ^ 1), pick(index ^ 3)]), axis, partner)
        theirs = (pick(index ^ 2).astype(jnp.float32) + got[1].astype(jnp.float32)).astype(
            blocks.dtype
        )
        back = lax.ppermute(theirs, axis, [(i, i ^ 2) for i in range(count)])
        return (
            pick(index).astype(jnp.float32)
            + got[0].astype(jnp.float32)
            + back.astype(jnp.float32)
        )
    total = pick(index).astype(jnp.float32)
    for d in range(1, count):
        part = lax.dynamic_index_in_dim(blocks, (index + d) % count, 0, keepdims=False)
        total = total + lax.ppermute(
            part, axis, [(i, (i + d) % count) for i in range(count)]
        ).astype(jnp.float32)
    return total


def per_device(
    image_tokens,
    keyval_weight,
    query_gain,
    key_norm_gain,
    gate_logit,
    text_queries,
    text_document,
    image_document,
    cotangent,
):
    section_count = lax.axis_size("section")
    section_index = lax.axis_index("section")
    micro_count = text_queries.shape[0]
    head_count = gate_logit.shape[1]
    key_width = key_norm_gain.shape[1]
    head_dim = query_gain.shape[1] // head_count
    keyval_heads = key_width // head_dim
    weights = keyval_weight[0]

    layer_params, layer_slots = gather_blocks(
        jnp.concatenate([query_gain, gate_logit], axis=1)[0], "section"
    )
    gains_all = layer_params[:, : query_gain.shape[1]]
    gates_all = layer_params[:, query_gain.shape[1] :]

    shard_count = lax.axis_size("shard")
    owned = image_tokens.shape[1]
    image_count = owned * section_count
    total_rows = micro_count * image_count
    pair_width = 2 * key_width
    phased = section_count == 4 and shard_count == 2 * micro_count
    if phased:
        images, _ = gather_blocks(image_tokens, "section")
        raw_parts = []
        for phase in range(2):
            block = images[2 * phase : 2 * phase + 2].transpose(1, 0, 2, 3)
            block = block.reshape(-1, image_tokens.shape[2])
            partial = jnp.dot(block, weights, preferred_element_type=jnp.float32)
            raw_parts.append(
                scatter_blocks(partial.reshape(shard_count, owned, pair_width), "shard", False)
            )
        raw_rows = jnp.stack(raw_parts)
        sections = jnp.arange(section_count, dtype=jnp.int32)
        distance = lax.bitwise_xor(section_index, sections)
        micro_ids = jnp.arange(micro_count, dtype=jnp.int32)
        natural = (2 * micro_ids[:, None] + distance[None, :] % 2) * 2 + distance[None, :] // 2
        owners = jnp.arange(shard_count, dtype=jnp.int32)[:, None]
        phases = jnp.arange(2, dtype=jnp.int32)[None, :]
        held = (owners // 2) * section_count + lax.bitwise_xor(
            section_index, 2 * phases + owners % 2
        )

        def to_natural(rows):
            blocks = in_order(rows.reshape(2, owned, pair_width), "shard")
            return jnp.take(
                blocks.reshape(2 * shard_count, owned, pair_width), natural.reshape(-1), axis=0
            ).reshape(total_rows, pair_width)

        def to_owned(rows):
            return jnp.take(
                rows.reshape(micro_count * section_count, owned, pair_width),
                held.reshape(-1),
                axis=0,
            ).reshape(shard_count, 2 * owned, pair_width)

    else:
        gathered = in_order(image_tokens, "section")
        gathered = gathered.transpose(1, 0, 2, 3).reshape(total_rows, image_tokens.shape[2])
        partial = jnp.dot(gathered, weights, preferred_element_type=jnp.float32)
        raw_rows = scatter_blocks(
            partial.reshape(shard_count, total_rows // shard_count, pair_width), "shard", False
        )

        def to_natural(rows):
            return in_order(rows, "shard").reshape(total_rows, pair_width)

        def to_owned(rows):
            return rows.reshape(shard_count, total_rows // shard_count, pair_width)

    raw_rows = raw_rows.reshape(-1, pair_width)
    key_rows = head_normalize(raw_rows[:, :key_width], key_norm_gain[0], keyval_heads)
    keyval_rows = jnp.concatenate(
        [key_rows.astype(jnp.bfloat16), raw_rows[:, key_width:].astype(jnp.bfloat16)], axis=1
    )
    keyval_own = to_natural(keyval_rows)
    keyval_all, _ = gather_blocks(keyval_own, "section")

    same_document = text_document[:, :, None] == image_document[:, None, :]
    leaving, grad_local = attention_layers(
        section_index,
        layer_slots,
        jnp.tanh(gates_all),
        text_queries,
        keyval_all.reshape(section_count, micro_count, image_count, 2 * key_width),
        gains_all,
        same_document,
        cotangent[0],
    )
    if phased and shard_count <= 8:
        shard_index = lax.axis_index("shard")
        grad_blocks = grad_local.reshape(micro_count * section_count, owned, pair_width)
        held_flat = held.reshape(-1)

        def owned_rows(j):
            return jnp.concatenate(
                [
                    lax.dynamic_index_in_dim(grad_blocks, held_flat[2 * j + h], 0, keepdims=False)
                    for h in range(2)
                ],
                axis=0,
            )

        grad_rows = owned_rows(shard_index).astype(jnp.float32)
        for d in range(1, shard_count):
            grad_rows = grad_rows + lax.ppermute(
                owned_rows((shard_index + d) % shard_count),
                "shard",
                [(i, (i + d) % shard_count) for i in range(shard_count)],
            ).astype(jnp.float32)
    else:
        grad_rows = scatter_blocks(to_owned(grad_local), "shard", False).reshape(-1, pair_width)
    key_portion = norm_gradient(
        raw_rows[:, :key_width], key_norm_gain[0], grad_rows[:, :key_width], keyval_heads
    )
    raw_grad_rows = jnp.concatenate([key_portion, grad_rows[:, key_width:]], axis=1).astype(
        jnp.bfloat16
    )
    owned = image_count // section_count
    if phased:
        raw_blocks = in_order(raw_grad_rows.reshape(2, owned, pair_width), "shard")
        raw_grad = jnp.take(
            raw_blocks.reshape(2 * shard_count, owned, pair_width),
            natural.T.reshape(-1),
            axis=0,
        ).reshape(total_rows, pair_width)
    else:
        raw_grad = to_natural(raw_grad_rows)
        raw_grad = (
            raw_grad.reshape(micro_count, section_count, owned, 2 * key_width)
            .transpose(1, 0, 2, 3)
            .reshape(total_rows, 2 * key_width)
        )
    image_part = lax.dot_general(
        raw_grad, weights, (((1,), (1,)), ((), ())), preferred_element_type=jnp.float32
    )
    image_part = image_part.astype(jnp.bfloat16).reshape(
        section_count, micro_count, owned, weights.shape[0]
    )
    image_grad = scatter_blocks(image_part, "section", True)
    return (leaving[None], image_grad)


def solution(mesh):
    placed = (
        P("group", "section", "shard"),
        P("section", "shard", None),
        P("section", None),
        P("section", None),
        P("section", None),
        P("group", "shard", None),
        P("group", "shard"),
        P("group", None),
        P("section", "group", "shard", None),
    )
    return jax.shard_map(
        per_device,
        mesh=mesh,
        in_specs=placed,
        out_specs=(P("section", "group", "shard", None), P("group", "section", "shard")),
        check_vma=False,
    )
```

```python
import functools
import math

import jax
import jax.numpy as jnp
from jax import lax
from jax.experimental import pallas as pl
from jax.experimental.pallas import tpu as pltpu
from jax.sharding import PartitionSpec as P

epsilon = 1e-05


def head_normalize(input_rows, gain_row, head_count):
    shaped = input_rows.reshape(input_rows.shape[:-1] + (head_count, -1))
    factor = lax.rsqrt(jnp.mean(shaped * shaped, axis=-1, keepdims=True) + epsilon)
    gain = gain_row.reshape((1,) * (shaped.ndim - 2) + (head_count, -1))
    return (shaped * factor * gain).reshape(input_rows.shape)


def norm_gradient(input_rows, gain_row, incoming_gradient, head_count):
    shaped = input_rows.reshape(input_rows.shape[0], head_count, -1)
    scaled = incoming_gradient.reshape(input_rows.shape[0], head_count, -1) * gain_row.reshape(
        1, head_count, -1
    )
    factor = lax.rsqrt(jnp.mean(shaped * shaped, axis=-1, keepdims=True) + epsilon)
    inner_mean = jnp.mean(shaped * scaled, axis=-1, keepdims=True)
    result = factor * scaled - shaped * factor * factor * factor * inner_mean
    return result.reshape(input_rows.shape[0], -1)


def attention_kernel(
    section_ref,
    slots_ref,
    gates_ref,
    queries_ref,
    keyval_ref,
    gains_ref,
    mask_ref,
    mask_t_ref,
    cot_ref,
    out_ref,
    grad_ref,
    *,
    head_count,
    keyval_heads,
):
    token_count, query_width = out_ref.shape
    head_dim = query_width // head_count
    key_width = keyval_heads * head_dim
    groups = head_count // keyval_heads
    scale = 1.0 / math.sqrt(head_dim)
    section = section_ref[0]
    out_ref[...] = queries_ref[...].astype(jnp.float32)

    def head_cols(h):
        return pl.ds(h * head_dim, head_dim)

    def queries_of(slot, k):
        parts = []
        for g in range(groups):
            h = k * groups + g
            x = out_ref[:, head_cols(h)]
            mean_square = jnp.sum(x * x, axis=-1, keepdims=True) * (1.0 / head_dim)
            gain = gains_ref[slot, :, head_cols(h)]
            parts.append((x * lax.rsqrt(mean_square + epsilon) * gain).astype(jnp.bfloat16))
        return jnp.concatenate(parts, axis=0)

    def forward(layer):
        slot = slots_ref[layer]
        same = mask_ref[...] > 0.5
        for k in range(keyval_heads):
            query = queries_of(slot, k)
            key = keyval_ref[slot, :, head_cols(k)]
            value = keyval_ref[slot, :, pl.ds(key_width + k * head_dim, head_dim)]
            scores = lax.dot_general(
                query, key, (((1,), (1,)), ((), ())), preferred_element_type=jnp.float32
            ) * scale
            scores = jnp.where(same, scores, -jnp.inf)
            powered = jnp.exp(scores - jnp.max(scores, axis=-1, keepdims=True))
            probs = powered * (1.0 / jnp.sum(powered, axis=-1, keepdims=True))
            attended = jnp.dot(
                probs.astype(jnp.bfloat16), value, preferred_element_type=jnp.float32
            )
            for g in range(groups):
                h = k * groups + g
                rows = attended[g * token_count : (g + 1) * token_count]
                out_ref[:, head_cols(h)] = out_ref[:, head_cols(h)] + gates_ref[slot, h] * rows

    def layer_step(layer, carry):
        forward(layer)
        return carry

    lax.fori_loop(0, section, layer_step, 0)

    same_t = mask_t_ref[...] > 0.5
    own = slots_ref[section]
    for k in range(keyval_heads):
        query = queries_of(own, k)
        key = keyval_ref[own, :, head_cols(k)]
        value = keyval_ref[own, :, pl.ds(key_width + k * head_dim, head_dim)]
        scores_t = lax.dot_general(
            key, query, (((1,), (1,)), ((), ())), preferred_element_type=jnp.float32
        ) * scale
        scores_t = jnp.where(same_t, scores_t, -jnp.inf)
        powered = jnp.exp(scores_t - jnp.max(scores_t, axis=0, keepdims=True))
        probs_t = powered * (1.0 / jnp.sum(powered, axis=0, keepdims=True))
        upstream = jnp.concatenate(
            [cot_ref[:, head_cols(k * groups + g)] for g in range(groups)], axis=0
        )
        value_grad = jnp.dot(
            probs_t.astype(jnp.bfloat16), upstream, preferred_element_type=jnp.float32
        )
        prob_grad_t = lax.dot_general(
            value, upstream, (((1,), (1,)), ((), ())), preferred_element_type=jnp.float32
        )
        inner = jnp.sum(probs_t * prob_grad_t, axis=0, keepdims=True)
        score_grad_t = (probs_t * (prob_grad_t - inner)).astype(jnp.bfloat16)
        key_grad = jnp.dot(score_grad_t, query, preferred_element_type=jnp.float32) * scale
        grad_ref[:, head_cols(k)] = key_grad.astype(grad_ref.dtype)
        grad_ref[:, pl.ds(key_width + k * head_dim, head_dim)] = value_grad.astype(grad_ref.dtype)

    forward(section)


def attention_layers(
    section_index, layer_slots, gates, queries, keyval_all, gains, same_document, upstream
):
    layer_count, micro_count, image_count, pair_width = keyval_all.shape
    token_count, query_width = queries.shape[1], queries.shape[2]
    head_count = gates.shape[1]
    head_dim = query_width // head_count
    keyval_heads = pair_width // 2 // head_dim
    groups = head_count // keyval_heads
    mask = jnp.tile(same_document.astype(jnp.float32), (1, groups, 1))
    mask_t = jnp.swapaxes(mask, 1, 2)
    smem = pl.BlockSpec(memory_space=pltpu.SMEM)
    flops = 2 * micro_count * (layer_count + 3) * head_count * token_count * image_count * head_dim * 2
    return pl.pallas_call(
        functools.partial(attention_kernel, head_count=head_count, keyval_heads=keyval_heads),
        grid=(micro_count,),
        in_specs=[
            smem,
            smem,
            smem,
            pl.BlockSpec((None, token_count, query_width), lambda m: (m, 0, 0)),
            pl.BlockSpec((layer_count, None, image_count, pair_width), lambda m: (0, m, 0, 0)),
            pl.BlockSpec((layer_count, 1, query_width), lambda m: (0, 0, 0)),
            pl.BlockSpec((None, groups * token_count, image_count), lambda m: (m, 0, 0)),
            pl.BlockSpec((None, image_count, groups * token_count), lambda m: (m, 0, 0)),
            pl.BlockSpec((None, token_count, query_width), lambda m: (m, 0, 0)),
        ],
        out_specs=[
            pl.BlockSpec((None, token_count, query_width), lambda m: (m, 0, 0)),
            pl.BlockSpec((None, image_count, pair_width), lambda m: (m, 0, 0)),
        ],
        out_shape=[
            jax.ShapeDtypeStruct((micro_count, token_count, query_width), jnp.float32),
            jax.ShapeDtypeStruct((micro_count, image_count, pair_width), jnp.bfloat16),
        ],
        compiler_params=pltpu.CompilerParams(dimension_semantics=("arbitrary",)),
        cost_estimate=pl.CostEstimate(
            flops=flops,
            transcendentals=micro_count * (layer_count + 1) * head_count * token_count * image_count,
            bytes_accessed=keyval_all.size * 2 + queries.size * 8 + upstream.size * 2,
        ),
    )(
        jnp.reshape(section_index, (1,)).astype(jnp.int32),
        layer_slots.astype(jnp.int32),
        gates,
        queries,
        keyval_all,
        gains.reshape(layer_count, 1, query_width),
        mask,
        mask_t,
        upstream,
    )


def gather_blocks(block, axis):
    count = lax.axis_size(axis)
    index = lax.axis_index(axis)
    positions = jnp.arange(count, dtype=jnp.int32)
    if count > 8:
        return lax.all_gather(block, axis, axis=0, tiled=False), positions
    if count == 4:
        partner = [(i, i ^ 1) for i in range(count)]
        across = lax.ppermute(block, axis, [(i, i ^ 2) for i in range(count)])
        received = [block, lax.ppermute(block, axis, partner), across, lax.ppermute(across, axis, partner)]
        return jnp.stack(received), lax.bitwise_xor(index, positions)
    received = [block] + [
        lax.ppermute(block, axis, [(i, (i + d) % count) for i in range(count)])
        for d in range(1, count)
    ]
    return jnp.stack(received), (index - positions) % count


def in_order(block, axis):
    stacked, slots = gather_blocks(block, axis)
    return jnp.take(stacked, slots, axis=0)


def scatter_blocks(blocks, axis, pairs):
    count = lax.axis_size(axis)
    if count > 8:
        return lax.psum_scatter(blocks, axis, scatter_dimension=0, tiled=True)[0].astype(
            jnp.float32
        )
    index = lax.axis_index(axis)

    def pick(i):
        return lax.dynamic_index_in_dim(blocks, i, 0, keepdims=False)

    if pairs and count == 4:
        partner = [(i, i ^ 1) for i in range(count)]
        got = lax.ppermute(jnp.stack([pick(index ^ 1), pick(index ^ 3)]), axis, partner)
        theirs = (pick(index ^ 2).astype(jnp.float32) + got[1].astype(jnp.float32)).astype(
            blocks.dtype
        )
        back = lax.ppermute(theirs, axis, [(i, i ^ 2) for i in range(count)])
        return (
            pick(index).astype(jnp.float32)
            + got[0].astype(jnp.float32)
            + back.astype(jnp.float32)
        )
    total = pick(index).astype(jnp.float32)
    for d in range(1, count):
        part = lax.dynamic_index_in_dim(blocks, (index + d) % count, 0, keepdims=False)
        total = total + lax.ppermute(
            part, axis, [(i, (i + d) % count) for i in range(count)]
        ).astype(jnp.float32)
    return total


def per_device(
    image_tokens,
    keyval_weight,
    query_gain,
    key_norm_gain,
    gate_logit,
    text_queries,
    text_document,
    image_document,
    cotangent,
):
    section_count = lax.axis_size("section")
    section_index = lax.axis_index("section")
    micro_count = text_queries.shape[0]
    head_count = gate_logit.shape[1]
    key_width = key_norm_gain.shape[1]
    head_dim = query_gain.shape[1] // head_count
    keyval_heads = key_width // head_dim
    weights = keyval_weight[0]

    layer_params, layer_slots = gather_blocks(
        jnp.concatenate([query_gain, gate_logit], axis=1)[0], "section"
    )
    gains_all = layer_params[:, : query_gain.shape[1]]
    gates_all = layer_params[:, query_gain.shape[1] :]

    shard_count = lax.axis_size("shard")
    owned = image_tokens.shape[1]
    image_count = owned * section_count
    total_rows = micro_count * image_count
    pair_width = 2 * key_width
    phased = section_count == 4 and shard_count == 2 * micro_count
    if phased:
        images, _ = gather_blocks(image_tokens, "section")
        raw_parts = []
        for phase in range(2):
            block = images[2 * phase : 2 * phase + 2].transpose(1, 0, 2, 3)
            block = block.reshape(-1, image_tokens.shape[2])
            partial = jnp.dot(block, weights, preferred_element_type=jnp.float32)
            raw_parts.append(
                scatter_blocks(partial.reshape(shard_count, owned, pair_width), "shard", False)
            )
        raw_rows = jnp.stack(raw_parts)
        sections = jnp.arange(section_count, dtype=jnp.int32)
        distance = lax.bitwise_xor(section_index, sections)
        micro_ids = jnp.arange(micro_count, dtype=jnp.int32)
        natural = (2 * micro_ids[:, None] + distance[None, :] % 2) * 2 + distance[None, :] // 2
        owners = jnp.arange(shard_count, dtype=jnp.int32)[:, None]
        phases = jnp.arange(2, dtype=jnp.int32)[None, :]
        held = (owners // 2) * section_count + lax.bitwise_xor(
            section_index, 2 * phases + owners % 2
        )

        def to_natural(rows):
            blocks = in_order(rows.reshape(2, owned, pair_width), "shard")
            return jnp.take(
                blocks.reshape(2 * shard_count, owned, pair_width), natural.reshape(-1), axis=0
            ).reshape(total_rows, pair_width)

        def to_owned(rows):
            return jnp.take(
                rows.reshape(micro_count * section_count, owned, pair_width),
                held.reshape(-1),
                axis=0,
            ).reshape(shard_count, 2 * owned, pair_width)

    else:
        gathered = in_order(image_tokens, "section")
        gathered = gathered.transpose(1, 0, 2, 3).reshape(total_rows, image_tokens.shape[2])
        partial = jnp.dot(gathered, weights, preferred_element_type=jnp.float32)
        raw_rows = scatter_blocks(
            partial.reshape(shard_count, total_rows // shard_count, pair_width), "shard", False
        )

        def to_natural(rows):
            return in_order(rows, "shard").reshape(total_rows, pair_width)

        def to_owned(rows):
            return rows.reshape(shard_count, total_rows // shard_count, pair_width)

    raw_rows = raw_rows.reshape(-1, pair_width)
    key_rows = head_normalize(raw_rows[:, :key_width], key_norm_gain[0], keyval_heads)
    keyval_rows = jnp.concatenate(
        [key_rows.astype(jnp.bfloat16), raw_rows[:, key_width:].astype(jnp.bfloat16)], axis=1
    )
    keyval_own = to_natural(keyval_rows)
    keyval_all, _ = gather_blocks(keyval_own, "section")

    same_document = text_document[:, :, None] == image_document[:, None, :]
    leaving, grad_local = attention_layers(
        section_index,
        layer_slots,
        jnp.tanh(gates_all),
        text_queries,
        keyval_all.reshape(section_count, micro_count, image_count, 2 * key_width),
        gains_all,
        same_document,
        cotangent[0],
    )
    grad_rows = scatter_blocks(to_owned(grad_local), "shard", False).reshape(-1, pair_width)
    key_portion = norm_gradient(
        raw_rows[:, :key_width], key_norm_gain[0], grad_rows[:, :key_width], keyval_heads
    )
    raw_grad_rows = jnp.concatenate([key_portion, grad_rows[:, key_width:]], axis=1).astype(
        jnp.bfloat16
    )
    owned = image_count // section_count
    if phased:
        raw_blocks = in_order(raw_grad_rows.reshape(2, owned, pair_width), "shard")
        raw_grad = jnp.take(
            raw_blocks.reshape(2 * shard_count, owned, pair_width),
            natural.T.reshape(-1),
            axis=0,
        ).reshape(total_rows, pair_width)
    else:
        raw_grad = to_natural(raw_grad_rows)
        raw_grad = (
            raw_grad.reshape(micro_count, section_count, owned, 2 * key_width)
            .transpose(1, 0, 2, 3)
            .reshape(total_rows, 2 * key_width)
        )
    image_part = lax.dot_general(
        raw_grad, weights, (((1,), (1,)), ((), ())), preferred_element_type=jnp.float32
    )
    image_part = image_part.astype(jnp.bfloat16).reshape(
        section_count, micro_count, owned, weights.shape[0]
    )
    image_grad = scatter_blocks(image_part, "section", True)
    return (leaving[None], image_grad)


def solution(mesh):
    placed = (
        P("group", "section", "shard"),
        P("section", "shard", None),
        P("section", None),
        P("section", None),
        P("section", None),
        P("group", "shard", None),
        P("group", "shard"),
        P("group", None),
        P("section", "group", "shard", None),
    )
    return jax.shard_map(
        per_device,
        mesh=mesh,
        in_specs=placed,
        out_specs=(P("section", "group", "shard", None), P("group", "section", "shard")),
        check_vma=False,
    )
```

```python
import functools
import math

import jax
import jax.numpy as jnp
from jax import lax
from jax.experimental import pallas as pl
from jax.experimental.pallas import tpu as pltpu
from jax.sharding import PartitionSpec as P

epsilon = 1e-05


def head_normalize(input_rows, gain_row, head_count):
    shaped = input_rows.reshape(input_rows.shape[:-1] + (head_count, -1))
    factor = lax.rsqrt(jnp.mean(shaped * shaped, axis=-1, keepdims=True) + epsilon)
    gain = gain_row.reshape((1,) * (shaped.ndim - 2) + (head_count, -1))
    return (shaped * factor * gain).reshape(input_rows.shape)


def norm_gradient(input_rows, gain_row, incoming_gradient, head_count):
    shaped = input_rows.reshape(input_rows.shape[0], head_count, -1)
    scaled = incoming_gradient.reshape(input_rows.shape[0], head_count, -1) * gain_row.reshape(
        1, head_count, -1
    )
    factor = lax.rsqrt(jnp.mean(shaped * shaped, axis=-1, keepdims=True) + epsilon)
    inner_mean = jnp.mean(shaped * scaled, axis=-1, keepdims=True)
    result = factor * scaled - shaped * factor * factor * factor * inner_mean
    return result.reshape(input_rows.shape[0], -1)


def attention_kernel(
    section_ref,
    slots_ref,
    gates_ref,
    queries_ref,
    keyval_ref,
    gains_ref,
    mask_ref,
    mask_t_ref,
    cot_ref,
    out_ref,
    grad_ref,
    *,
    head_count,
    keyval_heads,
):
    token_count, query_width = out_ref.shape
    head_dim = query_width // head_count
    key_width = keyval_heads * head_dim
    groups = head_count // keyval_heads
    scale = 1.0 / math.sqrt(head_dim)
    section = section_ref[0]
    out_ref[...] = queries_ref[...].astype(jnp.float32)

    def head_cols(h):
        return pl.ds(h * head_dim, head_dim)

    def queries_of(slot, k):
        parts = []
        for g in range(groups):
            h = k * groups + g
            x = out_ref[:, head_cols(h)]
            mean_square = jnp.sum(x * x, axis=-1, keepdims=True) * (1.0 / head_dim)
            gain = gains_ref[slot, :, head_cols(h)]
            parts.append((x * lax.rsqrt(mean_square + epsilon) * gain).astype(jnp.bfloat16))
        return jnp.concatenate(parts, axis=0)

    def forward(layer):
        slot = slots_ref[layer]
        same = mask_ref[...] > 0.5
        for k in range(keyval_heads):
            query = queries_of(slot, k)
            key = keyval_ref[slot, :, head_cols(k)]
            value = keyval_ref[slot, :, pl.ds(key_width + k * head_dim, head_dim)]
            scores = lax.dot_general(
                query, key, (((1,), (1,)), ((), ())), preferred_element_type=jnp.float32
            ) * scale
            scores = jnp.where(same, scores, -jnp.inf)
            powered = jnp.exp(scores - jnp.max(scores, axis=-1, keepdims=True))
            probs = powered * (1.0 / jnp.sum(powered, axis=-1, keepdims=True))
            attended = jnp.dot(
                probs.astype(jnp.bfloat16), value, preferred_element_type=jnp.float32
            )
            for g in range(groups):
                h = k * groups + g
                rows = attended[g * token_count : (g + 1) * token_count]
                out_ref[:, head_cols(h)] = out_ref[:, head_cols(h)] + gates_ref[slot, h] * rows

    def layer_step(layer, carry):
        forward(layer)
        return carry

    lax.fori_loop(0, section, layer_step, 0)

    same_t = mask_t_ref[...] > 0.5
    own = slots_ref[section]
    for k in range(keyval_heads):
        query = queries_of(own, k)
        key = keyval_ref[own, :, head_cols(k)]
        value = keyval_ref[own, :, pl.ds(key_width + k * head_dim, head_dim)]
        scores_t = lax.dot_general(
            key, query, (((1,), (1,)), ((), ())), preferred_element_type=jnp.float32
        ) * scale
        scores_t = jnp.where(same_t, scores_t, -jnp.inf)
        powered = jnp.exp(scores_t - jnp.max(scores_t, axis=0, keepdims=True))
        probs_t = powered * (1.0 / jnp.sum(powered, axis=0, keepdims=True))
        upstream = jnp.concatenate(
            [cot_ref[:, head_cols(k * groups + g)] for g in range(groups)], axis=0
        )
        value_grad = jnp.dot(
            probs_t.astype(jnp.bfloat16), upstream, preferred_element_type=jnp.float32
        )
        prob_grad_t = lax.dot_general(
            value, upstream, (((1,), (1,)), ((), ())), preferred_element_type=jnp.float32
        )
        inner = jnp.sum(probs_t * prob_grad_t, axis=0, keepdims=True)
        score_grad_t = (probs_t * (prob_grad_t - inner)).astype(jnp.bfloat16)
        key_grad = jnp.dot(score_grad_t, query, preferred_element_type=jnp.float32) * scale
        grad_ref[:, head_cols(k)] = key_grad.astype(grad_ref.dtype)
        grad_ref[:, pl.ds(key_width + k * head_dim, head_dim)] = value_grad.astype(grad_ref.dtype)

    forward(section)


def attention_layers(
    section_index, layer_slots, gates, queries, keyval_all, gains, same_document, upstream
):
    layer_count, micro_count, image_count, pair_width = keyval_all.shape
    token_count, query_width = queries.shape[1], queries.shape[2]
    head_count = gates.shape[1]
    head_dim = query_width // head_count
    keyval_heads = pair_width // 2 // head_dim
    groups = head_count // keyval_heads
    mask = jnp.tile(same_document.astype(jnp.float32), (1, groups, 1))
    mask_t = jnp.swapaxes(mask, 1, 2)
    smem = pl.BlockSpec(memory_space=pltpu.SMEM)
    flops = 2 * micro_count * (layer_count + 3) * head_count * token_count * image_count * head_dim * 2
    return pl.pallas_call(
        functools.partial(attention_kernel, head_count=head_count, keyval_heads=keyval_heads),
        grid=(micro_count,),
        in_specs=[
            smem,
            smem,
            smem,
            pl.BlockSpec((None, token_count, query_width), lambda m: (m, 0, 0)),
            pl.BlockSpec((layer_count, None, image_count, pair_width), lambda m: (0, m, 0, 0)),
            pl.BlockSpec((layer_count, 1, query_width), lambda m: (0, 0, 0)),
            pl.BlockSpec((None, groups * token_count, image_count), lambda m: (m, 0, 0)),
            pl.BlockSpec((None, image_count, groups * token_count), lambda m: (m, 0, 0)),
            pl.BlockSpec((None, token_count, query_width), lambda m: (m, 0, 0)),
        ],
        out_specs=[
            pl.BlockSpec((None, token_count, query_width), lambda m: (m, 0, 0)),
            pl.BlockSpec((None, image_count, pair_width), lambda m: (m, 0, 0)),
        ],
        out_shape=[
            jax.ShapeDtypeStruct((micro_count, token_count, query_width), jnp.float32),
            jax.ShapeDtypeStruct((micro_count, image_count, pair_width), jnp.bfloat16),
        ],
        compiler_params=pltpu.CompilerParams(dimension_semantics=("arbitrary",)),
        cost_estimate=pl.CostEstimate(
            flops=flops,
            transcendentals=micro_count * (layer_count + 1) * head_count * token_count * image_count,
            bytes_accessed=keyval_all.size * 2 + queries.size * 8 + upstream.size * 2,
        ),
    )(
        jnp.reshape(section_index, (1,)).astype(jnp.int32),
        layer_slots.astype(jnp.int32),
        gates,
        queries,
        keyval_all,
        gains.reshape(layer_count, 1, query_width),
        mask,
        mask_t,
        upstream,
    )


def gather_blocks(block, axis, below_only=False):
    count = lax.axis_size(axis)
    index = lax.axis_index(axis)
    positions = jnp.arange(count, dtype=jnp.int32)
    if count > 8:
        return lax.all_gather(block, axis, axis=0, tiled=False), positions
    if count == 4:
        partner = [(i, i ^ 1) for i in range(count)]
        across_pairs = [(i, i ^ 2) for i in range(count)]
        forward = partner
        if below_only:
            partner = [(i, j) for i, j in partner if i < j]
            across_pairs = [(i, j) for i, j in across_pairs if i < j]
            forward = [(i, j) for i, j in forward if i ^ 2 < j]
        across = lax.ppermute(block, axis, across_pairs)
        received = [block, lax.ppermute(block, axis, partner), across, lax.ppermute(across, axis, forward)]
        return jnp.stack(received), lax.bitwise_xor(index, positions)
    received = [block] + [
        lax.ppermute(block, axis, [(i, (i + d) % count) for i in range(count)])
        for d in range(1, count)
    ]
    return jnp.stack(received), (index - positions) % count


def in_order(block, axis):
    stacked, slots = gather_blocks(block, axis)
    return jnp.take(stacked, slots, axis=0)


def scatter_blocks(blocks, axis, pairs):
    count = lax.axis_size(axis)
    if count > 8:
        return lax.psum_scatter(blocks, axis, scatter_dimension=0, tiled=True)[0].astype(
            jnp.float32
        )
    index = lax.axis_index(axis)

    def pick(i):
        return lax.dynamic_index_in_dim(blocks, i, 0, keepdims=False)

    if pairs and count == 4:
        partner = [(i, i ^ 1) for i in range(count)]
        got = lax.ppermute(jnp.stack([pick(index ^ 1), pick(index ^ 3)]), axis, partner)
        theirs = (pick(index ^ 2).astype(jnp.float32) + got[1].astype(jnp.float32)).astype(
            blocks.dtype
        )
        back = lax.ppermute(theirs, axis, [(i, i ^ 2) for i in range(count)])
        return (
            pick(index).astype(jnp.float32)
            + got[0].astype(jnp.float32)
            + back.astype(jnp.float32)
        )
    total = pick(index).astype(jnp.float32)
    for d in range(1, count):
        part = lax.dynamic_index_in_dim(blocks, (index + d) % count, 0, keepdims=False)
        total = total + lax.ppermute(
            part, axis, [(i, (i + d) % count) for i in range(count)]
        ).astype(jnp.float32)
    return total


def per_device(
    image_tokens,
    keyval_weight,
    query_gain,
    key_norm_gain,
    gate_logit,
    text_queries,
    text_document,
    image_document,
    cotangent,
):
    section_count = lax.axis_size("section")
    section_index = lax.axis_index("section")
    micro_count = text_queries.shape[0]
    head_count = gate_logit.shape[1]
    key_width = key_norm_gain.shape[1]
    head_dim = query_gain.shape[1] // head_count
    keyval_heads = key_width // head_dim
    weights = keyval_weight[0]

    layer_params, layer_slots = gather_blocks(
        jnp.concatenate([query_gain, gate_logit], axis=1)[0], "section", True
    )
    gains_all = layer_params[:, : query_gain.shape[1]]
    gates_all = layer_params[:, query_gain.shape[1] :]

    shard_count = lax.axis_size("shard")
    owned = image_tokens.shape[1]
    image_count = owned * section_count
    total_rows = micro_count * image_count
    pair_width = 2 * key_width
    phased = section_count == 4 and shard_count == 2 * micro_count
    if phased:
        images, _ = gather_blocks(image_tokens, "section")
        raw_parts = []
        for phase in range(2):
            block = images[2 * phase : 2 * phase + 2].transpose(1, 0, 2, 3)
            block = block.reshape(-1, image_tokens.shape[2])
            partial = jnp.dot(block, weights, preferred_element_type=jnp.float32)
            raw_parts.append(
                scatter_blocks(partial.reshape(shard_count, owned, pair_width), "shard", False)
            )
        raw_rows = jnp.stack(raw_parts)
        sections = jnp.arange(section_count, dtype=jnp.int32)
        distance = lax.bitwise_xor(section_index, sections)
        micro_ids = jnp.arange(micro_count, dtype=jnp.int32)
        natural = (2 * micro_ids[:, None] + distance[None, :] % 2) * 2 + distance[None, :] // 2
        owners = jnp.arange(shard_count, dtype=jnp.int32)[:, None]
        phases = jnp.arange(2, dtype=jnp.int32)[None, :]
        held = (owners // 2) * section_count + lax.bitwise_xor(
            section_index, 2 * phases + owners % 2
        )

        def to_natural(rows):
            blocks = in_order(rows.reshape(2, owned, pair_width), "shard")
            return jnp.take(
                blocks.reshape(2 * shard_count, owned, pair_width), natural.reshape(-1), axis=0
            ).reshape(total_rows, pair_width)

        def to_owned(rows):
            return jnp.take(
                rows.reshape(micro_count * section_count, owned, pair_width),
                held.reshape(-1),
                axis=0,
            ).reshape(shard_count, 2 * owned, pair_width)

    else:
        gathered = in_order(image_tokens, "section")
        gathered = gathered.transpose(1, 0, 2, 3).reshape(total_rows, image_tokens.shape[2])
        partial = jnp.dot(gathered, weights, preferred_element_type=jnp.float32)
        raw_rows = scatter_blocks(
            partial.reshape(shard_count, total_rows // shard_count, pair_width), "shard", False
        )

        def to_natural(rows):
            return in_order(rows, "shard").reshape(total_rows, pair_width)

        def to_owned(rows):
            return rows.reshape(shard_count, total_rows // shard_count, pair_width)

    raw_rows = raw_rows.reshape(-1, pair_width)
    key_rows = head_normalize(raw_rows[:, :key_width], key_norm_gain[0], keyval_heads)
    keyval_rows = jnp.concatenate(
        [key_rows.astype(jnp.bfloat16), raw_rows[:, key_width:].astype(jnp.bfloat16)], axis=1
    )
    keyval_own = to_natural(keyval_rows)
    keyval_all, _ = gather_blocks(keyval_own, "section", True)

    same_document = text_document[:, :, None] == image_document[:, None, :]
    leaving, grad_local = attention_layers(
        section_index,
        layer_slots,
        jnp.tanh(gates_all),
        text_queries,
        keyval_all.reshape(section_count, micro_count, image_count, 2 * key_width),
        gains_all,
        same_document,
        cotangent[0],
    )
    grad_rows = scatter_blocks(to_owned(grad_local), "shard", False).reshape(-1, pair_width)
    key_portion = norm_gradient(
        raw_rows[:, :key_width], key_norm_gain[0], grad_rows[:, :key_width], keyval_heads
    )
    raw_grad_rows = jnp.concatenate([key_portion, grad_rows[:, key_width:]], axis=1).astype(
        jnp.bfloat16
    )
    raw_grad = to_natural(raw_grad_rows)
    owned = image_count // section_count
    raw_grad = (
        raw_grad.reshape(micro_count, section_count, owned, 2 * key_width)
        .transpose(1, 0, 2, 3)
        .reshape(total_rows, 2 * key_width)
    )
    image_part = lax.dot_general(
        raw_grad, weights, (((1,), (1,)), ((), ())), preferred_element_type=jnp.float32
    )
    image_part = image_part.astype(jnp.bfloat16).reshape(
        section_count, micro_count, owned, weights.shape[0]
    )
    image_grad = scatter_blocks(image_part, "section", True)
    return (leaving[None], image_grad)


def solution(mesh):
    placed = (
        P("group", "section", "shard"),
        P("section", "shard", None),
        P("section", None),
        P("section", None),
        P("section", None),
        P("group", "shard", None),
        P("group", "shard"),
        P("group", None),
        P("section", "group", "shard", None),
    )
    return jax.shard_map(
        per_device,
        mesh=mesh,
        in_specs=placed,
        out_specs=(P("section", "group", "shard", None), P("group", "section", "shard")),
        check_vma=False,
    )
```

```python
import functools
import math

import jax
import jax.numpy as jnp
from jax import lax
from jax.experimental import pallas as pl
from jax.experimental.pallas import tpu as pltpu
from jax.sharding import PartitionSpec as P

epsilon = 1e-05


def head_normalize(input_rows, gain_row, head_count):
    shaped = input_rows.reshape(input_rows.shape[:-1] + (head_count, -1))
    factor = lax.rsqrt(jnp.mean(shaped * shaped, axis=-1, keepdims=True) + epsilon)
    gain = gain_row.reshape((1,) * (shaped.ndim - 2) + (head_count, -1))
    return (shaped * factor * gain).reshape(input_rows.shape)


def norm_gradient(input_rows, gain_row, incoming_gradient, head_count):
    shaped = input_rows.reshape(input_rows.shape[0], head_count, -1)
    scaled = incoming_gradient.reshape(input_rows.shape[0], head_count, -1) * gain_row.reshape(
        1, head_count, -1
    )
    factor = lax.rsqrt(jnp.mean(shaped * shaped, axis=-1, keepdims=True) + epsilon)
    inner_mean = jnp.mean(shaped * scaled, axis=-1, keepdims=True)
    result = factor * scaled - shaped * factor * factor * factor * inner_mean
    return result.reshape(input_rows.shape[0], -1)


def attention_kernel(
    section_ref,
    slots_ref,
    gates_ref,
    queries_ref,
    keyval_ref,
    gains_ref,
    mask_ref,
    mask_t_ref,
    cot_ref,
    out_ref,
    grad_ref,
    query_scratch,
    *,
    head_count,
    keyval_heads,
):
    token_count, query_width = out_ref.shape
    head_dim = query_width // head_count
    key_width = keyval_heads * head_dim
    groups = head_count // keyval_heads
    scale = 1.0 / math.sqrt(head_dim)
    section = section_ref[0]
    out_ref[...] = queries_ref[...].astype(jnp.float32)

    def head_cols(h):
        return pl.ds(h * head_dim, head_dim)

    def queries_of(slot, k):
        parts = []
        for g in range(groups):
            h = k * groups + g
            x = out_ref[:, head_cols(h)]
            mean_square = jnp.sum(x * x, axis=-1, keepdims=True) * (1.0 / head_dim)
            gain = gains_ref[slot, :, head_cols(h)]
            parts.append((x * lax.rsqrt(mean_square + epsilon) * gain).astype(jnp.bfloat16))
        return jnp.concatenate(parts, axis=0)

    def forward(layer, saved=False):
        slot = slots_ref[layer]
        same = mask_ref[...] > 0.5
        for k in range(keyval_heads):
            query = query_scratch[k] if saved else queries_of(slot, k)
            key = keyval_ref[slot, :, head_cols(k)]
            value = keyval_ref[slot, :, pl.ds(key_width + k * head_dim, head_dim)]
            scores = lax.dot_general(
                query, key, (((1,), (1,)), ((), ())), preferred_element_type=jnp.float32
            ) * scale
            scores = jnp.where(same, scores, -jnp.inf)
            powered = jnp.exp(scores - jnp.max(scores, axis=-1, keepdims=True))
            probs = powered * (1.0 / jnp.sum(powered, axis=-1, keepdims=True))
            attended = jnp.dot(
                probs.astype(jnp.bfloat16), value, preferred_element_type=jnp.float32
            )
            for g in range(groups):
                h = k * groups + g
                rows = attended[g * token_count : (g + 1) * token_count]
                out_ref[:, head_cols(h)] = out_ref[:, head_cols(h)] + gates_ref[slot, h] * rows

    def layer_step(layer, carry):
        forward(layer)
        return carry

    lax.fori_loop(0, section, layer_step, 0)

    same_t = mask_t_ref[...] > 0.5
    own = slots_ref[section]
    for k in range(keyval_heads):
        query = queries_of(own, k)
        query_scratch[k] = query
        key = keyval_ref[own, :, head_cols(k)]
        value = keyval_ref[own, :, pl.ds(key_width + k * head_dim, head_dim)]
        scores_t = lax.dot_general(
            key, query, (((1,), (1,)), ((), ())), preferred_element_type=jnp.float32
        ) * scale
        scores_t = jnp.where(same_t, scores_t, -jnp.inf)
        powered = jnp.exp(scores_t - jnp.max(scores_t, axis=0, keepdims=True))
        probs_t = powered * (1.0 / jnp.sum(powered, axis=0, keepdims=True))
        upstream = jnp.concatenate(
            [cot_ref[:, head_cols(k * groups + g)] for g in range(groups)], axis=0
        )
        value_grad = jnp.dot(
            probs_t.astype(jnp.bfloat16), upstream, preferred_element_type=jnp.float32
        )
        prob_grad_t = lax.dot_general(
            value, upstream, (((1,), (1,)), ((), ())), preferred_element_type=jnp.float32
        )
        inner = jnp.sum(probs_t * prob_grad_t, axis=0, keepdims=True)
        score_grad_t = (probs_t * (prob_grad_t - inner)).astype(jnp.bfloat16)
        key_grad = jnp.dot(score_grad_t, query, preferred_element_type=jnp.float32) * scale
        grad_ref[:, head_cols(k)] = key_grad.astype(grad_ref.dtype)
        grad_ref[:, pl.ds(key_width + k * head_dim, head_dim)] = value_grad.astype(grad_ref.dtype)

    forward(section, saved=True)


def attention_layers(
    section_index, layer_slots, gates, queries, keyval_all, gains, same_document, upstream
):
    layer_count, micro_count, image_count, pair_width = keyval_all.shape
    token_count, query_width = queries.shape[1], queries.shape[2]
    head_count = gates.shape[1]
    head_dim = query_width // head_count
    keyval_heads = pair_width // 2 // head_dim
    groups = head_count // keyval_heads
    mask = jnp.tile(same_document.astype(jnp.float32), (1, groups, 1))
    mask_t = jnp.swapaxes(mask, 1, 2)
    smem = pl.BlockSpec(memory_space=pltpu.SMEM)
    flops = 2 * micro_count * (layer_count + 3) * head_count * token_count * image_count * head_dim * 2
    return pl.pallas_call(
        functools.partial(attention_kernel, head_count=head_count, keyval_heads=keyval_heads),
        grid=(micro_count,),
        in_specs=[
            smem,
            smem,
            smem,
            pl.BlockSpec((None, token_count, query_width), lambda m: (m, 0, 0)),
            pl.BlockSpec((layer_count, None, image_count, pair_width), lambda m: (0, m, 0, 0)),
            pl.BlockSpec((layer_count, 1, query_width), lambda m: (0, 0, 0)),
            pl.BlockSpec((None, groups * token_count, image_count), lambda m: (m, 0, 0)),
            pl.BlockSpec((None, image_count, groups * token_count), lambda m: (m, 0, 0)),
            pl.BlockSpec((None, token_count, query_width), lambda m: (m, 0, 0)),
        ],
        out_specs=[
            pl.BlockSpec((None, token_count, query_width), lambda m: (m, 0, 0)),
            pl.BlockSpec((None, image_count, pair_width), lambda m: (m, 0, 0)),
        ],
        out_shape=[
            jax.ShapeDtypeStruct((micro_count, token_count, query_width), jnp.float32),
            jax.ShapeDtypeStruct((micro_count, image_count, pair_width), jnp.bfloat16),
        ],
        scratch_shapes=[
            pltpu.VMEM((keyval_heads, groups * token_count, head_dim), jnp.bfloat16)
        ],
        compiler_params=pltpu.CompilerParams(dimension_semantics=("arbitrary",)),
        cost_estimate=pl.CostEstimate(
            flops=flops,
            transcendentals=micro_count * (layer_count + 1) * head_count * token_count * image_count,
            bytes_accessed=keyval_all.size * 2 + queries.size * 8 + upstream.size * 2,
        ),
    )(
        jnp.reshape(section_index, (1,)).astype(jnp.int32),
        layer_slots.astype(jnp.int32),
        gates,
        queries,
        keyval_all,
        gains.reshape(layer_count, 1, query_width),
        mask,
        mask_t,
        upstream,
    )


def gather_blocks(block, axis):
    count = lax.axis_size(axis)
    index = lax.axis_index(axis)
    positions = jnp.arange(count, dtype=jnp.int32)
    if count > 8:
        return lax.all_gather(block, axis, axis=0, tiled=False), positions
    if count == 4:
        partner = [(i, i ^ 1) for i in range(count)]
        across = lax.ppermute(block, axis, [(i, i ^ 2) for i in range(count)])
        received = [block, lax.ppermute(block, axis, partner), across, lax.ppermute(across, axis, partner)]
        return jnp.stack(received), lax.bitwise_xor(index, positions)
    received = [block] + [
        lax.ppermute(block, axis, [(i, (i + d) % count) for i in range(count)])
        for d in range(1, count)
    ]
    return jnp.stack(received), (index - positions) % count


def in_order(block, axis):
    stacked, slots = gather_blocks(block, axis)
    return jnp.take(stacked, slots, axis=0)


def scatter_blocks(blocks, axis, pairs):
    count = lax.axis_size(axis)
    if count > 8:
        return lax.psum_scatter(blocks, axis, scatter_dimension=0, tiled=True)[0].astype(
            jnp.float32
        )
    index = lax.axis_index(axis)

    def pick(i):
        return lax.dynamic_index_in_dim(blocks, i, 0, keepdims=False)

    if pairs and count == 4:
        partner = [(i, i ^ 1) for i in range(count)]
        got = lax.ppermute(jnp.stack([pick(index ^ 1), pick(index ^ 3)]), axis, partner)
        theirs = (pick(index ^ 2).astype(jnp.float32) + got[1].astype(jnp.float32)).astype(
            blocks.dtype
        )
        back = lax.ppermute(theirs, axis, [(i, i ^ 2) for i in range(count)])
        return (
            pick(index).astype(jnp.float32)
            + got[0].astype(jnp.float32)
            + back.astype(jnp.float32)
        )
    total = pick(index).astype(jnp.float32)
    for d in range(1, count):
        part = lax.dynamic_index_in_dim(blocks, (index + d) % count, 0, keepdims=False)
        total = total + lax.ppermute(
            part, axis, [(i, (i + d) % count) for i in range(count)]
        ).astype(jnp.float32)
    return total


def per_device(
    image_tokens,
    keyval_weight,
    query_gain,
    key_norm_gain,
    gate_logit,
    text_queries,
    text_document,
    image_document,
    cotangent,
):
    section_count = lax.axis_size("section")
    section_index = lax.axis_index("section")
    micro_count = text_queries.shape[0]
    head_count = gate_logit.shape[1]
    key_width = key_norm_gain.shape[1]
    head_dim = query_gain.shape[1] // head_count
    keyval_heads = key_width // head_dim
    weights = keyval_weight[0]

    layer_params, layer_slots = gather_blocks(
        jnp.concatenate([query_gain, gate_logit], axis=1)[0], "section"
    )
    gains_all = layer_params[:, : query_gain.shape[1]]
    gates_all = layer_params[:, query_gain.shape[1] :]

    shard_count = lax.axis_size("shard")
    owned = image_tokens.shape[1]
    image_count = owned * section_count
    total_rows = micro_count * image_count
    pair_width = 2 * key_width
    phased = section_count == 4 and shard_count == 2 * micro_count
    if phased:
        images, _ = gather_blocks(image_tokens, "section")
        raw_parts = []
        for phase in range(2):
            block = images[2 * phase : 2 * phase + 2].transpose(1, 0, 2, 3)
            block = block.reshape(-1, image_tokens.shape[2])
            partial = jnp.dot(block, weights, preferred_element_type=jnp.float32)
            raw_parts.append(
                scatter_blocks(partial.reshape(shard_count, owned, pair_width), "shard", False)
            )
        raw_rows = jnp.stack(raw_parts)
        sections = jnp.arange(section_count, dtype=jnp.int32)
        distance = lax.bitwise_xor(section_index, sections)
        micro_ids = jnp.arange(micro_count, dtype=jnp.int32)
        natural = (2 * micro_ids[:, None] + distance[None, :] % 2) * 2 + distance[None, :] // 2
        owners = jnp.arange(shard_count, dtype=jnp.int32)[:, None]
        phases = jnp.arange(2, dtype=jnp.int32)[None, :]
        held = (owners // 2) * section_count + lax.bitwise_xor(
            section_index, 2 * phases + owners % 2
        )

        def to_natural(rows):
            blocks = in_order(rows.reshape(2, owned, pair_width), "shard")
            return jnp.take(
                blocks.reshape(2 * shard_count, owned, pair_width), natural.reshape(-1), axis=0
            ).reshape(total_rows, pair_width)

        def to_owned(rows):
            return jnp.take(
                rows.reshape(micro_count * section_count, owned, pair_width),
                held.reshape(-1),
                axis=0,
            ).reshape(shard_count, 2 * owned, pair_width)

    else:
        gathered = in_order(image_tokens, "section")
        gathered = gathered.transpose(1, 0, 2, 3).reshape(total_rows, image_tokens.shape[2])
        partial = jnp.dot(gathered, weights, preferred_element_type=jnp.float32)
        raw_rows = scatter_blocks(
            partial.reshape(shard_count, total_rows // shard_count, pair_width), "shard", False
        )

        def to_natural(rows):
            return in_order(rows, "shard").reshape(total_rows, pair_width)

        def to_owned(rows):
            return rows.reshape(shard_count, total_rows // shard_count, pair_width)

    raw_rows = raw_rows.reshape(-1, pair_width)
    key_rows = head_normalize(raw_rows[:, :key_width], key_norm_gain[0], keyval_heads)
    keyval_rows = jnp.concatenate(
        [key_rows.astype(jnp.bfloat16), raw_rows[:, key_width:].astype(jnp.bfloat16)], axis=1
    )
    keyval_own = to_natural(keyval_rows)
    keyval_all, _ = gather_blocks(keyval_own, "section")

    same_document = text_document[:, :, None] == image_document[:, None, :]
    leaving, grad_local = attention_layers(
        section_index,
        layer_slots,
        jnp.tanh(gates_all),
        text_queries,
        keyval_all.reshape(section_count, micro_count, image_count, 2 * key_width),
        gains_all,
        same_document,
        cotangent[0],
    )
    grad_rows = scatter_blocks(to_owned(grad_local), "shard", False).reshape(-1, pair_width)
    key_portion = norm_gradient(
        raw_rows[:, :key_width], key_norm_gain[0], grad_rows[:, :key_width], keyval_heads
    )
    raw_grad_rows = jnp.concatenate([key_portion, grad_rows[:, key_width:]], axis=1).astype(
        jnp.bfloat16
    )
    raw_grad = to_natural(raw_grad_rows)
    owned = image_count // section_count
    raw_grad = (
        raw_grad.reshape(micro_count, section_count, owned, 2 * key_width)
        .transpose(1, 0, 2, 3)
        .reshape(total_rows, 2 * key_width)
    )
    image_part = lax.dot_general(
        raw_grad, weights, (((1,), (1,)), ((), ())), preferred_element_type=jnp.float32
    )
    image_part = image_part.astype(jnp.bfloat16).reshape(
        section_count, micro_count, owned, weights.shape[0]
    )
    image_grad = scatter_blocks(image_part, "section", True)
    return (leaving[None], image_grad)


def solution(mesh):
    placed = (
        P("group", "section", "shard"),
        P("section", "shard", None),
        P("section", None),
        P("section", None),
        P("section", None),
        P("group", "shard", None),
        P("group", "shard"),
        P("group", None),
        P("section", "group", "shard", None),
    )
    return jax.shard_map(
        per_device,
        mesh=mesh,
        in_specs=placed,
        out_specs=(P("section", "group", "shard", None), P("group", "section", "shard")),
        check_vma=False,
    )
```

```python
import functools
import math

import jax
import jax.numpy as jnp
from jax import lax
from jax.experimental import pallas as pl
from jax.experimental.pallas import tpu as pltpu
from jax.sharding import PartitionSpec as P

epsilon = 1e-05


def head_normalize(input_rows, gain_row, head_count):
    shaped = input_rows.reshape(input_rows.shape[:-1] + (head_count, -1))
    factor = lax.rsqrt(jnp.mean(shaped * shaped, axis=-1, keepdims=True) + epsilon)
    gain = gain_row.reshape((1,) * (shaped.ndim - 2) + (head_count, -1))
    return (shaped * factor * gain).reshape(input_rows.shape)


def norm_gradient(input_rows, gain_row, incoming_gradient, head_count):
    shaped = input_rows.reshape(input_rows.shape[0], head_count, -1)
    scaled = incoming_gradient.reshape(input_rows.shape[0], head_count, -1) * gain_row.reshape(
        1, head_count, -1
    )
    factor = lax.rsqrt(jnp.mean(shaped * shaped, axis=-1, keepdims=True) + epsilon)
    inner_mean = jnp.mean(shaped * scaled, axis=-1, keepdims=True)
    result = factor * scaled - shaped * factor * factor * factor * inner_mean
    return result.reshape(input_rows.shape[0], -1)


def attention_kernel(
    section_ref,
    slots_ref,
    gates_ref,
    queries_ref,
    keyval_ref,
    gains_ref,
    mask_ref,
    mask_t_ref,
    cot_ref,
    out_ref,
    grad_ref,
    *,
    head_count,
    keyval_heads,
):
    token_count, query_width = out_ref.shape
    head_dim = query_width // head_count
    key_width = keyval_heads * head_dim
    groups = head_count // keyval_heads
    scale = 1.0 / math.sqrt(head_dim)
    section = section_ref[0]
    out_ref[...] = queries_ref[...].astype(jnp.float32)

    def head_cols(h):
        return pl.ds(h * head_dim, head_dim)

    def queries_of(slot, k):
        parts = []
        for g in range(groups):
            h = k * groups + g
            x = out_ref[:, head_cols(h)]
            mean_square = jnp.sum(x * x, axis=-1, keepdims=True) * (1.0 / head_dim)
            gain = gains_ref[slot, :, head_cols(h)]
            parts.append((x * lax.rsqrt(mean_square + epsilon) * gain).astype(jnp.bfloat16))
        return jnp.concatenate(parts, axis=0)

    def forward(layer):
        slot = slots_ref[layer]
        bias = mask_ref[...]
        for k in range(keyval_heads):
            query = queries_of(slot, k)
            key = keyval_ref[slot, :, head_cols(k)]
            value = keyval_ref[slot, :, pl.ds(key_width + k * head_dim, head_dim)]
            scores = lax.dot_general(
                query, key, (((1,), (1,)), ((), ())), preferred_element_type=jnp.float32
            ) * scale + bias
            powered = jnp.exp(scores - jnp.max(scores, axis=-1, keepdims=True))
            probs = powered * (1.0 / jnp.sum(powered, axis=-1, keepdims=True))
            attended = jnp.dot(
                probs.astype(jnp.bfloat16), value, preferred_element_type=jnp.float32
            )
            for g in range(groups):
                h = k * groups + g
                rows = attended[g * token_count : (g + 1) * token_count]
                out_ref[:, head_cols(h)] = out_ref[:, head_cols(h)] + gates_ref[slot, h] * rows

    def layer_step(layer, carry):
        forward(layer)
        return carry

    lax.fori_loop(0, section, layer_step, 0)

    bias_t = mask_t_ref[...]
    own = slots_ref[section]
    for k in range(keyval_heads):
        query = queries_of(own, k)
        key = keyval_ref[own, :, head_cols(k)]
        value = keyval_ref[own, :, pl.ds(key_width + k * head_dim, head_dim)]
        scores_t = lax.dot_general(
            key, query, (((1,), (1,)), ((), ())), preferred_element_type=jnp.float32
        ) * scale + bias_t
        powered = jnp.exp(scores_t - jnp.max(scores_t, axis=0, keepdims=True))
        probs_t = powered * (1.0 / jnp.sum(powered, axis=0, keepdims=True))
        upstream = jnp.concatenate(
            [cot_ref[:, head_cols(k * groups + g)] for g in range(groups)], axis=0
        )
        value_grad = jnp.dot(
            probs_t.astype(jnp.bfloat16), upstream, preferred_element_type=jnp.float32
        )
        prob_grad_t = lax.dot_general(
            value, upstream, (((1,), (1,)), ((), ())), preferred_element_type=jnp.float32
        )
        inner = jnp.sum(probs_t * prob_grad_t, axis=0, keepdims=True)
        score_grad_t = (probs_t * (prob_grad_t - inner)).astype(jnp.bfloat16)
        key_grad = jnp.dot(score_grad_t, query, preferred_element_type=jnp.float32) * scale
        grad_ref[:, head_cols(k)] = key_grad.astype(grad_ref.dtype)
        grad_ref[:, pl.ds(key_width + k * head_dim, head_dim)] = value_grad.astype(grad_ref.dtype)

    forward(section)


def attention_layers(
    section_index, layer_slots, gates, queries, keyval_all, gains, same_document, upstream
):
    layer_count, micro_count, image_count, pair_width = keyval_all.shape
    token_count, query_width = queries.shape[1], queries.shape[2]
    head_count = gates.shape[1]
    head_dim = query_width // head_count
    keyval_heads = pair_width // 2 // head_dim
    groups = head_count // keyval_heads
    bias = jnp.where(same_document, 0.0, -jnp.inf).astype(jnp.float32)
    mask = jnp.tile(bias, (1, groups, 1))
    mask_t = jnp.swapaxes(mask, 1, 2)
    smem = pl.BlockSpec(memory_space=pltpu.SMEM)
    flops = 2 * micro_count * (layer_count + 3) * head_count * token_count * image_count * head_dim * 2
    return pl.pallas_call(
        functools.partial(attention_kernel, head_count=head_count, keyval_heads=keyval_heads),
        grid=(micro_count,),
        in_specs=[
            smem,
            smem,
            smem,
            pl.BlockSpec((None, token_count, query_width), lambda m: (m, 0, 0)),
            pl.BlockSpec((layer_count, None, image_count, pair_width), lambda m: (0, m, 0, 0)),
            pl.BlockSpec((layer_count, 1, query_width), lambda m: (0, 0, 0)),
            pl.BlockSpec((None, groups * token_count, image_count), lambda m: (m, 0, 0)),
            pl.BlockSpec((None, image_count, groups * token_count), lambda m: (m, 0, 0)),
            pl.BlockSpec((None, token_count, query_width), lambda m: (m, 0, 0)),
        ],
        out_specs=[
            pl.BlockSpec((None, token_count, query_width), lambda m: (m, 0, 0)),
            pl.BlockSpec((None, image_count, pair_width), lambda m: (m, 0, 0)),
        ],
        out_shape=[
            jax.ShapeDtypeStruct((micro_count, token_count, query_width), jnp.float32),
            jax.ShapeDtypeStruct((micro_count, image_count, pair_width), jnp.bfloat16),
        ],
        compiler_params=pltpu.CompilerParams(dimension_semantics=("arbitrary",)),
        cost_estimate=pl.CostEstimate(
            flops=flops,
            transcendentals=micro_count * (layer_count + 1) * head_count * token_count * image_count,
            bytes_accessed=keyval_all.size * 2 + queries.size * 8 + upstream.size * 2,
        ),
    )(
        jnp.reshape(section_index, (1,)).astype(jnp.int32),
        layer_slots.astype(jnp.int32),
        gates,
        queries,
        keyval_all,
        gains.reshape(layer_count, 1, query_width),
        mask,
        mask_t,
        upstream,
    )


def gather_blocks(block, axis):
    count = lax.axis_size(axis)
    index = lax.axis_index(axis)
    positions = jnp.arange(count, dtype=jnp.int32)
    if count > 8:
        return lax.all_gather(block, axis, axis=0, tiled=False), positions
    if count == 4:
        partner = [(i, i ^ 1) for i in range(count)]
        across = lax.ppermute(block, axis, [(i, i ^ 2) for i in range(count)])
        received = [block, lax.ppermute(block, axis, partner), across, lax.ppermute(across, axis, partner)]
        return jnp.stack(received), lax.bitwise_xor(index, positions)
    received = [block] + [
        lax.ppermute(block, axis, [(i, (i + d) % count) for i in range(count)])
        for d in range(1, count)
    ]
    return jnp.stack(received), (index - positions) % count


def in_order(block, axis):
    stacked, slots = gather_blocks(block, axis)
    return jnp.take(stacked, slots, axis=0)


def scatter_blocks(blocks, axis, pairs):
    count = lax.axis_size(axis)
    if count > 8:
        return lax.psum_scatter(blocks, axis, scatter_dimension=0, tiled=True)[0].astype(
            jnp.float32
        )
    index = lax.axis_index(axis)

    def pick(i):
        return lax.dynamic_index_in_dim(blocks, i, 0, keepdims=False)

    if pairs and count == 4:
        partner = [(i, i ^ 1) for i in range(count)]
        got = lax.ppermute(jnp.stack([pick(index ^ 1), pick(index ^ 3)]), axis, partner)
        theirs = (pick(index ^ 2).astype(jnp.float32) + got[1].astype(jnp.float32)).astype(
            blocks.dtype
        )
        back = lax.ppermute(theirs, axis, [(i, i ^ 2) for i in range(count)])
        return (
            pick(index).astype(jnp.float32)
            + got[0].astype(jnp.float32)
            + back.astype(jnp.float32)
        )
    total = pick(index).astype(jnp.float32)
    for d in range(1, count):
        part = lax.dynamic_index_in_dim(blocks, (index + d) % count, 0, keepdims=False)
        total = total + lax.ppermute(
            part, axis, [(i, (i + d) % count) for i in range(count)]
        ).astype(jnp.float32)
    return total


def per_device(
    image_tokens,
    keyval_weight,
    query_gain,
    key_norm_gain,
    gate_logit,
    text_queries,
    text_document,
    image_document,
    cotangent,
):
    section_count = lax.axis_size("section")
    section_index = lax.axis_index("section")
    micro_count = text_queries.shape[0]
    head_count = gate_logit.shape[1]
    key_width = key_norm_gain.shape[1]
    head_dim = query_gain.shape[1] // head_count
    keyval_heads = key_width // head_dim
    weights = keyval_weight[0]

    layer_params, layer_slots = gather_blocks(
        jnp.concatenate([query_gain, gate_logit], axis=1)[0], "section"
    )
    gains_all = layer_params[:, : query_gain.shape[1]]
    gates_all = layer_params[:, query_gain.shape[1] :]

    shard_count = lax.axis_size("shard")
    owned = image_tokens.shape[1]
    image_count = owned * section_count
    total_rows = micro_count * image_count
    pair_width = 2 * key_width
    phased = section_count == 4 and shard_count == 2 * micro_count
    if phased:
        images, _ = gather_blocks(image_tokens, "section")
        raw_parts = []
        for phase in range(2):
            block = images[2 * phase : 2 * phase + 2].transpose(1, 0, 2, 3)
            block = block.reshape(-1, image_tokens.shape[2])
            partial = jnp.dot(block, weights, preferred_element_type=jnp.float32)
            raw_parts.append(
                scatter_blocks(partial.reshape(shard_count, owned, pair_width), "shard", False)
            )
        raw_rows = jnp.stack(raw_parts)
        sections = jnp.arange(section_count, dtype=jnp.int32)
        distance = lax.bitwise_xor(section_index, sections)
        micro_ids = jnp.arange(micro_count, dtype=jnp.int32)
        natural = (2 * micro_ids[:, None] + distance[None, :] % 2) * 2 + distance[None, :] // 2
        owners = jnp.arange(shard_count, dtype=jnp.int32)[:, None]
        phases = jnp.arange(2, dtype=jnp.int32)[None, :]
        held = (owners // 2) * section_count + lax.bitwise_xor(
            section_index, 2 * phases + owners % 2
        )

        def to_natural(rows):
            blocks = in_order(rows.reshape(2, owned, pair_width), "shard")
            return jnp.take(
                blocks.reshape(2 * shard_count, owned, pair_width), natural.reshape(-1), axis=0
            ).reshape(total_rows, pair_width)

        def to_owned(rows):
            return jnp.take(
                rows.reshape(micro_count * section_count, owned, pair_width),
                held.reshape(-1),
                axis=0,
            ).reshape(shard_count, 2 * owned, pair_width)

    else:
        gathered = in_order(image_tokens, "section")
        gathered = gathered.transpose(1, 0, 2, 3).reshape(total_rows, image_tokens.shape[2])
        partial = jnp.dot(gathered, weights, preferred_element_type=jnp.float32)
        raw_rows = scatter_blocks(
            partial.reshape(shard_count, total_rows // shard_count, pair_width), "shard", False
        )

        def to_natural(rows):
            return in_order(rows, "shard").reshape(total_rows, pair_width)

        def to_owned(rows):
            return rows.reshape(shard_count, total_rows // shard_count, pair_width)

    raw_rows = raw_rows.reshape(-1, pair_width)
    key_rows = head_normalize(raw_rows[:, :key_width], key_norm_gain[0], keyval_heads)
    keyval_rows = jnp.concatenate(
        [key_rows.astype(jnp.bfloat16), raw_rows[:, key_width:].astype(jnp.bfloat16)], axis=1
    )
    keyval_own = to_natural(keyval_rows)
    keyval_all, _ = gather_blocks(keyval_own, "section")

    same_document = text_document[:, :, None] == image_document[:, None, :]
    leaving, grad_local = attention_layers(
        section_index,
        layer_slots,
        jnp.tanh(gates_all),
        text_queries,
        keyval_all.reshape(section_count, micro_count, image_count, 2 * key_width),
        gains_all,
        same_document,
        cotangent[0],
    )
    grad_rows = scatter_blocks(to_owned(grad_local), "shard", False).reshape(-1, pair_width)
    key_portion = norm_gradient(
        raw_rows[:, :key_width], key_norm_gain[0], grad_rows[:, :key_width], keyval_heads
    )
    raw_grad_rows = jnp.concatenate([key_portion, grad_rows[:, key_width:]], axis=1).astype(
        jnp.bfloat16
    )
    raw_grad = to_natural(raw_grad_rows)
    owned = image_count // section_count
    raw_grad = (
        raw_grad.reshape(micro_count, section_count, owned, 2 * key_width)
        .transpose(1, 0, 2, 3)
        .reshape(total_rows, 2 * key_width)
    )
    image_part = lax.dot_general(
        raw_grad, weights, (((1,), (1,)), ((), ())), preferred_element_type=jnp.float32
    )
    image_part = image_part.astype(jnp.bfloat16).reshape(
        section_count, micro_count, owned, weights.shape[0]
    )
    image_grad = scatter_blocks(image_part, "section", True)
    return (leaving[None], image_grad)


def solution(mesh):
    placed = (
        P("group", "section", "shard"),
        P("section", "shard", None),
        P("section", None),
        P("section", None),
        P("section", None),
        P("group", "shard", None),
        P("group", "shard"),
        P("group", None),
        P("section", "group", "shard", None),
    )
    return jax.shard_map(
        per_device,
        mesh=mesh,
        in_specs=placed,
        out_specs=(P("section", "group", "shard", None), P("group", "section", "shard")),
        check_vma=False,
    )
```
